128 devices in a mesh: blk: 16 (over y_lo, x, core), rep: 8 (over z, y_hi).
Axes of the slice: x: 4, y: 4 (y_hi: 2, y_lo: 2; y = y_hi * 2 + y_lo), z: 4, core: 2. Of those that a mesh axis runs over, the one named last changes fastest.
Arguments:
- entities: bfloat16 [32768, 256], P('blk'), may hold values from -1.5 to 1.5
- entity_state: float32 [32768], P(('blk', 'rep')), may hold values from 0.05 to 4
- shared_table: bfloat16 [8192, 256], replicated, may hold values from -1.5 to 1.5
- shared_state: float32 [8192], P(('blk', 'rep')), may hold values from 0.05 to 4
- edge_src: int32 [16, 4, 4096], P('blk', None, 'rep'), may hold values from 0 to 2047
- edge_dst: int32 [16, 4, 4096], P('blk', None, 'rep'), may hold values from 0 to 2047
- edge_slot: int32 [16, 4, 4096], P('blk', None, 'rep'), may hold values from 0 to 255
- neg_rows: int32 [16, 4, 32, 512], P('blk', None, 'rep'), may hold values from 0 to 2047
- list_owner: int32 [16, 2048, 1], P('blk', 'rep'), may hold values from 0 to 127; in each aligned block of 256 rows (0 to 255, 256 to 511, ..., all dimensions but the last counted through in order) at most 4 rows name the same one
- list_row: int32 [16, 2048], P('blk', 'rep'), may hold values from 0 to 63
Outputs:
- new_entities: float32 [32768, 256], P(('blk', 'rep'))
- new_entity_state: float32 [32768], P(('blk', 'rep'))
- new_shared: float32 [8192, 256], P(('blk', 'rep'))
- new_shared_state: float32 [8192], P(('blk', 'rep'))
The draws below stay inside these ranges and needn't reach their ends.
Inputs may be any that keep to these rules, and one draw needn't show every extreme that they name: Within the 256 list entries of one device (aligned blocks of 256 entries of list_owner), no owner is named more than 4 times, a bound that some block reaches.
All inputs are finite; a program needn't handle non-finite values.
Results may differ from the reference program's by a relative error of at most 0.0022.
Values may be sent and summed in bfloat16 or wider, within the bound.
No kernel may reach another device: no remote copies, remote signals or barrier semaphores. Data moves between devices by JAX's collectives and lax.ppermute only.
A program may use at most 64 MiB of HBM per device.

```python
import math
import jax
import jax.numpy as jnp
import numpy as np
from jax import lax

D = 256
ENT = 2048
E_DEV = 512
GROUP = 128
NEG = 512
STEPS = 4
CAP = 4
SH_DEV = 64
BLOCKS = 16
ENTITIES = 32768
EDGES = 4096
GROUPS = 32
SHARED = 8192
LIST = 256
LIST_ALL = 2048
DEVICES = 128


def with_ends(values, stream_key, smallest, high):
    dims = values.shape
    index_at = [jax.random.randint(jax.random.fold_in(stream_key, axis), (), 0, dims[axis]) for axis in range(len(dims))]
    values = values.at[tuple(index_at)].set(smallest)
    longest = dims.index(max(dims))
    index_at[longest] = (index_at[longest] + 1) % dims[longest]
    return values.at[tuple(index_at)].set(high)


def block_scale(own_key, dims, pieces, smallest, largest):
    factor_of = 1.0
    for axis_at, blocks in pieces:
        heights = jax.random.uniform(jax.random.fold_in(jax.random.fold_in(own_key, 6), axis_at), (blocks,), jnp.float32, smallest / len(pieces), largest / len(pieces))
        factor_of = factor_of * jnp.repeat(jnp.exp(heights), dims[axis_at] // blocks).reshape((-1,) + (1,) * (len(dims) - 1 - axis_at))
    return factor_of


def assign_block(key, own, number, rows, amount, top, reach, skew):
    sequence = jax.random.permutation(key, amount)
    packed, common = portions_of(amount, rows * top, reach, skew, True), portions_of(amount, rows * top, reach, skew, False)
    places = jnp.arange(amount)

    def named(lengths, offset_by):
        used = int((lengths > 0).sum())
        fixed = max(1, used // 4)
        shifted = fixed + (places - fixed + offset_by * (used - fixed)) % max(1, amount - fixed)
        return jnp.zeros((amount,), jnp.int32).at[sequence[jnp.where(places < fixed, places, shifted)]].set(jnp.asarray(lengths, jnp.int32))

    lengths = jnp.where(number % 4 == 0, named(packed, number // 4), named(common, number - number // 4 - 1))
    mixed = jax.random.permutation(jax.random.fold_in(own, 3), amount)
    donor, taker = mixed[0:amount // 2 * 2:2], mixed[1:amount // 2 * 2:2]
    slack = jnp.minimum(lengths[donor] - 1, reach - lengths[taker]) // 2
    slack = jnp.where((donor == sequence[0]) | (taker == sequence[0]) | (lengths[taker] == 0), 0, jnp.maximum(slack, 0))
    shifted = jax.random.randint(jax.random.fold_in(own, 4), (amount // 2,), 0, 1 << 20) % (slack + 1)
    lengths = lengths.at[donor].add(-shifted).at[taker].add(shifted)
    items = jnp.searchsorted(jnp.cumsum(lengths), jnp.arange(rows * top), side="right").astype(jnp.int32)
    listing = items.reshape(top, rows).T
    listing = listing[jax.random.permutation(jax.random.fold_in(own, 1), rows)]
    offset_by = jax.random.randint(jax.random.fold_in(own, 2), (rows, 1), 0, top)
    return jnp.take_along_axis(listing, (jnp.arange(top)[None, :] + offset_by) % top, axis=1)


def portions_of(count, total, limit, lean, full):
    portions = [(1 << 20) // math.isqrt(standing ** lean) + 1 for standing in range(1, count + 1)]
    largest = limit if full else min(limit, max(-(-total // count), total * portions[0] // sum(portions)))
    least = 1 if total - largest >= count - 1 else 0
    given, spare = [largest] + [least] * (count - 1), total - largest - least * (count - 1)
    while spare > 0:
        free = [i for i in range(1, count) if given[i] < largest] or [i for i in range(1, count) if given[i] < limit]
        mass, budget = sum([portions[i] for i in free]), spare
        for i in free:
            more = min(limit - given[i], max(1, budget * portions[i] // mass), spare)
            given[i] = given[i] + more
            spare = spare - more
    return np.array(given)


def gaussian(own_key, extent, width, bound, shards=(), kind=jnp.bfloat16):
    factor_of = block_scale(own_key, extent, shards, -0.22, 0.18) if shards else 1.0
    result = jax.random.normal(own_key, extent, jnp.float32) * width * factor_of
    return jnp.minimum(jnp.maximum(result, -bound), bound).astype(kind)


def setup_inputs(seed: int = 0) -> dict:
    key_of = jax.random.split(jax.random.key(seed), 11)
    entities = gaussian(key_of[0], (ENTITIES, D), 0.25, 1.5, ((0, 16),))
    entity_state = jnp.clip(jnp.exp(math.log(4.0) - 4.3820266 * jax.random.uniform(key_of[1], (ENTITIES,), jnp.float32) ** block_scale(key_of[1], (ENTITIES,), ((0, 128),), -0.2, 0.2)), 0.05, 4.0)
    shared_table = gaussian(key_of[2], (SHARED, D), 0.25, 1.5)
    shared_state = jnp.clip(jnp.exp(math.log(4.0) - 4.3820266 * jax.random.uniform(key_of[3], (SHARED,), jnp.float32) ** block_scale(key_of[3], (SHARED,), ((0, 128),), -0.2, 0.2)), 0.05, 4.0)
    edge_src = with_ends(jax.random.randint(key_of[4], (BLOCKS, STEPS, EDGES), 0, ENT), jax.random.fold_in(key_of[4], 1), 0, ENT - 1).astype(jnp.int32)
    edge_dst = with_ends(jax.random.randint(key_of[5], (BLOCKS, STEPS, EDGES), 0, ENT), jax.random.fold_in(key_of[5], 1), 0, ENT - 1).astype(jnp.int32)
    edge_slot = with_ends(jax.random.randint(key_of[6], (BLOCKS, STEPS, EDGES), 0, LIST), jax.random.fold_in(key_of[6], 1), 0, LIST - 1).astype(jnp.int32)
    neg_rows = with_ends(jax.random.randint(key_of[7], (BLOCKS, STEPS, GROUPS, NEG), 0, ENT), jax.random.fold_in(key_of[7], 1), 0, ENT - 1).astype(jnp.int32)
    list_owner_keys = jax.random.split(jax.random.fold_in(key_of[8], 1), BLOCKS * LIST_ALL // LIST)
    list_owner_turns = jax.random.permutation(jax.random.fold_in(key_of[8], 3), BLOCKS * LIST_ALL // LIST)
    list_owner = jax.vmap(lambda own, number: assign_block(jax.random.fold_in(key_of[8], 2), own, number, LIST, DEVICES, 1, CAP, 2))(list_owner_keys, list_owner_turns).reshape((BLOCKS, LIST_ALL, 1))
    list_row = with_ends(jax.random.randint(key_of[9], (BLOCKS, LIST_ALL), 0, SH_DEV), jax.random.fold_in(key_of[9], 1), 0, SH_DEV - 1).astype(jnp.int32)
    return {"entities": entities, "entity_state": entity_state, "shared_table": shared_table, "shared_state": shared_state, "edge_src": edge_src, "edge_dst": edge_dst, "edge_slot": edge_slot, "neg_rows": neg_rows, "list_owner": list_owner, "list_row": list_row}


learn_rate = 0.1
negative_weight = 8.0

def row_adagrad(rows, state, grad):
    new_state = state + lax.optimization_barrier(jnp.mean(grad * grad, axis=-1))
    return (rows.astype(jnp.float32) - learn_rate * grad / jnp.sqrt(new_state)[:, None], new_state)

def reference(entities, entity_state, shared_table, shared_state, edge_src, edge_dst, edge_slot, neg_rows, list_owner, list_row):
    shared_ids = list_owner[:, :, 0] * SH_DEV + list_row
    list_base = jnp.arange(EDGES, dtype=jnp.int32) // E_DEV * LIST

    def visit(carry, bucket_index):
        entity_grad, shared_grad = carry
        source_part = bucket_index // STEPS
        bucket = bucket_index % STEPS
        target_part = (source_part - bucket) % BLOCKS
        sources = edge_src[source_part, bucket] + source_part * ENT
        targets = edge_dst[source_part, bucket] + target_part * ENT
        slots = shared_ids[source_part][edge_slot[source_part, bucket] + list_base]
        negatives = neg_rows[source_part, bucket] + target_part * ENT
        query = (entities[sources].astype(jnp.float32) + shared_table[slots].astype(jnp.float32)).astype(jnp.bfloat16)
        query = lax.optimization_barrier(query)
        query_wide = query.astype(jnp.float32)
        target_rows = entities[targets].astype(jnp.float32)
        positive = lax.optimization_barrier(jnp.sum(query_wide * target_rows, axis=-1))
        samples = entities[negatives].astype(jnp.float32)
        query_groups = query_wide.reshape(GROUPS, GROUP, D)
        negative = jnp.einsum('cqd,cnd->cqn', query_groups, samples)
        positive_weight = -jax.nn.sigmoid(-positive)
        sample_weight = (jax.nn.sigmoid(negative) * (negative_weight / NEG)).astype(jnp.bfloat16)
        sample_weight = lax.optimization_barrier(sample_weight).astype(jnp.float32)
        query_grad = positive_weight[:, None] * target_rows + jnp.einsum('cqn,cnd->cqd', sample_weight, samples).reshape(EDGES, D)
        target_grad = positive_weight[:, None] * query_wide
        sample_grad = jnp.einsum('cqn,cqd->cnd', sample_weight, query_groups).reshape(GROUPS * NEG, D)
        entity_grad = entity_grad.at[sources].add(query_grad).at[targets].add(target_grad).at[negatives.reshape(-1)].add(sample_grad)
        shared_grad = shared_grad.at[slots].add(query_grad)
        return ((entity_grad, shared_grad), None)
    start = (jnp.zeros((ENTITIES, D), jnp.float32), jnp.zeros((SHARED, D), jnp.float32))
    (entity_grad, shared_grad), unused = lax.scan(visit, start, jnp.arange(BLOCKS * STEPS, dtype=jnp.int32))
    new_entities, new_entity_state = row_adagrad(entities, entity_state, entity_grad)
    new_shared, new_shared_state = row_adagrad(shared_table, shared_state, shared_grad)
    return (new_entities, new_entity_state, new_shared, new_shared_state)
```

```python
import jax
import jax.numpy as jnp
from jax import lax
from jax.sharding import PartitionSpec as P

CAP = 4
SH_DEV = 64


learn_rate = 0.1
negative_weight = 8.0


def passed_along(value, axis, by):
    peers = lax.axis_size(axis)
    return lax.ppermute(value, axis, [(i, (i + by) % peers) for i in range(peers)])


def bucket_grads(resident, visiting, sources, targets, slots, negatives, shared_rows):
    part_rows = visiting.shape[0]
    model_width = visiting.shape[1]
    group_count = negatives.shape[0]
    sample_count = negatives.shape[1]
    entity_ids = jnp.arange(part_rows, dtype=jnp.int32)
    list_ids = jnp.arange(shared_rows.shape[0], dtype=jnp.int32)
    source_pick = (sources[:, None] == entity_ids[None, :]).astype(jnp.bfloat16)
    target_pick = (targets[:, None] == entity_ids[None, :]).astype(jnp.bfloat16)
    slot_pick = (slots[:, None] == list_ids[None, :]).astype(jnp.bfloat16)
    sample_pick = (negatives[:, :, None] == entity_ids[None, None, :]).astype(jnp.bfloat16)
    source_rows = jnp.dot(source_pick, resident, preferred_element_type=jnp.float32)
    shared_part = jnp.dot(slot_pick, shared_rows, preferred_element_type=jnp.float32)
    query = (source_rows + shared_part).astype(jnp.bfloat16)
    target_rows = jnp.dot(target_pick, visiting, preferred_element_type=jnp.float32).astype(
        jnp.bfloat16
    )
    positive = jnp.einsum("ed,ed->e", query, target_rows, preferred_element_type=jnp.float32)
    query_groups = query.reshape(group_count, -1, model_width)
    samples = jnp.einsum(
        "cnx,xd->cnd", sample_pick, visiting, preferred_element_type=jnp.float32
    ).astype(jnp.bfloat16)
    negative = jnp.einsum("cqd,cnd->cqn", query_groups, samples, preferred_element_type=jnp.float32)
    positive_weight = -jax.nn.sigmoid(-positive)
    sample_weight = (jax.nn.sigmoid(negative) * (negative_weight / sample_count)).astype(
        jnp.bfloat16
    )
    sampled_sum = jnp.einsum(
        "cqn,cnd->cqd", sample_weight, samples, preferred_element_type=jnp.float32
    )
    query_grad = positive_weight[:, None] * target_rows.astype(jnp.float32) + sampled_sum.reshape(
        -1, model_width
    )
    weight_map = jnp.einsum(
        "cnx,cqn->xcq", sample_pick, sample_weight, preferred_element_type=jnp.float32
    ).reshape(part_rows, -1)
    weight_map = weight_map + jnp.einsum(
        "ex,e->xe", target_pick.astype(jnp.float32), positive_weight
    )
    visiting_grad = jnp.dot(weight_map, query.astype(jnp.float32), precision=lax.Precision.HIGHEST)
    return (query_grad, visiting_grad, source_pick, slot_pick)


def row_adagrad(rows, state, grad):
    new_state = state + jnp.mean(grad * grad, axis=-1)
    return (rows.astype(jnp.float32) - learn_rate * grad / jnp.sqrt(new_state)[:, None], new_state)


def shards(
    entities,
    entity_state,
    shared_table,
    shared_state,
    edge_src,
    edge_dst,
    edge_slot,
    neg_rows,
    list_owner,
    list_row,
):
    rep_count = lax.axis_size("rep")
    rep_place = lax.axis_index("rep")
    device_count = lax.axis_size("blk") * rep_count
    device_place = lax.axis_index("blk") * rep_count + rep_place
    part_rows = entities.shape[0]
    model_width = entities.shape[1]
    share_rows = part_rows // rep_count
    bucket_count = edge_src.shape[1]
    owners = list_owner[0, :, 0]
    local_rows = list_row[0]
    shared_rows = shared_table[owners * SH_DEV + local_rows]
    source_total = jnp.zeros((part_rows, model_width), jnp.float32)
    slot_total = jnp.zeros((owners.shape[0], model_width), jnp.float32)
    visiting = entities
    carried = jnp.zeros((part_rows, model_width), jnp.float32)
    for bucket in range(bucket_count):
        if bucket > 0:
            visiting = passed_along(visiting, "blk", 1)
        query_grad, visiting_grad, source_pick, slot_pick = bucket_grads(
            entities,
            visiting,
            edge_src[0, bucket],
            edge_dst[0, bucket],
            edge_slot[0, bucket],
            neg_rows[0, bucket],
            shared_rows,
        )
        source_total = source_total + jnp.einsum(
            "ex,ed->xd",
            source_pick.astype(jnp.float32),
            query_grad,
            precision=lax.Precision.HIGHEST,
        )
        slot_total = slot_total + jnp.einsum(
            "el,ed->ld", slot_pick.astype(jnp.float32), query_grad, precision=lax.Precision.HIGHEST
        )
        if bucket == 0:
            source_total = source_total + visiting_grad
        elif bucket == 1:
            carried = visiting_grad
        else:
            carried = (
                passed_along(carried.astype(jnp.bfloat16), "blk", 1).astype(carried.dtype)
                + visiting_grad
            )
    source_total = source_total + passed_along(
        carried.astype(jnp.bfloat16), "blk", 1 - bucket_count
    ).astype(carried.dtype)
    own_grad = jnp.sum(
        lax.all_to_all(
            source_total.reshape(rep_count, share_rows, model_width),
            "rep",
            split_axis=0,
            concat_axis=0,
            tiled=True,
        ),
        axis=0,
    )
    own_entities = lax.dynamic_slice_in_dim(entities, rep_place * share_rows, share_rows, 0)
    new_entities, new_entity_state = row_adagrad(own_entities, entity_state, own_grad)
    slot_count = owners.shape[0]
    slot_order = jnp.arange(slot_count, dtype=jnp.int32)
    earlier_same = (owners[:, None] == owners[None, :]) & (
        slot_order[None, :] < slot_order[:, None]
    )
    slot_ranks = jnp.sum(earlier_same.astype(jnp.int32), axis=1)
    send_keys = owners * CAP + slot_ranks
    send_ids = jnp.arange(device_count * CAP, dtype=jnp.int32)
    send_pick = (send_keys[:, None] == send_ids[None, :]).astype(jnp.float32)
    outbound = jnp.einsum(
        "lk,ld->kd", send_pick, slot_total, precision=lax.Precision.HIGHEST
    ).reshape(device_count, CAP, model_width)
    labels = jnp.einsum(
        "lk,l->k", send_pick, local_rows.astype(jnp.float32), precision=lax.Precision.HIGHEST
    ).reshape(device_count, CAP)
    label_row = jnp.zeros((device_count, 1, model_width), jnp.float32)
    label_row = label_row.at[:, 0, :CAP].set(labels)
    packed = jnp.concatenate([outbound, label_row], axis=1).astype(jnp.bfloat16)
    arrived = lax.all_to_all(
        packed, ("blk", "rep"), split_axis=0, concat_axis=0, tiled=True
    ).astype(jnp.float32)
    inbound = arrived[:, :CAP, :]
    inbound_labels = arrived[:, CAP, :CAP]
    table_rows = jnp.arange(SH_DEV, dtype=jnp.int32)
    selector = (
        inbound_labels.reshape(-1).astype(jnp.int32)[:, None] == table_rows[None, :]
    ).astype(jnp.float32)
    shared_grad = jnp.einsum(
        "rs,rd->sd",
        selector,
        inbound.reshape(-1, model_width),
        preferred_element_type=jnp.float32,
        precision=lax.Precision.HIGHEST,
    )
    own_shared = lax.dynamic_slice_in_dim(shared_table, device_place * SH_DEV, SH_DEV, 0)
    new_shared, new_shared_state = row_adagrad(own_shared, shared_state, shared_grad)
    return (new_entities, new_entity_state, new_shared, new_shared_state)


def solution(mesh):
    return jax.shard_map(
        shards,
        mesh=mesh,
        in_specs=(
            P("blk", None),
            P(("blk", "rep")),
            P(),
            P(("blk", "rep")),
            P("blk", None, "rep"),
            P("blk", None, "rep"),
            P("blk", None, "rep"),
            P("blk", None, "rep", None),
            P("blk", "rep", None),
            P("blk", "rep"),
        ),
        out_specs=(
            P(("blk", "rep"), None),
            P(("blk", "rep")),
            P(("blk", "rep"), None),
            P(("blk", "rep")),
        ),
        check_vma=False,
    )
```

```python
import jax
import jax.numpy as jnp
from jax import lax
from jax.sharding import PartitionSpec as P

CAP = 4
SH_DEV = 64


learn_rate = 0.1
negative_weight = 8.0


def passed_along(value, axis, by):
    peers = lax.axis_size(axis)
    return lax.ppermute(value, axis, [(i, (i + by) % peers) for i in range(peers)])


def make_query(resident, sources, slots, shared_rows):
    part_rows = resident.shape[0]
    entity_ids = jnp.arange(part_rows, dtype=jnp.int32)
    list_ids = jnp.arange(shared_rows.shape[0], dtype=jnp.int32)
    source_pick = (sources[:, None] == entity_ids[None, :]).astype(jnp.bfloat16)
    slot_pick = (slots[:, None] == list_ids[None, :]).astype(jnp.bfloat16)
    source_rows = jnp.dot(source_pick, resident, preferred_element_type=jnp.float32)
    shared_part = jnp.dot(slot_pick, shared_rows, preferred_element_type=jnp.float32)
    query = (source_rows + shared_part).astype(jnp.bfloat16)
    return query, source_pick, slot_pick


def target_side(visiting, query, targets, negatives):
    part_rows = visiting.shape[0]
    model_width = visiting.shape[1]
    group_count = negatives.shape[0]
    sample_count = negatives.shape[1]
    entity_ids = jnp.arange(part_rows, dtype=jnp.int32)
    target_pick = (targets[:, None] == entity_ids[None, :]).astype(jnp.bfloat16)
    sample_pick = (negatives[:, :, None] == entity_ids[None, None, :]).astype(jnp.bfloat16)
    target_rows = jnp.dot(target_pick, visiting, preferred_element_type=jnp.float32).astype(
        jnp.bfloat16
    )
    positive = jnp.einsum("ed,ed->e", query, target_rows, preferred_element_type=jnp.float32)
    query_groups = query.reshape(group_count, -1, model_width)
    samples = jnp.einsum(
        "cnx,xd->cnd", sample_pick, visiting, preferred_element_type=jnp.float32
    ).astype(jnp.bfloat16)
    negative = jnp.einsum("cqd,cnd->cqn", query_groups, samples, preferred_element_type=jnp.float32)
    positive_weight = -jax.nn.sigmoid(-positive)
    sample_weight = (jax.nn.sigmoid(negative) * (negative_weight / sample_count)).astype(
        jnp.bfloat16
    )
    sampled_sum = jnp.einsum(
        "cqn,cnd->cqd", sample_weight, samples, preferred_element_type=jnp.float32
    )
    query_grad = positive_weight[:, None] * target_rows.astype(jnp.float32) + sampled_sum.reshape(
        -1, model_width
    )
    weight_map = jnp.einsum(
        "cnx,cqn->xcq", sample_pick, sample_weight, preferred_element_type=jnp.float32
    ).reshape(part_rows, -1)
    weight_map = weight_map + jnp.einsum(
        "ex,e->xe", target_pick.astype(jnp.float32), positive_weight
    )
    visiting_grad = jnp.dot(weight_map, query.astype(jnp.float32), precision=lax.Precision.HIGHEST)
    return query_grad, visiting_grad


def row_adagrad(rows, state, grad):
    new_state = state + jnp.mean(grad * grad, axis=-1)
    return (rows.astype(jnp.float32) - learn_rate * grad / jnp.sqrt(new_state)[:, None], new_state)


def shards(
    entities,
    entity_state,
    shared_table,
    shared_state,
    edge_src,
    edge_dst,
    edge_slot,
    neg_rows,
    list_owner,
    list_row,
):
    rep_count = lax.axis_size("rep")
    rep_place = lax.axis_index("rep")
    device_count = lax.axis_size("blk") * rep_count
    device_place = lax.axis_index("blk") * rep_count + rep_place
    part_rows = entities.shape[0]
    model_width = entities.shape[1]
    share_rows = part_rows // rep_count
    bucket_count = edge_src.shape[1]
    edge_count = edge_src.shape[2]
    owners = list_owner[0, :, 0]
    local_rows = list_row[0]
    shared_rows = shared_table[owners * SH_DEV + local_rows]
    queries = []
    picks = []
    for bucket in range(bucket_count):
        query, source_pick, slot_pick = make_query(
            entities, edge_src[0, bucket], edge_slot[0, bucket], shared_rows
        )
        queries.append(query)
        picks.append((source_pick, slot_pick))
    arrivals = []
    for bucket in range(bucket_count):
        indices = jnp.concatenate([edge_dst[0, bucket], neg_rows[0, bucket].reshape(-1)])
        if bucket == 0:
            arrivals.append((queries[bucket], indices))
        else:
            arrivals.append(
                (
                    passed_along(queries[bucket], "blk", -bucket),
                    passed_along(indices, "blk", -bucket),
                )
            )
    group_shape = neg_rows.shape[2:]
    target_total = jnp.zeros((part_rows, model_width), jnp.float32)
    returned = []
    for bucket in range(bucket_count):
        query, indices = arrivals[bucket]
        targets = indices[:edge_count]
        negatives = indices[edge_count:].reshape(group_shape)
        query_grad, visiting_grad = target_side(entities, query, targets, negatives)
        target_total = target_total + visiting_grad
        if bucket == 0:
            returned.append(query_grad)
        else:
            returned.append(passed_along(query_grad, "blk", bucket))
    source_total = target_total
    slot_total = jnp.zeros((owners.shape[0], model_width), jnp.float32)
    for bucket in range(bucket_count):
        source_pick, slot_pick = picks[bucket]
        query_grad = returned[bucket]
        source_total = source_total + jnp.einsum(
            "ex,ed->xd",
            source_pick.astype(jnp.float32),
            query_grad,
            precision=lax.Precision.HIGHEST,
        )
        slot_total = slot_total + jnp.einsum(
            "el,ed->ld", slot_pick.astype(jnp.float32), query_grad, precision=lax.Precision.HIGHEST
        )
    own_grad = jnp.sum(
        lax.all_to_all(
            source_total.reshape(rep_count, share_rows, model_width),
            "rep",
            split_axis=0,
            concat_axis=0,
            tiled=True,
        ),
        axis=0,
    )
    own_entities = lax.dynamic_slice_in_dim(entities, rep_place * share_rows, share_rows, 0)
    new_entities, new_entity_state = row_adagrad(own_entities, entity_state, own_grad)
    slot_count = owners.shape[0]
    slot_order = jnp.arange(slot_count, dtype=jnp.int32)
    earlier_same = (owners[:, None] == owners[None, :]) & (
        slot_order[None, :] < slot_order[:, None]
    )
    slot_ranks = jnp.sum(earlier_same.astype(jnp.int32), axis=1)
    send_keys = owners * CAP + slot_ranks
    send_ids = jnp.arange(device_count * CAP, dtype=jnp.int32)
    send_pick = (send_keys[:, None] == send_ids[None, :]).astype(jnp.float32)
    outbound = jnp.einsum(
        "lk,ld->kd", send_pick, slot_total, precision=lax.Precision.HIGHEST
    ).reshape(device_count, CAP, model_width)
    labels = jnp.einsum(
        "lk,l->k", send_pick, local_rows.astype(jnp.float32), precision=lax.Precision.HIGHEST
    ).reshape(device_count, CAP)
    label_row = jnp.zeros((device_count, 1, model_width), jnp.float32)
    label_row = label_row.at[:, 0, :CAP].set(labels)
    packed = jnp.concatenate([outbound, label_row], axis=1).astype(jnp.bfloat16)
    arrived = lax.all_to_all(
        packed, ("blk", "rep"), split_axis=0, concat_axis=0, tiled=True
    ).astype(jnp.float32)
    inbound = arrived[:, :CAP, :]
    inbound_labels = arrived[:, CAP, :CAP]
    table_rows = jnp.arange(SH_DEV, dtype=jnp.int32)
    selector = (
        inbound_labels.reshape(-1).astype(jnp.int32)[:, None] == table_rows[None, :]
    ).astype(jnp.float32)
    shared_grad = jnp.einsum(
        "rs,rd->sd",
        selector,
        inbound.reshape(-1, model_width),
        preferred_element_type=jnp.float32,
        precision=lax.Precision.HIGHEST,
    )
    own_shared = lax.dynamic_slice_in_dim(shared_table, device_place * SH_DEV, SH_DEV, 0)
    new_shared, new_shared_state = row_adagrad(own_shared, shared_state, shared_grad)
    return (new_entities, new_entity_state, new_shared, new_shared_state)


def solution(mesh):
    return jax.shard_map(
        shards,
        mesh=mesh,
        in_specs=(
            P("blk", None),
            P(("blk", "rep")),
            P(),
            P(("blk", "rep")),
            P("blk", None, "rep"),
            P("blk", None, "rep"),
            P("blk", None, "rep"),
            P("blk", None, "rep", None),
            P("blk", "rep", None),
            P("blk", "rep"),
        ),
        out_specs=(
            P(("blk", "rep"), None),
            P(("blk", "rep")),
            P(("blk", "rep"), None),
            P(("blk", "rep")),
        ),
        check_vma=False,
    )
```

```python
import jax
import jax.numpy as jnp
from jax import lax
from jax.sharding import PartitionSpec as P

CAP = 4
SH_DEV = 64


learn_rate = 0.1
negative_weight = 8.0


def passed_along(value, axis, by):
    peers = lax.axis_size(axis)
    return lax.ppermute(value, axis, [(i, (i + by) % peers) for i in range(peers)])


def make_query(resident, sources, slots, shared_rows):
    part_rows = resident.shape[0]
    entity_ids = jnp.arange(part_rows, dtype=jnp.int32)
    list_ids = jnp.arange(shared_rows.shape[0], dtype=jnp.int32)
    source_pick = (sources[:, None] == entity_ids[None, :]).astype(jnp.bfloat16)
    slot_pick = (slots[:, None] == list_ids[None, :]).astype(jnp.bfloat16)
    source_rows = jnp.dot(source_pick, resident, preferred_element_type=jnp.float32)
    shared_part = jnp.dot(slot_pick, shared_rows, preferred_element_type=jnp.float32)
    query = (source_rows + shared_part).astype(jnp.bfloat16)
    return query, source_pick, slot_pick


def target_side(visiting, query, targets, negatives):
    part_rows = visiting.shape[0]
    model_width = visiting.shape[1]
    group_count = negatives.shape[0]
    sample_count = negatives.shape[1]
    entity_ids = jnp.arange(part_rows, dtype=jnp.int32)
    target_pick = (targets[:, None] == entity_ids[None, :]).astype(jnp.bfloat16)
    sample_pick = (negatives[:, :, None] == entity_ids[None, None, :]).astype(jnp.bfloat16)
    target_rows = jnp.dot(target_pick, visiting, preferred_element_type=jnp.float32).astype(
        jnp.bfloat16
    )
    positive = jnp.einsum("ed,ed->e", query, target_rows, preferred_element_type=jnp.float32)
    query_groups = query.reshape(group_count, -1, model_width)
    samples = jnp.einsum(
        "cnx,xd->cnd", sample_pick, visiting, preferred_element_type=jnp.float32
    ).astype(jnp.bfloat16)
    negative = jnp.einsum("cqd,cnd->cqn", query_groups, samples, preferred_element_type=jnp.float32)
    positive_weight = -jax.nn.sigmoid(-positive)
    sample_weight = (jax.nn.sigmoid(negative) * (negative_weight / sample_count)).astype(
        jnp.bfloat16
    )
    sampled_sum = jnp.einsum(
        "cqn,cnd->cqd", sample_weight, samples, preferred_element_type=jnp.float32
    )
    query_grad = positive_weight[:, None] * target_rows.astype(jnp.float32) + sampled_sum.reshape(
        -1, model_width
    )
    weight_map = jnp.einsum(
        "cnx,cqn->xcq", sample_pick, sample_weight, preferred_element_type=jnp.float32
    ).reshape(part_rows, -1)
    weight_map = weight_map + jnp.einsum(
        "ex,e->xe", target_pick.astype(jnp.float32), positive_weight
    )
    visiting_grad = split_dot("xe,ed->xd", weight_map, query)
    return query_grad, visiting_grad


def split_dot(spec, wide, narrow):
    high = wide.astype(jnp.bfloat16)
    low = (wide - high.astype(jnp.float32)).astype(jnp.bfloat16)
    return jnp.einsum(spec, high, narrow, preferred_element_type=jnp.float32) + jnp.einsum(
        spec, low, narrow, preferred_element_type=jnp.float32
    )


def row_adagrad(rows, state, grad):
    new_state = state + jnp.mean(grad * grad, axis=-1)
    return (rows.astype(jnp.float32) - learn_rate * grad / jnp.sqrt(new_state)[:, None], new_state)


def shards(
    entities,
    entity_state,
    shared_table,
    shared_state,
    edge_src,
    edge_dst,
    edge_slot,
    neg_rows,
    list_owner,
    list_row,
):
    rep_count = lax.axis_size("rep")
    rep_place = lax.axis_index("rep")
    device_count = lax.axis_size("blk") * rep_count
    device_place = lax.axis_index("blk") * rep_count + rep_place
    part_rows = entities.shape[0]
    model_width = entities.shape[1]
    share_rows = part_rows // rep_count
    bucket_count = edge_src.shape[1]
    edge_count = edge_src.shape[2]
    owners = list_owner[0, :, 0]
    local_rows = list_row[0]
    shared_rows = shared_table[owners * SH_DEV + local_rows]
    queries = []
    picks = []
    for bucket in range(bucket_count):
        query, source_pick, slot_pick = make_query(
            entities, edge_src[0, bucket], edge_slot[0, bucket], shared_rows
        )
        queries.append(query)
        picks.append((source_pick, slot_pick))
    arrivals = []
    for bucket in range(bucket_count):
        indices = jnp.concatenate([edge_dst[0, bucket], neg_rows[0, bucket].reshape(-1)])
        if bucket == 0:
            arrivals.append((queries[bucket], indices))
        else:
            arrivals.append(
                (
                    passed_along(queries[bucket], "blk", -bucket),
                    passed_along(indices, "blk", -bucket),
                )
            )
    group_shape = neg_rows.shape[2:]
    target_total = jnp.zeros((part_rows, model_width), jnp.float32)
    returned = [None] * bucket_count
    for bucket in [0] + list(range(bucket_count - 1, 0, -1)):
        query, indices = arrivals[bucket]
        targets = indices[:edge_count]
        negatives = indices[edge_count:].reshape(group_shape)
        query_grad, visiting_grad = target_side(entities, query, targets, negatives)
        target_total = target_total + visiting_grad
        if bucket == 0:
            returned[bucket] = query_grad
        else:
            returned[bucket] = passed_along(query_grad, "blk", bucket)
    source_total = target_total
    slot_total = jnp.zeros((owners.shape[0], model_width), jnp.float32)
    for bucket in [0] + list(range(bucket_count - 1, 0, -1)):
        source_pick, slot_pick = picks[bucket]
        query_grad = returned[bucket]
        source_total = source_total + split_dot("ed,ex->xd", query_grad, source_pick)
        slot_total = slot_total + split_dot("ed,el->ld", query_grad, slot_pick)
    own_grad = jnp.sum(
        lax.all_to_all(
            source_total.reshape(rep_count, share_rows, model_width).astype(jnp.bfloat16),
            "rep",
            split_axis=0,
            concat_axis=0,
            tiled=True,
        ),
        axis=0,
        dtype=jnp.float32,
    )
    own_entities = lax.dynamic_slice_in_dim(entities, rep_place * share_rows, share_rows, 0)
    new_entities, new_entity_state = row_adagrad(own_entities, entity_state, own_grad)
    slot_count = owners.shape[0]
    slot_order = jnp.arange(slot_count, dtype=jnp.int32)
    earlier_same = (owners[:, None] == owners[None, :]) & (
        slot_order[None, :] < slot_order[:, None]
    )
    slot_ranks = jnp.sum(earlier_same.astype(jnp.int32), axis=1)
    send_keys = owners * CAP + slot_ranks
    send_ids = jnp.arange(device_count * CAP, dtype=jnp.int32)
    send_pick = (send_keys[:, None] == send_ids[None, :]).astype(jnp.float32)
    outbound = jnp.einsum(
        "lk,ld->kd", send_pick, slot_total, precision=lax.Precision.HIGHEST
    ).reshape(device_count, CAP, model_width)
    labels = jnp.einsum(
        "lk,l->k", send_pick, local_rows.astype(jnp.float32), precision=lax.Precision.HIGHEST
    ).reshape(device_count, CAP)
    label_row = jnp.zeros((device_count, 1, model_width), jnp.float32)
    label_row = label_row.at[:, 0, :CAP].set(labels)
    packed = jnp.concatenate([outbound, label_row], axis=1).astype(jnp.bfloat16)
    arrived = lax.all_to_all(
        packed, ("blk", "rep"), split_axis=0, concat_axis=0, tiled=True
    ).astype(jnp.float32)
    inbound = arrived[:, :CAP, :]
    inbound_labels = arrived[:, CAP, :CAP]
    table_rows = jnp.arange(SH_DEV, dtype=jnp.int32)
    selector = (
        inbound_labels.reshape(-1).astype(jnp.int32)[:, None] == table_rows[None, :]
    ).astype(jnp.float32)
    shared_grad = jnp.einsum(
        "rs,rd->sd",
        selector,
        inbound.reshape(-1, model_width),
        preferred_element_type=jnp.float32,
        precision=lax.Precision.HIGHEST,
    )
    own_shared = lax.dynamic_slice_in_dim(shared_table, device_place * SH_DEV, SH_DEV, 0)
    new_shared, new_shared_state = row_adagrad(own_shared, shared_state, shared_grad)
    return (new_entities, new_entity_state, new_shared, new_shared_state)


def solution(mesh):
    return jax.shard_map(
        shards,
        mesh=mesh,
        in_specs=(
            P("blk", None),
            P(("blk", "rep")),
            P(),
            P(("blk", "rep")),
            P("blk", None, "rep"),
            P("blk", None, "rep"),
            P("blk", None, "rep"),
            P("blk", None, "rep", None),
            P("blk", "rep", None),
            P("blk", "rep"),
        ),
        out_specs=(
            P(("blk", "rep"), None),
            P(("blk", "rep")),
            P(("blk", "rep"), None),
            P(("blk", "rep")),
        ),
        check_vma=False,
    )
```

```python
import jax
import jax.numpy as jnp
from jax import lax
from jax.sharding import PartitionSpec as P

CAP = 4
SH_DEV = 64
INDEX_SPLIT = 64


learn_rate = 0.1
negative_weight = 8.0


def passed_along(value, axis, by):
    peers = lax.axis_size(axis)
    return lax.ppermute(value, axis, [(i, (i + by) % peers) for i in range(peers)])


def make_query(resident, sources, slots, shared_rows):
    part_rows = resident.shape[0]
    entity_ids = jnp.arange(part_rows, dtype=jnp.int32)
    list_ids = jnp.arange(shared_rows.shape[0], dtype=jnp.int32)
    source_pick = (sources[:, None] == entity_ids[None, :]).astype(jnp.bfloat16)
    slot_pick = (slots[:, None] == list_ids[None, :]).astype(jnp.bfloat16)
    source_rows = jnp.dot(source_pick, resident, preferred_element_type=jnp.float32)
    shared_part = jnp.dot(slot_pick, shared_rows, preferred_element_type=jnp.float32)
    query = (source_rows + shared_part).astype(jnp.bfloat16)
    return query, source_pick, slot_pick


def target_side(visiting, query, targets, negatives):
    part_rows = visiting.shape[0]
    model_width = visiting.shape[1]
    group_count = negatives.shape[0]
    sample_count = negatives.shape[1]
    entity_ids = jnp.arange(part_rows, dtype=jnp.int32)
    target_pick = (targets[:, None] == entity_ids[None, :]).astype(jnp.bfloat16)
    sample_pick = (negatives[:, :, None] == entity_ids[None, None, :]).astype(jnp.bfloat16)
    target_rows = jnp.dot(target_pick, visiting, preferred_element_type=jnp.float32).astype(
        jnp.bfloat16
    )
    positive = jnp.einsum("ed,ed->e", query, target_rows, preferred_element_type=jnp.float32)
    query_groups = query.reshape(group_count, -1, model_width)
    samples = jnp.einsum(
        "cnx,xd->cnd", sample_pick, visiting, preferred_element_type=jnp.float32
    ).astype(jnp.bfloat16)
    negative = jnp.einsum("cqd,cnd->cqn", query_groups, samples, preferred_element_type=jnp.float32)
    positive_weight = -jax.nn.sigmoid(-positive)
    sample_weight = (jax.nn.sigmoid(negative) * (negative_weight / sample_count)).astype(
        jnp.bfloat16
    )
    sampled_sum = jnp.einsum(
        "cqn,cnd->cqd", sample_weight, samples, preferred_element_type=jnp.float32
    )
    query_grad = positive_weight[:, None] * target_rows.astype(jnp.float32) + sampled_sum.reshape(
        -1, model_width
    )
    weight_map = jnp.einsum(
        "cnx,cqn->xcq", sample_pick, sample_weight, preferred_element_type=jnp.float32
    ).reshape(part_rows, -1)
    weight_map = weight_map + jnp.einsum(
        "ex,e->xe", target_pick.astype(jnp.float32), positive_weight
    )
    visiting_grad = split_dot("xe,ed->xd", weight_map, query)
    return query_grad, visiting_grad


def split_dot(spec, wide, narrow):
    high = wide.astype(jnp.bfloat16)
    low = (wide - high.astype(jnp.float32)).astype(jnp.bfloat16)
    return jnp.einsum(spec, high, narrow, preferred_element_type=jnp.float32) + jnp.einsum(
        spec, low, narrow, preferred_element_type=jnp.float32
    )


def rep_reduce(total):
    rep_count = lax.axis_size("rep")
    pieces = total.reshape(rep_count, -1, total.shape[1]).astype(jnp.bfloat16)
    pieces = lax.all_to_all(pieces, "rep", split_axis=0, concat_axis=0, tiled=True)
    return jnp.sum(pieces, axis=0, dtype=jnp.float32)


def row_adagrad(rows, state, grad):
    new_state = state + jnp.mean(grad * grad, axis=-1)
    return (rows.astype(jnp.float32) - learn_rate * grad / jnp.sqrt(new_state)[:, None], new_state)


def shards(
    entities,
    entity_state,
    shared_table,
    shared_state,
    edge_src,
    edge_dst,
    edge_slot,
    neg_rows,
    list_owner,
    list_row,
):
    rep_count = lax.axis_size("rep")
    rep_place = lax.axis_index("rep")
    device_count = lax.axis_size("blk") * rep_count
    device_place = lax.axis_index("blk") * rep_count + rep_place
    part_rows = entities.shape[0]
    model_width = entities.shape[1]
    share_rows = part_rows // rep_count
    bucket_count = edge_src.shape[1]
    edge_count = edge_src.shape[2]
    owners = list_owner[0, :, 0]
    local_rows = list_row[0]
    shared_rows = shared_table[owners * SH_DEV + local_rows]
    queries = []
    picks = []
    for bucket in range(bucket_count):
        query, source_pick, slot_pick = make_query(
            entities, edge_src[0, bucket], edge_slot[0, bucket], shared_rows
        )
        queries.append(query)
        picks.append((source_pick, slot_pick))
    arrivals = []
    for bucket in range(bucket_count):
        indices = jnp.concatenate([edge_dst[0, bucket], neg_rows[0, bucket].reshape(-1)])
        if bucket == 0:
            arrivals.append((queries[bucket], indices))
        else:
            coded = jnp.stack([indices // INDEX_SPLIT, indices % INDEX_SPLIT]).astype(jnp.bfloat16)
            parcel = jnp.concatenate([queries[bucket], coded.reshape(-1, model_width)], axis=0)
            parcel = passed_along(parcel, "blk", -bucket)
            coded = parcel[edge_count:].reshape(2, -1).astype(jnp.int32)
            arrivals.append((parcel[:edge_count], coded[0] * INDEX_SPLIT + coded[1]))
    group_shape = neg_rows.shape[2:]
    target_total = jnp.zeros((part_rows, model_width), jnp.float32)
    returned = [None] * bucket_count
    previous = None
    for bucket in [0] + list(range(bucket_count - 1, 0, -1)):
        if previous is not None:
            arrivals, _ = lax.optimization_barrier((arrivals, previous))
        if bucket == 1 and bucket_count > 2:
            arrivals, early = lax.optimization_barrier((arrivals, returned[bucket_count - 1]))
            returned[bucket_count - 1] = early
        query, indices = arrivals[bucket]
        targets = indices[:edge_count]
        negatives = indices[edge_count:].reshape(group_shape)
        query_grad, visiting_grad = target_side(entities, query, targets, negatives)
        previous = query_grad
        target_total = target_total + visiting_grad
        if bucket == 0:
            returned[bucket] = query_grad
        else:
            returned[bucket] = passed_along(query_grad, "blk", bucket)
    target_sum = rep_reduce(target_total)
    source_total = jnp.zeros((part_rows, model_width), jnp.float32)
    slot_total = jnp.zeros((owners.shape[0], model_width), jnp.float32)
    for bucket in [0] + list(range(bucket_count - 1, 0, -1)):
        source_pick, slot_pick = picks[bucket]
        query_grad = returned[bucket]
        source_total = source_total + split_dot("ed,ex->xd", query_grad, source_pick)
        slot_total = slot_total + split_dot("ed,el->ld", query_grad, slot_pick)
    own_grad = target_sum + rep_reduce(source_total)
    own_entities = lax.dynamic_slice_in_dim(entities, rep_place * share_rows, share_rows, 0)
    new_entities, new_entity_state = row_adagrad(own_entities, entity_state, own_grad)
    slot_count = owners.shape[0]
    slot_order = jnp.arange(slot_count, dtype=jnp.int32)
    earlier_same = (owners[:, None] == owners[None, :]) & (
        slot_order[None, :] < slot_order[:, None]
    )
    slot_ranks = jnp.sum(earlier_same.astype(jnp.int32), axis=1)
    send_keys = owners * CAP + slot_ranks
    send_ids = jnp.arange(device_count * CAP, dtype=jnp.int32)
    send_pick = (send_keys[:, None] == send_ids[None, :]).astype(jnp.float32)
    outbound = jnp.einsum(
        "lk,ld->kd", send_pick, slot_total, precision=lax.Precision.HIGHEST
    ).reshape(device_count, CAP, model_width)
    labels = jnp.einsum(
        "lk,l->k", send_pick, local_rows.astype(jnp.float32), precision=lax.Precision.HIGHEST
    ).reshape(device_count, CAP)
    label_row = jnp.zeros((device_count, 1, model_width), jnp.float32)
    label_row = label_row.at[:, 0, :CAP].set(labels)
    packed = jnp.concatenate([outbound, label_row], axis=1).astype(jnp.bfloat16)
    arrived = lax.all_to_all(
        packed, ("blk", "rep"), split_axis=0, concat_axis=0, tiled=True
    ).astype(jnp.float32)
    inbound = arrived[:, :CAP, :]
    inbound_labels = arrived[:, CAP, :CAP]
    table_rows = jnp.arange(SH_DEV, dtype=jnp.int32)
    selector = (
        inbound_labels.reshape(-1).astype(jnp.int32)[:, None] == table_rows[None, :]
    ).astype(jnp.float32)
    shared_grad = jnp.einsum(
        "rs,rd->sd",
        selector,
        inbound.reshape(-1, model_width),
        preferred_element_type=jnp.float32,
        precision=lax.Precision.HIGHEST,
    )
    own_shared = lax.dynamic_slice_in_dim(shared_table, device_place * SH_DEV, SH_DEV, 0)
    new_shared, new_shared_state = row_adagrad(own_shared, shared_state, shared_grad)
    return (new_entities, new_entity_state, new_shared, new_shared_state)


def solution(mesh):
    return jax.shard_map(
        shards,
        mesh=mesh,
        in_specs=(
            P("blk", None),
            P(("blk", "rep")),
            P(),
            P(("blk", "rep")),
            P("blk", None, "rep"),
            P("blk", None, "rep"),
            P("blk", None, "rep"),
            P("blk", None, "rep", None),
            P("blk", "rep", None),
            P("blk", "rep"),
        ),
        out_specs=(
            P(("blk", "rep"), None),
            P(("blk", "rep")),
            P(("blk", "rep"), None),
            P(("blk", "rep")),
        ),
        check_vma=False,
    )
```

```python
import jax
import jax.numpy as jnp
from jax import lax
from jax.sharding import PartitionSpec as P

CAP = 4
SH_DEV = 64
INDEX_SPLIT = 64


learn_rate = 0.1
negative_weight = 8.0


def passed_along(value, axis, by):
    peers = lax.axis_size(axis)
    return lax.ppermute(value, axis, [(i, (i + by) % peers) for i in range(peers)])


def make_query(resident, sources, slots, shared_rows):
    part_rows = resident.shape[0]
    entity_ids = jnp.arange(part_rows, dtype=jnp.int32)
    list_ids = jnp.arange(shared_rows.shape[0], dtype=jnp.int32)
    source_pick = (sources[:, None] == entity_ids[None, :]).astype(jnp.bfloat16)
    slot_pick = (slots[:, None] == list_ids[None, :]).astype(jnp.bfloat16)
    source_rows = jnp.dot(source_pick, resident, preferred_element_type=jnp.float32)
    shared_part = jnp.dot(slot_pick, shared_rows, preferred_element_type=jnp.float32)
    query = (source_rows + shared_part).astype(jnp.bfloat16)
    return query, source_pick, slot_pick


def target_side(visiting, query, targets, negatives):
    part_rows = visiting.shape[0]
    model_width = visiting.shape[1]
    group_count = negatives.shape[0]
    sample_count = negatives.shape[1]
    entity_ids = jnp.arange(part_rows, dtype=jnp.int32)
    target_pick = (targets[:, None] == entity_ids[None, :]).astype(jnp.bfloat16)
    sample_pick = (negatives[:, :, None] == entity_ids[None, None, :]).astype(jnp.bfloat16)
    target_rows = jnp.dot(target_pick, visiting, preferred_element_type=jnp.float32).astype(
        jnp.bfloat16
    )
    positive = jnp.einsum("ed,ed->e", query, target_rows, preferred_element_type=jnp.float32)
    query_groups = query.reshape(group_count, -1, model_width)
    samples = jnp.einsum(
        "cnx,xd->cnd", sample_pick, visiting, preferred_element_type=jnp.float32
    ).astype(jnp.bfloat16)
    negative = jnp.einsum("cqd,cnd->cqn", query_groups, samples, preferred_element_type=jnp.float32)
    positive_weight = -jax.nn.sigmoid(-positive)
    sample_weight = (jax.nn.sigmoid(negative) * (negative_weight / sample_count)).astype(
        jnp.bfloat16
    )
    sampled_sum = jnp.einsum(
        "cqn,cnd->cqd", sample_weight, samples, preferred_element_type=jnp.float32
    )
    query_grad = positive_weight[:, None] * target_rows.astype(jnp.float32) + sampled_sum.reshape(
        -1, model_width
    )
    weight_map = jnp.einsum(
        "cnx,cqn->xcq", sample_pick, sample_weight, preferred_element_type=jnp.float32
    ).reshape(part_rows, -1)
    weight_map = weight_map + jnp.einsum(
        "ex,e->xe", target_pick.astype(jnp.float32), positive_weight
    )
    visiting_grad = split_dot("xe,ed->xd", weight_map, query)
    return query_grad, visiting_grad


def split_dot(spec, wide, narrow):
    high = wide.astype(jnp.bfloat16)
    low = (wide - high.astype(jnp.float32)).astype(jnp.bfloat16)
    return jnp.einsum(spec, high, narrow, preferred_element_type=jnp.float32) + jnp.einsum(
        spec, low, narrow, preferred_element_type=jnp.float32
    )


def rep_reduce(total):
    rep_count = lax.axis_size("rep")
    rep_place = lax.axis_index("rep")
    pieces = total.reshape(rep_count, -1, total.shape[1])
    own = lax.dynamic_index_in_dim(pieces, rep_place, 0, keepdims=False)
    for shift in range(1, rep_count):
        outgoing = lax.dynamic_index_in_dim(
            pieces, (rep_place + shift) % rep_count, 0, keepdims=False
        ).astype(jnp.bfloat16)
        own = own + passed_along(outgoing, "rep", shift).astype(jnp.float32)
    return own


def row_adagrad(rows, state, grad):
    new_state = state + jnp.mean(grad * grad, axis=-1)
    return (rows.astype(jnp.float32) - learn_rate * grad / jnp.sqrt(new_state)[:, None], new_state)


def shards(
    entities,
    entity_state,
    shared_table,
    shared_state,
    edge_src,
    edge_dst,
    edge_slot,
    neg_rows,
    list_owner,
    list_row,
):
    rep_count = lax.axis_size("rep")
    rep_place = lax.axis_index("rep")
    device_count = lax.axis_size("blk") * rep_count
    device_place = lax.axis_index("blk") * rep_count + rep_place
    part_rows = entities.shape[0]
    model_width = entities.shape[1]
    share_rows = part_rows // rep_count
    bucket_count = edge_src.shape[1]
    edge_count = edge_src.shape[2]
    owners = list_owner[0, :, 0]
    local_rows = list_row[0]
    shared_rows = shared_table[owners * SH_DEV + local_rows]
    queries = []
    picks = []
    for bucket in range(bucket_count):
        query, source_pick, slot_pick = make_query(
            entities, edge_src[0, bucket], edge_slot[0, bucket], shared_rows
        )
        queries.append(query)
        picks.append((source_pick, slot_pick))
    arrivals = []
    for bucket in range(bucket_count):
        indices = jnp.concatenate([edge_dst[0, bucket], neg_rows[0, bucket].reshape(-1)])
        if bucket == 0:
            arrivals.append((queries[bucket], indices))
        else:
            coded = jnp.stack([indices // INDEX_SPLIT, indices % INDEX_SPLIT]).astype(jnp.bfloat16)
            parcel = jnp.concatenate([queries[bucket], coded.reshape(-1, model_width)], axis=0)
            parcel = passed_along(parcel, "blk", -bucket)
            coded = parcel[edge_count:].reshape(2, -1).astype(jnp.int32)
            arrivals.append((parcel[:edge_count], coded[0] * INDEX_SPLIT + coded[1]))
    group_shape = neg_rows.shape[2:]
    target_total = jnp.zeros((part_rows, model_width), jnp.float32)
    returned = [None] * bucket_count
    for bucket in [0] + list(range(bucket_count - 1, 0, -1)):
        query, indices = arrivals[bucket]
        targets = indices[:edge_count]
        negatives = indices[edge_count:].reshape(group_shape)
        query_grad, visiting_grad = target_side(entities, query, targets, negatives)
        target_total = target_total + visiting_grad
        if bucket == 0:
            returned[bucket] = query_grad
        else:
            returned[bucket] = passed_along(query_grad, "blk", bucket)
    source_total = target_total
    slot_total = jnp.zeros((owners.shape[0], model_width), jnp.float32)
    for bucket in [0] + list(range(bucket_count - 1, 0, -1)):
        source_pick, slot_pick = picks[bucket]
        query_grad = returned[bucket]
        source_total = source_total + split_dot("ed,ex->xd", query_grad, source_pick)
        slot_total = slot_total + split_dot("ed,el->ld", query_grad, slot_pick)
    own_grad = rep_reduce(source_total)
    own_entities = lax.dynamic_slice_in_dim(entities, rep_place * share_rows, share_rows, 0)
    new_entities, new_entity_state = row_adagrad(own_entities, entity_state, own_grad)
    slot_count = owners.shape[0]
    slot_order = jnp.arange(slot_count, dtype=jnp.int32)
    earlier_same = (owners[:, None] == owners[None, :]) & (
        slot_order[None, :] < slot_order[:, None]
    )
    slot_ranks = jnp.sum(earlier_same.astype(jnp.int32), axis=1)
    send_keys = owners * CAP + slot_ranks
    send_ids = jnp.arange(device_count * CAP, dtype=jnp.int32)
    send_pick = (send_keys[:, None] == send_ids[None, :]).astype(jnp.float32)
    outbound = jnp.einsum(
        "lk,ld->kd", send_pick, slot_total, precision=lax.Precision.HIGHEST
    ).reshape(device_count, CAP, model_width)
    labels = jnp.einsum(
        "lk,l->k", send_pick, local_rows.astype(jnp.float32), precision=lax.Precision.HIGHEST
    ).reshape(device_count, CAP)
    label_row = jnp.zeros((device_count, 1, model_width), jnp.float32)
    label_row = label_row.at[:, 0, :CAP].set(labels)
    packed = jnp.concatenate([outbound, label_row], axis=1).astype(jnp.bfloat16)
    arrived = lax.all_to_all(
        packed, ("blk", "rep"), split_axis=0, concat_axis=0, tiled=True
    ).astype(jnp.float32)
    inbound = arrived[:, :CAP, :]
    inbound_labels = arrived[:, CAP, :CAP]
    table_rows = jnp.arange(SH_DEV, dtype=jnp.int32)
    selector = (
        inbound_labels.reshape(-1).astype(jnp.int32)[:, None] == table_rows[None, :]
    ).astype(jnp.float32)
    shared_grad = jnp.einsum(
        "rs,rd->sd",
        selector,
        inbound.reshape(-1, model_width),
        preferred_element_type=jnp.float32,
        precision=lax.Precision.HIGHEST,
    )
    own_shared = lax.dynamic_slice_in_dim(shared_table, device_place * SH_DEV, SH_DEV, 0)
    new_shared, new_shared_state = row_adagrad(own_shared, shared_state, shared_grad)
    return (new_entities, new_entity_state, new_shared, new_shared_state)


def solution(mesh):
    return jax.shard_map(
        shards,
        mesh=mesh,
        in_specs=(
            P("blk", None),
            P(("blk", "rep")),
            P(),
            P(("blk", "rep")),
            P("blk", None, "rep"),
            P("blk", None, "rep"),
            P("blk", None, "rep"),
            P("blk", None, "rep", None),
            P("blk", "rep", None),
            P("blk", "rep"),
        ),
        out_specs=(
            P(("blk", "rep"), None),
            P(("blk", "rep")),
            P(("blk", "rep"), None),
            P(("blk", "rep")),
        ),
        check_vma=False,
    )
```

```python
import jax
import jax.numpy as jnp
from jax import lax
from jax.sharding import PartitionSpec as P

CAP = 4
SH_DEV = 64
INDEX_SPLIT = 64


learn_rate = 0.1
negative_weight = 8.0


def passed_along(value, axis, by):
    peers = lax.axis_size(axis)
    return lax.ppermute(value, axis, [(i, (i + by) % peers) for i in range(peers)])


def make_query(resident, sources, slots, shared_rows):
    part_rows = resident.shape[0]
    entity_ids = jnp.arange(part_rows, dtype=jnp.int32)
    list_ids = jnp.arange(shared_rows.shape[0], dtype=jnp.int32)
    source_pick = (sources[:, None] == entity_ids[None, :]).astype(jnp.bfloat16)
    slot_pick = (slots[:, None] == list_ids[None, :]).astype(jnp.bfloat16)
    source_rows = jnp.dot(source_pick, resident, preferred_element_type=jnp.float32)
    shared_part = jnp.dot(slot_pick, shared_rows, preferred_element_type=jnp.float32)
    query = (source_rows + shared_part).astype(jnp.bfloat16)
    return query, source_pick, slot_pick


def target_side(visiting, query, targets, negatives):
    part_rows = visiting.shape[0]
    model_width = visiting.shape[1]
    group_count = negatives.shape[0]
    sample_count = negatives.shape[1]
    entity_ids = jnp.arange(part_rows, dtype=jnp.int32)
    target_pick = (targets[:, None] == entity_ids[None, :]).astype(jnp.bfloat16)
    sample_pick = (negatives[:, :, None] == entity_ids[None, None, :]).astype(jnp.bfloat16)
    target_rows = jnp.dot(target_pick, visiting, preferred_element_type=jnp.float32).astype(
        jnp.bfloat16
    )
    positive = jnp.einsum("ed,ed->e", query, target_rows, preferred_element_type=jnp.float32)
    query_groups = query.reshape(group_count, -1, model_width)
    samples = jnp.einsum(
        "cnx,xd->cnd", sample_pick, visiting, preferred_element_type=jnp.float32
    ).astype(jnp.bfloat16)
    negative = jnp.einsum("cqd,cnd->cqn", query_groups, samples, preferred_element_type=jnp.float32)
    positive_weight = -jax.nn.sigmoid(-positive)
    sample_weight = (jax.nn.sigmoid(negative) * (negative_weight / sample_count)).astype(
        jnp.bfloat16
    )
    sampled_sum = jnp.einsum(
        "cqn,cnd->cqd", sample_weight, samples, preferred_element_type=jnp.float32
    )
    query_grad = positive_weight[:, None] * target_rows.astype(jnp.float32) + sampled_sum.reshape(
        -1, model_width
    )
    weight_map = jnp.einsum(
        "cnx,cqn->xcq", sample_pick, sample_weight, preferred_element_type=jnp.float32
    ).reshape(part_rows, -1)
    weight_map = weight_map + jnp.einsum(
        "ex,e->xe", target_pick.astype(jnp.float32), positive_weight
    )
    visiting_grad = split_dot("xe,ed->xd", weight_map, query)
    return query_grad, visiting_grad


def split_dot(spec, wide, narrow):
    high = wide.astype(jnp.bfloat16)
    low = (wide - high.astype(jnp.float32)).astype(jnp.bfloat16)
    return jnp.einsum(spec, high, narrow, preferred_element_type=jnp.float32) + jnp.einsum(
        spec, low, narrow, preferred_element_type=jnp.float32
    )


def rep_reduce(total):
    rep_count = lax.axis_size("rep")
    rep_place = lax.axis_index("rep")
    pieces = total.reshape(rep_count, -1, total.shape[1])
    own = lax.dynamic_index_in_dim(pieces, rep_place, 0, keepdims=False)
    for shift in range(1, rep_count):
        outgoing = lax.dynamic_index_in_dim(
            pieces, (rep_place + shift) % rep_count, 0, keepdims=False
        ).astype(jnp.bfloat16)
        own = own + passed_along(outgoing, "rep", shift).astype(jnp.float32)
    return own


def row_adagrad(rows, state, grad):
    new_state = state + jnp.mean(grad * grad, axis=-1)
    return (rows.astype(jnp.float32) - learn_rate * grad / jnp.sqrt(new_state)[:, None], new_state)


def shards(
    entities,
    entity_state,
    shared_table,
    shared_state,
    edge_src,
    edge_dst,
    edge_slot,
    neg_rows,
    list_owner,
    list_row,
):
    rep_count = lax.axis_size("rep")
    rep_place = lax.axis_index("rep")
    device_count = lax.axis_size("blk") * rep_count
    device_place = lax.axis_index("blk") * rep_count + rep_place
    part_rows = entities.shape[0]
    model_width = entities.shape[1]
    share_rows = part_rows // rep_count
    bucket_count = edge_src.shape[1]
    edge_count = edge_src.shape[2]
    owners = list_owner[0, :, 0]
    local_rows = list_row[0]
    table_ids = jnp.arange(shared_table.shape[0], dtype=jnp.int32)
    table_pick = ((owners * SH_DEV + local_rows)[:, None] == table_ids[None, :]).astype(jnp.bfloat16)
    shared_rows = jnp.dot(table_pick, shared_table, preferred_element_type=jnp.float32).astype(
        jnp.bfloat16
    )
    queries = []
    picks = []
    for bucket in range(bucket_count):
        query, source_pick, slot_pick = make_query(
            entities, edge_src[0, bucket], edge_slot[0, bucket], shared_rows
        )
        queries.append(query)
        picks.append((source_pick, slot_pick))
    arrivals = []
    for bucket in range(bucket_count):
        indices = jnp.concatenate([edge_dst[0, bucket], neg_rows[0, bucket].reshape(-1)])
        if bucket == 0:
            arrivals.append((queries[bucket], indices))
        else:
            coded = jnp.stack([indices // INDEX_SPLIT, indices % INDEX_SPLIT]).astype(jnp.bfloat16)
            parcel = jnp.concatenate([queries[bucket], coded.reshape(-1, model_width)], axis=0)
            parcel = passed_along(parcel, "blk", -bucket)
            coded = parcel[edge_count:].reshape(2, -1).astype(jnp.int32)
            arrivals.append((parcel[:edge_count], coded[0] * INDEX_SPLIT + coded[1]))
    group_shape = neg_rows.shape[2:]
    target_total = jnp.zeros((part_rows, model_width), jnp.float32)
    returned = [None] * bucket_count
    for bucket in [0] + list(range(bucket_count - 1, 0, -1)):
        query, indices = arrivals[bucket]
        targets = indices[:edge_count]
        negatives = indices[edge_count:].reshape(group_shape)
        query_grad, visiting_grad = target_side(entities, query, targets, negatives)
        target_total = target_total + visiting_grad
        if bucket == 0:
            returned[bucket] = query_grad
        else:
            returned[bucket] = passed_along(query_grad.astype(jnp.bfloat16), "blk", bucket)
    source_total = target_total
    slot_total = jnp.zeros((owners.shape[0], model_width), jnp.float32)
    for bucket in [0] + list(range(bucket_count - 1, 0, -1)):
        source_pick, slot_pick = picks[bucket]
        query_grad = returned[bucket]
        if query_grad.dtype == jnp.float32:
            source_total = source_total + split_dot("ed,ex->xd", query_grad, source_pick)
            slot_total = slot_total + split_dot("ed,el->ld", query_grad, slot_pick)
        else:
            source_total = source_total + jnp.einsum(
                "ed,ex->xd", query_grad, source_pick, preferred_element_type=jnp.float32
            )
            slot_total = slot_total + jnp.einsum(
                "ed,el->ld", query_grad, slot_pick, preferred_element_type=jnp.float32
            )
    own_grad = rep_reduce(source_total)
    own_entities = lax.dynamic_slice_in_dim(entities, rep_place * share_rows, share_rows, 0)
    new_entities, new_entity_state = row_adagrad(own_entities, entity_state, own_grad)
    slot_count = owners.shape[0]
    slot_order = jnp.arange(slot_count, dtype=jnp.int32)
    earlier_same = (owners[:, None] == owners[None, :]) & (
        slot_order[None, :] < slot_order[:, None]
    )
    slot_ranks = jnp.sum(earlier_same.astype(jnp.int32), axis=1)
    send_keys = owners * CAP + slot_ranks
    send_ids = jnp.arange(device_count * CAP, dtype=jnp.int32)
    send_pick = (send_keys[:, None] == send_ids[None, :]).astype(jnp.float32)
    outbound = jnp.einsum(
        "lk,ld->kd", send_pick, slot_total, precision=lax.Precision.HIGHEST
    ).reshape(device_count, CAP, model_width)
    labels = jnp.einsum(
        "lk,l->k", send_pick, local_rows.astype(jnp.float32), precision=lax.Precision.HIGHEST
    ).reshape(device_count, CAP)
    label_row = jnp.zeros((device_count, 1, model_width), jnp.float32)
    label_row = label_row.at[:, 0, :CAP].set(labels)
    packed = jnp.concatenate([outbound, label_row], axis=1).astype(jnp.bfloat16)
    arrived = lax.all_to_all(
        packed, ("blk", "rep"), split_axis=0, concat_axis=0, tiled=True
    ).astype(jnp.float32)
    inbound = arrived[:, :CAP, :]
    inbound_labels = arrived[:, CAP, :CAP]
    table_rows = jnp.arange(SH_DEV, dtype=jnp.int32)
    selector = (
        inbound_labels.reshape(-1).astype(jnp.int32)[:, None] == table_rows[None, :]
    ).astype(jnp.float32)
    shared_grad = jnp.einsum(
        "rs,rd->sd",
        selector,
        inbound.reshape(-1, model_width),
        preferred_element_type=jnp.float32,
        precision=lax.Precision.HIGHEST,
    )
    own_shared = lax.dynamic_slice_in_dim(shared_table, device_place * SH_DEV, SH_DEV, 0)
    new_shared, new_shared_state = row_adagrad(own_shared, shared_state, shared_grad)
    return (new_entities, new_entity_state, new_shared, new_shared_state)


def solution(mesh):
    return jax.shard_map(
        shards,
        mesh=mesh,
        in_specs=(
            P("blk", None),
            P(("blk", "rep")),
            P(),
            P(("blk", "rep")),
            P("blk", None, "rep"),
            P("blk", None, "rep"),
            P("blk", None, "rep"),
            P("blk", None, "rep", None),
            P("blk", "rep", None),
            P("blk", "rep"),
        ),
        out_specs=(
            P(("blk", "rep"), None),
            P(("blk", "rep")),
            P(("blk", "rep"), None),
            P(("blk", "rep")),
        ),
        check_vma=False,
    )
```

```python
import jax
import jax.numpy as jnp
from jax import lax
from jax.sharding import PartitionSpec as P

CAP = 4
SH_DEV = 64
INDEX_SPLIT = 64


learn_rate = 0.1
negative_weight = 8.0


def passed_along(value, axis, by):
    peers = lax.axis_size(axis)
    return lax.ppermute(value, axis, [(i, (i + by) % peers) for i in range(peers)])


def make_query(resident, sources, slots, shared_rows):
    part_rows = resident.shape[0]
    entity_ids = jnp.arange(part_rows, dtype=jnp.int32)
    list_ids = jnp.arange(shared_rows.shape[0], dtype=jnp.int32)
    source_pick = (sources[:, None] == entity_ids[None, :]).astype(jnp.bfloat16)
    slot_pick = (slots[:, None] == list_ids[None, :]).astype(jnp.bfloat16)
    source_rows = jnp.dot(source_pick, resident, preferred_element_type=jnp.float32)
    shared_part = jnp.dot(slot_pick, shared_rows, preferred_element_type=jnp.float32)
    query = (source_rows + shared_part).astype(jnp.bfloat16)
    return query, source_pick, slot_pick


def target_side(visiting, query, targets, negatives):
    part_rows = visiting.shape[0]
    model_width = visiting.shape[1]
    group_count = negatives.shape[0]
    sample_count = negatives.shape[1]
    entity_ids = jnp.arange(part_rows, dtype=jnp.int32)
    target_pick = (targets[:, None] == entity_ids[None, :]).astype(jnp.bfloat16)
    sample_pick = (negatives[:, :, None] == entity_ids[None, None, :]).astype(jnp.bfloat16)
    target_rows = jnp.dot(target_pick, visiting, preferred_element_type=jnp.float32).astype(
        jnp.bfloat16
    )
    positive = jnp.einsum("ed,ed->e", query, target_rows, preferred_element_type=jnp.float32)
    query_groups = query.reshape(group_count, -1, model_width)
    samples = jnp.einsum(
        "cnx,xd->cnd", sample_pick, visiting, preferred_element_type=jnp.float32
    ).astype(jnp.bfloat16)
    negative = jnp.einsum("cqd,cnd->cqn", query_groups, samples, preferred_element_type=jnp.float32)
    positive_weight = -jax.nn.sigmoid(-positive)
    sample_weight = (jax.nn.sigmoid(negative) * (negative_weight / sample_count)).astype(
        jnp.bfloat16
    )
    sampled_sum = jnp.einsum(
        "cqn,cnd->cqd", sample_weight, samples, preferred_element_type=jnp.float32
    )
    query_grad = positive_weight[:, None] * target_rows.astype(jnp.float32) + sampled_sum.reshape(
        -1, model_width
    )
    weight_map = jnp.einsum(
        "cnx,cqn->xcq", sample_pick, sample_weight, preferred_element_type=jnp.float32
    ).reshape(part_rows, -1)
    weight_map = weight_map + jnp.einsum(
        "ex,e->xe", target_pick.astype(jnp.float32), positive_weight
    )
    visiting_grad = split_dot("xe,ed->xd", weight_map, query)
    return query_grad, visiting_grad


def split_dot(spec, wide, narrow):
    high = wide.astype(jnp.bfloat16)
    low = (wide - high.astype(jnp.float32)).astype(jnp.bfloat16)
    return jnp.einsum(spec, high, narrow, preferred_element_type=jnp.float32) + jnp.einsum(
        spec, low, narrow, preferred_element_type=jnp.float32
    )


def rep_reduce(total):
    rep_count = lax.axis_size("rep")
    pieces = total.reshape(rep_count, -1, total.shape[1]).astype(jnp.bfloat16)
    pieces = lax.all_to_all(pieces, "rep", split_axis=0, concat_axis=0, tiled=True)
    return jnp.sum(pieces, axis=0, dtype=jnp.float32)


def row_adagrad(rows, state, grad):
    new_state = state + jnp.mean(grad * grad, axis=-1)
    return (rows.astype(jnp.float32) - learn_rate * grad / jnp.sqrt(new_state)[:, None], new_state)


def shards(
    entities,
    entity_state,
    shared_table,
    shared_state,
    edge_src,
    edge_dst,
    edge_slot,
    neg_rows,
    list_owner,
    list_row,
):
    rep_count = lax.axis_size("rep")
    rep_place = lax.axis_index("rep")
    device_count = lax.axis_size("blk") * rep_count
    device_place = lax.axis_index("blk") * rep_count + rep_place
    part_rows = entities.shape[0]
    model_width = entities.shape[1]
    share_rows = part_rows // rep_count
    bucket_count = edge_src.shape[1]
    edge_count = edge_src.shape[2]
    owners = list_owner[0, :, 0]
    local_rows = list_row[0]
    table_ids = jnp.arange(shared_table.shape[0], dtype=jnp.int32)
    table_pick = ((owners * SH_DEV + local_rows)[:, None] == table_ids[None, :]).astype(jnp.bfloat16)
    shared_rows = jnp.dot(table_pick, shared_table, preferred_element_type=jnp.float32).astype(
        jnp.bfloat16
    )
    queries = []
    picks = []
    for bucket in range(bucket_count):
        query, source_pick, slot_pick = make_query(
            entities, edge_src[0, bucket], edge_slot[0, bucket], shared_rows
        )
        queries.append(query)
        picks.append((source_pick, slot_pick))
    arrivals = []
    for bucket in range(bucket_count):
        indices = jnp.concatenate([edge_dst[0, bucket], neg_rows[0, bucket].reshape(-1)])
        if bucket == 0:
            arrivals.append((queries[bucket], indices))
        else:
            coded = jnp.stack([indices // INDEX_SPLIT, indices % INDEX_SPLIT]).astype(jnp.bfloat16)
            parcel = jnp.concatenate([queries[bucket], coded.reshape(-1, model_width)], axis=0)
            parcel = passed_along(parcel, "blk", -bucket)
            coded = parcel[edge_count:].reshape(2, -1).astype(jnp.int32)
            arrivals.append((parcel[:edge_count], coded[0] * INDEX_SPLIT + coded[1]))
    group_shape = neg_rows.shape[2:]
    target_total = jnp.zeros((part_rows, model_width), jnp.float32)
    returned = [None] * bucket_count
    for bucket in [0] + list(range(bucket_count - 1, 0, -1)):
        query, indices = arrivals[bucket]
        targets = indices[:edge_count]
        negatives = indices[edge_count:].reshape(group_shape)
        query_grad, visiting_grad = target_side(entities, query, targets, negatives)
        target_total = target_total + visiting_grad
        if bucket == 0:
            returned[bucket] = query_grad
        else:
            returned[bucket] = passed_along(query_grad.astype(jnp.bfloat16), "blk", bucket)
    source_total = target_total
    slot_total = jnp.zeros((owners.shape[0], model_width), jnp.float32)
    for bucket in [0] + list(range(bucket_count - 1, 0, -1)):
        source_pick, slot_pick = picks[bucket]
        query_grad = returned[bucket]
        if query_grad.dtype == jnp.float32:
            source_total = source_total + split_dot("ed,ex->xd", query_grad, source_pick)
            slot_total = slot_total + split_dot("ed,el->ld", query_grad, slot_pick)
        else:
            source_total = source_total + jnp.einsum(
                "ed,ex->xd", query_grad, source_pick, preferred_element_type=jnp.float32
            )
            slot_total = slot_total + jnp.einsum(
                "ed,el->ld", query_grad, slot_pick, preferred_element_type=jnp.float32
            )
    own_grad = rep_reduce(source_total)
    own_entities = lax.dynamic_slice_in_dim(entities, rep_place * share_rows, share_rows, 0)
    new_entities, new_entity_state = row_adagrad(own_entities, entity_state, own_grad)
    slot_count = owners.shape[0]
    slot_order = jnp.arange(slot_count, dtype=jnp.int32)
    earlier_same = (owners[:, None] == owners[None, :]) & (
        slot_order[None, :] < slot_order[:, None]
    )
    slot_ranks = jnp.sum(earlier_same.astype(jnp.int32), axis=1)
    send_keys = owners * CAP + slot_ranks
    send_ids = jnp.arange(device_count * CAP, dtype=jnp.int32)
    send_pick = (send_keys[:, None] == send_ids[None, :]).astype(jnp.float32)
    outbound = jnp.einsum(
        "lk,ld->kd", send_pick, slot_total, precision=lax.Precision.HIGHEST
    ).reshape(device_count, CAP, model_width)
    labels = jnp.einsum(
        "lk,l->k", send_pick, local_rows.astype(jnp.float32), precision=lax.Precision.HIGHEST
    ).reshape(device_count, CAP)
    label_row = jnp.zeros((device_count, 1, model_width), jnp.float32)
    label_row = label_row.at[:, 0, :CAP].set(labels)
    packed = jnp.concatenate([outbound, label_row], axis=1).astype(jnp.bfloat16)
    arrived = lax.all_to_all(
        packed, ("blk", "rep"), split_axis=0, concat_axis=0, tiled=True
    ).astype(jnp.float32)
    inbound = arrived[:, :CAP, :]
    inbound_labels = arrived[:, CAP, :CAP]
    table_rows = jnp.arange(SH_DEV, dtype=jnp.int32)
    selector = (
        inbound_labels.reshape(-1).astype(jnp.int32)[:, None] == table_rows[None, :]
    ).astype(jnp.float32)
    shared_grad = jnp.einsum(
        "rs,rd->sd",
        selector,
        inbound.reshape(-1, model_width),
        preferred_element_type=jnp.float32,
        precision=lax.Precision.HIGHEST,
    )
    own_shared = lax.dynamic_slice_in_dim(shared_table, device_place * SH_DEV, SH_DEV, 0)
    new_shared, new_shared_state = row_adagrad(own_shared, shared_state, shared_grad)
    return (new_entities, new_entity_state, new_shared, new_shared_state)


def solution(mesh):
    return jax.shard_map(
        shards,
        mesh=mesh,
        in_specs=(
            P("blk", None),
            P(("blk", "rep")),
            P(),
            P(("blk", "rep")),
            P("blk", None, "rep"),
            P("blk", None, "rep"),
            P("blk", None, "rep"),
            P("blk", None, "rep", None),
            P("blk", "rep", None),
            P("blk", "rep"),
        ),
        out_specs=(
            P(("blk", "rep"), None),
            P(("blk", "rep")),
            P(("blk", "rep"), None),
            P(("blk", "rep")),
        ),
        check_vma=False,
    )
```

```python
import jax
import jax.numpy as jnp
from jax import lax
from jax.experimental import pallas as pl
from jax.sharding import PartitionSpec as P

CAP = 4
SH_DEV = 64
INDEX_SPLIT = 64


learn_rate = 0.1
negative_weight = 8.0


def passed_along(value, axis, by):
    peers = lax.axis_size(axis)
    return lax.ppermute(value, axis, [(i, (i + by) % peers) for i in range(peers)])


def make_query(resident, sources, slots, shared_rows):
    part_rows = resident.shape[0]
    entity_ids = jnp.arange(part_rows, dtype=jnp.int32)
    list_ids = jnp.arange(shared_rows.shape[0], dtype=jnp.int32)
    source_pick = (sources[:, None] == entity_ids[None, :]).astype(jnp.bfloat16)
    slot_pick = (slots[:, None] == list_ids[None, :]).astype(jnp.bfloat16)
    source_rows = jnp.dot(source_pick, resident, preferred_element_type=jnp.float32)
    shared_part = jnp.dot(slot_pick, shared_rows, preferred_element_type=jnp.float32)
    query = (source_rows + shared_part).astype(jnp.bfloat16)
    return query, source_pick, slot_pick


def target_side(visiting, query, targets, negatives):
    part_rows = visiting.shape[0]
    model_width = visiting.shape[1]
    group_count = negatives.shape[0]
    sample_count = negatives.shape[1]
    entity_ids = jnp.arange(part_rows, dtype=jnp.int32)
    target_pick = (targets[:, None] == entity_ids[None, :]).astype(jnp.bfloat16)
    sample_pick = (negatives[:, :, None] == entity_ids[None, None, :]).astype(jnp.bfloat16)
    target_rows = jnp.dot(target_pick, visiting, preferred_element_type=jnp.float32).astype(
        jnp.bfloat16
    )
    positive = jnp.einsum("ed,ed->e", query, target_rows, preferred_element_type=jnp.float32)
    query_groups = query.reshape(group_count, -1, model_width)
    samples = jnp.einsum(
        "cnx,xd->cnd", sample_pick, visiting, preferred_element_type=jnp.float32
    ).astype(jnp.bfloat16)
    negative = jnp.einsum("cqd,cnd->cqn", query_groups, samples, preferred_element_type=jnp.float32)
    positive_weight = -jax.nn.sigmoid(-positive)
    sample_weight = (jax.nn.sigmoid(negative) * (negative_weight / sample_count)).astype(
        jnp.bfloat16
    )
    sampled_sum = jnp.einsum(
        "cqn,cnd->cqd", sample_weight, samples, preferred_element_type=jnp.float32
    )
    query_grad = positive_weight[:, None] * target_rows.astype(jnp.float32) + sampled_sum.reshape(
        -1, model_width
    )
    weight_map = jnp.einsum(
        "cnx,cqn->xcq", sample_pick, sample_weight, preferred_element_type=jnp.float32
    ).reshape(part_rows, -1)
    weight_map = weight_map + jnp.einsum(
        "ex,e->xe", target_pick.astype(jnp.float32), positive_weight
    )
    visiting_grad = split_dot("xe,ed->xd", weight_map, query)
    return query_grad, visiting_grad


def _target_kernel(neg_ref, tgt_ref, q_ref, v_ref, qg_ref, vg_ref):
    group = pl.program_id(0)
    idx = neg_ref[0]
    tidx = tgt_ref[0]
    query = q_ref[0]
    table = v_ref[...]
    sample_count = idx.shape[0]
    part_rows = table.shape[0]
    lanes = lax.broadcasted_iota(jnp.int32, (sample_count, part_rows), 1)
    pick = (idx == lanes).astype(jnp.bfloat16)
    samples = jnp.dot(pick, table, preferred_element_type=jnp.float32).astype(jnp.bfloat16)
    negative = lax.dot_general(
        query, samples, (((1,), (1,)), ((), ())), preferred_element_type=jnp.float32
    )
    sample_weight = (
        (1.0 / (1.0 + jnp.exp(-negative))) * (negative_weight / sample_count)
    ).astype(jnp.bfloat16)
    sampled_sum = jnp.dot(sample_weight, samples, preferred_element_type=jnp.float32)
    target_lanes = lax.broadcasted_iota(jnp.int32, (tidx.shape[0], part_rows), 1)
    target_pick = (tidx == target_lanes).astype(jnp.bfloat16)
    target_rows = jnp.dot(target_pick, table, preferred_element_type=jnp.float32).astype(
        jnp.bfloat16
    ).astype(jnp.float32)
    positive = jnp.sum(query.astype(jnp.float32) * target_rows, axis=1, keepdims=True)
    positive_weight = -(1.0 / (1.0 + jnp.exp(positive)))
    qg_ref[0] = positive_weight * target_rows + sampled_sum
    weight_map = jnp.dot(sample_weight, pick, preferred_element_type=jnp.float32)
    weight_map = (weight_map + positive_weight * target_pick.astype(jnp.float32)).T
    high = weight_map.astype(jnp.bfloat16)
    low = (weight_map - high.astype(jnp.float32)).astype(jnp.bfloat16)
    grad = jnp.dot(high, query, preferred_element_type=jnp.float32) + jnp.dot(
        low, query, preferred_element_type=jnp.float32
    )

    @pl.when(group == 0)
    def _():
        vg_ref[...] = grad

    @pl.when(group > 0)
    def _():
        vg_ref[...] = vg_ref[...] + grad


def target_side_kernel(visiting, query, targets, negatives):
    part_rows, model_width = visiting.shape
    group_count, sample_count = negatives.shape
    group_size = query.shape[0] // group_count
    query_groups = query.reshape(group_count, group_size, model_width)
    query_grad, visiting_grad = pl.pallas_call(
        _target_kernel,
        grid=(group_count,),
        in_specs=[
            pl.BlockSpec((1, sample_count, 1), lambda c: (c, 0, 0)),
            pl.BlockSpec((1, group_size, 1), lambda c: (c, 0, 0)),
            pl.BlockSpec((1, group_size, model_width), lambda c: (c, 0, 0)),
            pl.BlockSpec((part_rows, model_width), lambda c: (0, 0)),
        ],
        out_specs=[
            pl.BlockSpec((1, group_size, model_width), lambda c: (c, 0, 0)),
            pl.BlockSpec((part_rows, model_width), lambda c: (0, 0)),
        ],
        out_shape=[
            jax.ShapeDtypeStruct((group_count, group_size, model_width), jnp.float32),
            jax.ShapeDtypeStruct((part_rows, model_width), jnp.float32),
        ],
    )(
        negatives.reshape(group_count, sample_count, 1),
        targets.reshape(group_count, group_size, 1),
        query_groups,
        visiting,
    )
    return query_grad.reshape(-1, model_width), visiting_grad


def split_dot(spec, wide, narrow):
    high = wide.astype(jnp.bfloat16)
    low = (wide - high.astype(jnp.float32)).astype(jnp.bfloat16)
    return jnp.einsum(spec, high, narrow, preferred_element_type=jnp.float32) + jnp.einsum(
        spec, low, narrow, preferred_element_type=jnp.float32
    )


def rep_reduce(total):
    rep_count = lax.axis_size("rep")
    pieces = total.reshape(rep_count, -1, total.shape[1]).astype(jnp.bfloat16)
    pieces = lax.all_to_all(pieces, "rep", split_axis=0, concat_axis=0, tiled=True)
    return jnp.sum(pieces, axis=0, dtype=jnp.float32)


def row_adagrad(rows, state, grad):
    new_state = state + jnp.mean(grad * grad, axis=-1)
    return (rows.astype(jnp.float32) - learn_rate * grad / jnp.sqrt(new_state)[:, None], new_state)


def shards(
    entities,
    entity_state,
    shared_table,
    shared_state,
    edge_src,
    edge_dst,
    edge_slot,
    neg_rows,
    list_owner,
    list_row,
):
    rep_count = lax.axis_size("rep")
    rep_place = lax.axis_index("rep")
    device_count = lax.axis_size("blk") * rep_count
    device_place = lax.axis_index("blk") * rep_count + rep_place
    part_rows = entities.shape[0]
    model_width = entities.shape[1]
    share_rows = part_rows // rep_count
    bucket_count = edge_src.shape[1]
    edge_count = edge_src.shape[2]
    owners = list_owner[0, :, 0]
    local_rows = list_row[0]
    table_ids = jnp.arange(shared_table.shape[0], dtype=jnp.int32)
    table_pick = ((owners * SH_DEV + local_rows)[:, None] == table_ids[None, :]).astype(jnp.bfloat16)
    shared_rows = jnp.dot(table_pick, shared_table, preferred_element_type=jnp.float32).astype(
        jnp.bfloat16
    )
    queries = []
    picks = []
    for bucket in range(bucket_count):
        query, source_pick, slot_pick = make_query(
            entities, edge_src[0, bucket], edge_slot[0, bucket], shared_rows
        )
        queries.append(query)
        picks.append((source_pick, slot_pick))
    arrivals = []
    for bucket in range(bucket_count):
        indices = jnp.concatenate([edge_dst[0, bucket], neg_rows[0, bucket].reshape(-1)])
        if bucket == 0:
            arrivals.append((queries[bucket], indices))
        else:
            coded = jnp.stack([indices // INDEX_SPLIT, indices % INDEX_SPLIT]).astype(jnp.bfloat16)
            parcel = jnp.concatenate([queries[bucket], coded.reshape(-1, model_width)], axis=0)
            parcel = passed_along(parcel, "blk", -bucket)
            coded = parcel[edge_count:].reshape(2, -1).astype(jnp.int32)
            arrivals.append((parcel[:edge_count], coded[0] * INDEX_SPLIT + coded[1]))
    group_shape = neg_rows.shape[2:]
    target_total = jnp.zeros((part_rows, model_width), jnp.float32)
    returned = [None] * bucket_count
    for bucket in [0] + list(range(bucket_count - 1, 0, -1)):
        query, indices = arrivals[bucket]
        targets = indices[:edge_count]
        negatives = indices[edge_count:].reshape(group_shape)
        query_grad, visiting_grad = target_side_kernel(entities, query, targets, negatives)
        target_total = target_total + visiting_grad
        if bucket == 0:
            returned[bucket] = query_grad
        else:
            returned[bucket] = passed_along(query_grad.astype(jnp.bfloat16), "blk", bucket)
    source_total = target_total
    slot_total = jnp.zeros((owners.shape[0], model_width), jnp.float32)
    for bucket in [0] + list(range(bucket_count - 1, 0, -1)):
        source_pick, slot_pick = picks[bucket]
        query_grad = returned[bucket]
        if query_grad.dtype == jnp.float32:
            source_total = source_total + split_dot("ed,ex->xd", query_grad, source_pick)
            slot_total = slot_total + split_dot("ed,el->ld", query_grad, slot_pick)
        else:
            source_total = source_total + jnp.einsum(
                "ed,ex->xd", query_grad, source_pick, preferred_element_type=jnp.float32
            )
            slot_total = slot_total + jnp.einsum(
                "ed,el->ld", query_grad, slot_pick, preferred_element_type=jnp.float32
            )
    own_grad = rep_reduce(source_total)
    own_entities = lax.dynamic_slice_in_dim(entities, rep_place * share_rows, share_rows, 0)
    new_entities, new_entity_state = row_adagrad(own_entities, entity_state, own_grad)
    slot_count = owners.shape[0]
    slot_order = jnp.arange(slot_count, dtype=jnp.int32)
    earlier_same = (owners[:, None] == owners[None, :]) & (
        slot_order[None, :] < slot_order[:, None]
    )
    slot_ranks = jnp.sum(earlier_same.astype(jnp.int32), axis=1)
    send_keys = owners * CAP + slot_ranks
    send_ids = jnp.arange(device_count * CAP, dtype=jnp.int32)
    send_pick = (send_keys[:, None] == send_ids[None, :]).astype(jnp.float32)
    outbound = jnp.einsum(
        "lk,ld->kd", send_pick, slot_total, precision=lax.Precision.HIGHEST
    ).reshape(device_count, CAP, model_width)
    labels = jnp.einsum(
        "lk,l->k", send_pick, local_rows.astype(jnp.float32), precision=lax.Precision.HIGHEST
    ).reshape(device_count, CAP)
    label_row = jnp.zeros((device_count, 1, model_width), jnp.float32)
    label_row = label_row.at[:, 0, :CAP].set(labels)
    packed = jnp.concatenate([outbound, label_row], axis=1).astype(jnp.bfloat16)
    arrived = lax.all_to_all(
        packed, ("blk", "rep"), split_axis=0, concat_axis=0, tiled=True
    ).astype(jnp.float32)
    inbound = arrived[:, :CAP, :]
    inbound_labels = arrived[:, CAP, :CAP]
    table_rows = jnp.arange(SH_DEV, dtype=jnp.int32)
    selector = (
        inbound_labels.reshape(-1).astype(jnp.int32)[:, None] == table_rows[None, :]
    ).astype(jnp.float32)
    shared_grad = jnp.einsum(
        "rs,rd->sd",
        selector,
        inbound.reshape(-1, model_width),
        preferred_element_type=jnp.float32,
        precision=lax.Precision.HIGHEST,
    )
    own_shared = lax.dynamic_slice_in_dim(shared_table, device_place * SH_DEV, SH_DEV, 0)
    new_shared, new_shared_state = row_adagrad(own_shared, shared_state, shared_grad)
    return (new_entities, new_entity_state, new_shared, new_shared_state)


def solution(mesh):
    return jax.shard_map(
        shards,
        mesh=mesh,
        in_specs=(
            P("blk", None),
            P(("blk", "rep")),
            P(),
            P(("blk", "rep")),
            P("blk", None, "rep"),
            P("blk", None, "rep"),
            P("blk", None, "rep"),
            P("blk", None, "rep", None),
            P("blk", "rep", None),
            P("blk", "rep"),
        ),
        out_specs=(
            P(("blk", "rep"), None),
            P(("blk", "rep")),
            P(("blk", "rep"), None),
            P(("blk", "rep")),
        ),
        check_vma=False,
    )
```

```python
import jax
import jax.numpy as jnp
from jax import lax
from jax.sharding import PartitionSpec as P

CAP = 4
SH_DEV = 64
INDEX_SPLIT = 64


learn_rate = 0.1
negative_weight = 8.0


def passed_along(value, axis, by):
    peers = lax.axis_size(axis)
    return lax.ppermute(value, axis, [(i, (i + by) % peers) for i in range(peers)])


def make_query(resident, sources, slots, shared_rows):
    part_rows = resident.shape[0]
    entity_ids = jnp.arange(part_rows, dtype=jnp.int32)
    list_ids = jnp.arange(shared_rows.shape[0], dtype=jnp.int32)
    source_pick = (sources[:, None] == entity_ids[None, :]).astype(jnp.bfloat16)
    slot_pick = (slots[:, None] == list_ids[None, :]).astype(jnp.bfloat16)
    source_rows = jnp.dot(source_pick, resident, preferred_element_type=jnp.float32)
    shared_part = jnp.dot(slot_pick, shared_rows, preferred_element_type=jnp.float32)
    query = (source_rows + shared_part).astype(jnp.bfloat16)
    return query, source_pick, slot_pick


def target_side(visiting, query, targets, negatives):
    part_rows = visiting.shape[0]
    model_width = visiting.shape[1]
    group_count = negatives.shape[0]
    sample_count = negatives.shape[1]
    entity_ids = jnp.arange(part_rows, dtype=jnp.int32)
    target_pick = (targets[:, None] == entity_ids[None, :]).astype(jnp.bfloat16)
    sample_pick = (negatives[:, :, None] == entity_ids[None, None, :]).astype(jnp.bfloat16)
    target_rows = jnp.dot(target_pick, visiting, preferred_element_type=jnp.float32).astype(
        jnp.bfloat16
    )
    positive = jnp.einsum("ed,ed->e", query, target_rows, preferred_element_type=jnp.float32)
    query_groups = query.reshape(group_count, -1, model_width)
    samples = jnp.einsum(
        "cnx,xd->cnd", sample_pick, visiting, preferred_element_type=jnp.float32
    ).astype(jnp.bfloat16)
    negative = jnp.einsum("cqd,cnd->cqn", query_groups, samples, preferred_element_type=jnp.float32)
    positive_weight = -jax.nn.sigmoid(-positive)
    sample_weight = (jax.nn.sigmoid(negative) * (negative_weight / sample_count)).astype(
        jnp.bfloat16
    )
    sampled_sum = jnp.einsum(
        "cqn,cnd->cqd", sample_weight, samples, preferred_element_type=jnp.float32
    )
    query_grad = positive_weight[:, None] * target_rows.astype(jnp.float32) + sampled_sum.reshape(
        -1, model_width
    )
    weight_map = jnp.einsum(
        "cnx,cqn->xcq", sample_pick, sample_weight, preferred_element_type=jnp.float32
    ).reshape(part_rows, -1)
    weight_map = weight_map + jnp.einsum(
        "ex,e->xe", target_pick.astype(jnp.float32), positive_weight
    )
    visiting_grad = split_dot("xe,ed->xd", weight_map, query)
    return query_grad, visiting_grad


def split_dot(spec, wide, narrow):
    high = wide.astype(jnp.bfloat16)
    low = (wide - high.astype(jnp.float32)).astype(jnp.bfloat16)
    return jnp.einsum(spec, high, narrow, preferred_element_type=jnp.float32) + jnp.einsum(
        spec, low, narrow, preferred_element_type=jnp.float32
    )


def rep_reduce(total):
    rep_count = lax.axis_size("rep")
    rep_place = lax.axis_index("rep")
    pieces = total.reshape(rep_count, -1, total.shape[1])
    own = lax.dynamic_index_in_dim(pieces, rep_place, 0, keepdims=False)
    for shift in range(1, rep_count):
        outgoing = lax.dynamic_index_in_dim(
            pieces, (rep_place + shift) % rep_count, 0, keepdims=False
        ).astype(jnp.bfloat16)
        own = own + passed_along(outgoing, "rep", shift).astype(jnp.float32)
    return own


def row_adagrad(rows, state, grad):
    new_state = state + jnp.mean(grad * grad, axis=-1)
    return (rows.astype(jnp.float32) - learn_rate * grad / jnp.sqrt(new_state)[:, None], new_state)


def shards(
    entities,
    entity_state,
    shared_table,
    shared_state,
    edge_src,
    edge_dst,
    edge_slot,
    neg_rows,
    list_owner,
    list_row,
):
    rep_count = lax.axis_size("rep")
    rep_place = lax.axis_index("rep")
    device_count = lax.axis_size("blk") * rep_count
    device_place = lax.axis_index("blk") * rep_count + rep_place
    part_rows = entities.shape[0]
    model_width = entities.shape[1]
    share_rows = part_rows // rep_count
    bucket_count = edge_src.shape[1]
    edge_count = edge_src.shape[2]
    owners = list_owner[0, :, 0]
    local_rows = list_row[0]
    table_ids = jnp.arange(shared_table.shape[0], dtype=jnp.int32)
    table_pick = ((owners * SH_DEV + local_rows)[:, None] == table_ids[None, :]).astype(jnp.bfloat16)
    shared_rows = jnp.dot(table_pick, shared_table, preferred_element_type=jnp.float32).astype(
        jnp.bfloat16
    )
    queries = []
    picks = []
    for bucket in range(bucket_count):
        query, source_pick, slot_pick = make_query(
            entities, edge_src[0, bucket], edge_slot[0, bucket], shared_rows
        )
        queries.append(query)
        picks.append((source_pick, slot_pick))
    arrivals = []
    for bucket in range(bucket_count):
        indices = jnp.concatenate([edge_dst[0, bucket], neg_rows[0, bucket].reshape(-1)])
        if bucket == 0:
            arrivals.append((queries[bucket], indices))
        else:
            coded = jnp.stack([indices // INDEX_SPLIT, indices % INDEX_SPLIT]).astype(jnp.bfloat16)
            parcel = jnp.concatenate([queries[bucket], coded.reshape(-1, model_width)], axis=0)
            parcel = passed_along(parcel, "blk", -bucket)
            coded = parcel[edge_count:].reshape(2, -1).astype(jnp.int32)
            arrivals.append((parcel[:edge_count], coded[0] * INDEX_SPLIT + coded[1]))
    group_shape = neg_rows.shape[2:]
    target_total = jnp.zeros((part_rows, model_width), jnp.float32)
    returned = [None] * bucket_count
    previous = None
    for bucket in list(range(bucket_count - 1, -1, -1)):
        if previous is not None:
            arrivals, _ = lax.optimization_barrier((arrivals, previous))
        query, indices = arrivals[bucket]
        targets = indices[:edge_count]
        negatives = indices[edge_count:].reshape(group_shape)
        query_grad, visiting_grad = target_side(entities, query, targets, negatives)
        previous = query_grad
        target_total = target_total + visiting_grad
        if bucket == 0:
            returned[bucket] = query_grad
        else:
            returned[bucket] = passed_along(query_grad.astype(jnp.bfloat16), "blk", bucket)
    source_total = target_total
    slot_total = jnp.zeros((owners.shape[0], model_width), jnp.float32)
    for bucket in [0] + list(range(bucket_count - 1, 0, -1)):
        source_pick, slot_pick = picks[bucket]
        query_grad = returned[bucket]
        if query_grad.dtype == jnp.float32:
            source_total = source_total + split_dot("ed,ex->xd", query_grad, source_pick)
            slot_total = slot_total + split_dot("ed,el->ld", query_grad, slot_pick)
        else:
            source_total = source_total + jnp.einsum(
                "ed,ex->xd", query_grad, source_pick, preferred_element_type=jnp.float32
            )
            slot_total = slot_total + jnp.einsum(
                "ed,el->ld", query_grad, slot_pick, preferred_element_type=jnp.float32
            )
    own_grad = rep_reduce(source_total)
    own_entities = lax.dynamic_slice_in_dim(entities, rep_place * share_rows, share_rows, 0)
    new_entities, new_entity_state = row_adagrad(own_entities, entity_state, own_grad)
    slot_count = owners.shape[0]
    slot_order = jnp.arange(slot_count, dtype=jnp.int32)
    earlier_same = (owners[:, None] == owners[None, :]) & (
        slot_order[None, :] < slot_order[:, None]
    )
    slot_ranks = jnp.sum(earlier_same.astype(jnp.int32), axis=1)
    send_keys = owners * CAP + slot_ranks
    send_ids = jnp.arange(device_count * CAP, dtype=jnp.int32)
    send_pick = (send_keys[:, None] == send_ids[None, :]).astype(jnp.float32)
    outbound = jnp.einsum(
        "lk,ld->kd", send_pick, slot_total, precision=lax.Precision.HIGHEST
    ).reshape(device_count, CAP, model_width)
    labels = jnp.einsum(
        "lk,l->k", send_pick, local_rows.astype(jnp.float32), precision=lax.Precision.HIGHEST
    ).reshape(device_count, CAP)
    label_row = jnp.zeros((device_count, 1, model_width), jnp.float32)
    label_row = label_row.at[:, 0, :CAP].set(labels)
    packed = jnp.concatenate([outbound, label_row], axis=1).astype(jnp.bfloat16)
    arrived = lax.all_to_all(
        packed, ("blk", "rep"), split_axis=0, concat_axis=0, tiled=True
    ).astype(jnp.float32)
    inbound = arrived[:, :CAP, :]
    inbound_labels = arrived[:, CAP, :CAP]
    table_rows = jnp.arange(SH_DEV, dtype=jnp.int32)
    selector = (
        inbound_labels.reshape(-1).astype(jnp.int32)[:, None] == table_rows[None, :]
    ).astype(jnp.float32)
    shared_grad = jnp.einsum(
        "rs,rd->sd",
        selector,
        inbound.reshape(-1, model_width),
        preferred_element_type=jnp.float32,
        precision=lax.Precision.HIGHEST,
    )
    own_shared = lax.dynamic_slice_in_dim(shared_table, device_place * SH_DEV, SH_DEV, 0)
    new_shared, new_shared_state = row_adagrad(own_shared, shared_state, shared_grad)
    return (new_entities, new_entity_state, new_shared, new_shared_state)


def solution(mesh):
    return jax.shard_map(
        shards,
        mesh=mesh,
        in_specs=(
            P("blk", None),
            P(("blk", "rep")),
            P(),
            P(("blk", "rep")),
            P("blk", None, "rep"),
            P("blk", None, "rep"),
            P("blk", None, "rep"),
            P("blk", None, "rep", None),
            P("blk", "rep", None),
            P("blk", "rep"),
        ),
        out_specs=(
            P(("blk", "rep"), None),
            P(("blk", "rep")),
            P(("blk", "rep"), None),
            P(("blk", "rep")),
        ),
        check_vma=False,
    )
```

```python
import jax
import jax.numpy as jnp
from jax import lax
from jax.sharding import PartitionSpec as P

CAP = 4
SH_DEV = 64
INDEX_SPLIT = 64


learn_rate = 0.1
negative_weight = 8.0


def passed_along(value, axis, by):
    peers = lax.axis_size(axis)
    return lax.ppermute(value, axis, [(i, (i + by) % peers) for i in range(peers)])


def make_query(resident, sources, slots, shared_rows):
    part_rows = resident.shape[0]
    entity_ids = jnp.arange(part_rows, dtype=jnp.int32)
    list_ids = jnp.arange(shared_rows.shape[0], dtype=jnp.int32)
    source_pick = (sources[:, None] == entity_ids[None, :]).astype(jnp.bfloat16)
    slot_pick = (slots[:, None] == list_ids[None, :]).astype(jnp.bfloat16)
    source_rows = jnp.dot(source_pick, resident, preferred_element_type=jnp.float32)
    shared_part = jnp.dot(slot_pick, shared_rows, preferred_element_type=jnp.float32)
    query = (source_rows + shared_part).astype(jnp.bfloat16)
    return query, source_pick, slot_pick


def target_side(visiting, query, targets, negatives):
    part_rows = visiting.shape[0]
    model_width = visiting.shape[1]
    group_count = negatives.shape[0]
    sample_count = negatives.shape[1]
    entity_ids = jnp.arange(part_rows, dtype=jnp.int32)
    target_pick = (targets[:, None] == entity_ids[None, :]).astype(jnp.bfloat16)
    sample_pick = (negatives[:, :, None] == entity_ids[None, None, :]).astype(jnp.bfloat16)
    target_rows = jnp.dot(target_pick, visiting, preferred_element_type=jnp.float32).astype(
        jnp.bfloat16
    )
    positive = jnp.einsum("ed,ed->e", query, target_rows, preferred_element_type=jnp.float32)
    query_groups = query.reshape(group_count, -1, model_width)
    samples = jnp.einsum(
        "cnx,xd->cnd", sample_pick, visiting, preferred_element_type=jnp.float32
    ).astype(jnp.bfloat16)
    negative = jnp.einsum("cqd,cnd->cqn", query_groups, samples, preferred_element_type=jnp.float32)
    positive_weight = -jax.nn.sigmoid(-positive)
    sample_weight = (jax.nn.sigmoid(negative) * (negative_weight / sample_count)).astype(
        jnp.bfloat16
    )
    sampled_sum = jnp.einsum(
        "cqn,cnd->cqd", sample_weight, samples, preferred_element_type=jnp.float32
    )
    query_grad = positive_weight[:, None] * target_rows.astype(jnp.float32) + sampled_sum.reshape(
        -1, model_width
    )
    weight_map = jnp.einsum(
        "cnx,cqn->xcq", sample_pick, sample_weight, preferred_element_type=jnp.float32
    ).reshape(part_rows, -1)
    weight_map = weight_map + jnp.einsum(
        "ex,e->xe", target_pick.astype(jnp.float32), positive_weight
    )
    visiting_grad = split_dot("xe,ed->xd", weight_map, query)
    return query_grad, visiting_grad


def split_dot(spec, wide, narrow):
    high = wide.astype(jnp.bfloat16)
    low = (wide - high.astype(jnp.float32)).astype(jnp.bfloat16)
    return jnp.einsum(spec, high, narrow, preferred_element_type=jnp.float32) + jnp.einsum(
        spec, low, narrow, preferred_element_type=jnp.float32
    )


def swapped(value, axis, mask):
    peers = lax.axis_size(axis)
    return lax.ppermute(value, axis, [(i, i ^ mask) for i in range(peers)])


def rep_reduce(total):
    rep_count = lax.axis_size("rep")
    rep_place = lax.axis_index("rep")
    width = total.shape[1]
    kept = total
    masks = []
    while rep_count > 1 << len(masks):
        masks.insert(0, 1 << len(masks))
    for mask in masks:
        halves = kept.reshape(2, -1, width)
        upper = (rep_place // mask) % 2
        mine = lax.dynamic_index_in_dim(halves, upper, 0, keepdims=False)
        other = lax.dynamic_index_in_dim(halves, 1 - upper, 0, keepdims=False)
        kept = mine + swapped(other.astype(jnp.bfloat16), "rep", mask).astype(jnp.float32)
    return kept


def row_adagrad(rows, state, grad):
    new_state = state + jnp.mean(grad * grad, axis=-1)
    return (rows.astype(jnp.float32) - learn_rate * grad / jnp.sqrt(new_state)[:, None], new_state)


def shards(
    entities,
    entity_state,
    shared_table,
    shared_state,
    edge_src,
    edge_dst,
    edge_slot,
    neg_rows,
    list_owner,
    list_row,
):
    rep_count = lax.axis_size("rep")
    rep_place = lax.axis_index("rep")
    device_count = lax.axis_size("blk") * rep_count
    device_place = lax.axis_index("blk") * rep_count + rep_place
    part_rows = entities.shape[0]
    model_width = entities.shape[1]
    share_rows = part_rows // rep_count
    bucket_count = edge_src.shape[1]
    edge_count = edge_src.shape[2]
    owners = list_owner[0, :, 0]
    local_rows = list_row[0]
    table_ids = jnp.arange(shared_table.shape[0], dtype=jnp.int32)
    table_pick = ((owners * SH_DEV + local_rows)[:, None] == table_ids[None, :]).astype(jnp.bfloat16)
    shared_rows = jnp.dot(table_pick, shared_table, preferred_element_type=jnp.float32).astype(
        jnp.bfloat16
    )
    queries = []
    picks = []
    for bucket in range(bucket_count):
        query, source_pick, slot_pick = make_query(
            entities, edge_src[0, bucket], edge_slot[0, bucket], shared_rows
        )
        queries.append(query)
        picks.append((source_pick, slot_pick))
    arrivals = []
    for bucket in range(bucket_count):
        indices = jnp.concatenate([edge_dst[0, bucket], neg_rows[0, bucket].reshape(-1)])
        if bucket == 0:
            arrivals.append((queries[bucket], indices))
        else:
            coded = jnp.stack([indices // INDEX_SPLIT, indices % INDEX_SPLIT]).astype(jnp.bfloat16)
            parcel = jnp.concatenate([queries[bucket], coded.reshape(-1, model_width)], axis=0)
            parcel = passed_along(parcel, "blk", -bucket)
            coded = parcel[edge_count:].reshape(2, -1).astype(jnp.int32)
            arrivals.append((parcel[:edge_count], coded[0] * INDEX_SPLIT + coded[1]))
    group_shape = neg_rows.shape[2:]
    target_total = jnp.zeros((part_rows, model_width), jnp.float32)
    returned = [None] * bucket_count
    for bucket in [0] + list(range(bucket_count - 1, 0, -1)):
        query, indices = arrivals[bucket]
        targets = indices[:edge_count]
        negatives = indices[edge_count:].reshape(group_shape)
        query_grad, visiting_grad = target_side(entities, query, targets, negatives)
        target_total = target_total + visiting_grad
        if bucket == 0:
            returned[bucket] = query_grad
        else:
            returned[bucket] = passed_along(query_grad.astype(jnp.bfloat16), "blk", bucket)
    source_total = target_total
    slot_total = jnp.zeros((owners.shape[0], model_width), jnp.float32)
    for bucket in [0] + list(range(bucket_count - 1, 0, -1)):
        source_pick, slot_pick = picks[bucket]
        query_grad = returned[bucket]
        if query_grad.dtype == jnp.float32:
            source_total = source_total + split_dot("ed,ex->xd", query_grad, source_pick)
            slot_total = slot_total + split_dot("ed,el->ld", query_grad, slot_pick)
        else:
            source_total = source_total + jnp.einsum(
                "ed,ex->xd", query_grad, source_pick, preferred_element_type=jnp.float32
            )
            slot_total = slot_total + jnp.einsum(
                "ed,el->ld", query_grad, slot_pick, preferred_element_type=jnp.float32
            )
    own_grad = rep_reduce(source_total)
    own_entities = lax.dynamic_slice_in_dim(entities, rep_place * share_rows, share_rows, 0)
    new_entities, new_entity_state = row_adagrad(own_entities, entity_state, own_grad)
    slot_count = owners.shape[0]
    slot_order = jnp.arange(slot_count, dtype=jnp.int32)
    earlier_same = (owners[:, None] == owners[None, :]) & (
        slot_order[None, :] < slot_order[:, None]
    )
    slot_ranks = jnp.sum(earlier_same.astype(jnp.int32), axis=1)
    send_keys = owners * CAP + slot_ranks
    send_ids = jnp.arange(device_count * CAP, dtype=jnp.int32)
    send_pick = (send_keys[:, None] == send_ids[None, :]).astype(jnp.float32)
    outbound = jnp.einsum(
        "lk,ld->kd", send_pick, slot_total, precision=lax.Precision.HIGHEST
    ).reshape(device_count, CAP, model_width)
    labels = jnp.einsum(
        "lk,l->k", send_pick, local_rows.astype(jnp.float32), precision=lax.Precision.HIGHEST
    ).reshape(device_count, CAP)
    label_row = jnp.zeros((device_count, 1, model_width), jnp.float32)
    label_row = label_row.at[:, 0, :CAP].set(labels)
    packed = jnp.concatenate([outbound, label_row], axis=1).astype(jnp.bfloat16)
    arrived = lax.all_to_all(
        packed, ("blk", "rep"), split_axis=0, concat_axis=0, tiled=True
    ).astype(jnp.float32)
    inbound = arrived[:, :CAP, :]
    inbound_labels = arrived[:, CAP, :CAP]
    table_rows = jnp.arange(SH_DEV, dtype=jnp.int32)
    selector = (
        inbound_labels.reshape(-1).astype(jnp.int32)[:, None] == table_rows[None, :]
    ).astype(jnp.float32)
    shared_grad = jnp.einsum(
        "rs,rd->sd",
        selector,
        inbound.reshape(-1, model_width),
        preferred_element_type=jnp.float32,
        precision=lax.Precision.HIGHEST,
    )
    own_shared = lax.dynamic_slice_in_dim(shared_table, device_place * SH_DEV, SH_DEV, 0)
    new_shared, new_shared_state = row_adagrad(own_shared, shared_state, shared_grad)
    return (new_entities, new_entity_state, new_shared, new_shared_state)


def solution(mesh):
    return jax.shard_map(
        shards,
        mesh=mesh,
        in_specs=(
            P("blk", None),
            P(("blk", "rep")),
            P(),
            P(("blk", "rep")),
            P("blk", None, "rep"),
            P("blk", None, "rep"),
            P("blk", None, "rep"),
            P("blk", None, "rep", None),
            P("blk", "rep", None),
            P("blk", "rep"),
        ),
        out_specs=(
            P(("blk", "rep"), None),
            P(("blk", "rep")),
            P(("blk", "rep"), None),
            P(("blk", "rep")),
        ),
        check_vma=False,
    )
```

```python
import jax
import jax.numpy as jnp
from jax import lax
from jax.sharding import PartitionSpec as P

CAP = 4
SH_DEV = 64
INDEX_SPLIT = 64


learn_rate = 0.1
negative_weight = 8.0


def passed_along(value, axis, by):
    peers = lax.axis_size(axis)
    return lax.ppermute(value, axis, [(i, (i + by) % peers) for i in range(peers)])


def make_query(resident, sources, slots, shared_rows):
    part_rows = resident.shape[0]
    entity_ids = jnp.arange(part_rows, dtype=jnp.int32)
    list_ids = jnp.arange(shared_rows.shape[0], dtype=jnp.int32)
    source_pick = (sources[:, None] == entity_ids[None, :]).astype(jnp.bfloat16)
    slot_pick = (slots[:, None] == list_ids[None, :]).astype(jnp.bfloat16)
    source_rows = jnp.dot(source_pick, resident, preferred_element_type=jnp.float32)
    shared_part = jnp.dot(slot_pick, shared_rows, preferred_element_type=jnp.float32)
    query = (source_rows + shared_part).astype(jnp.bfloat16)
    return query, source_pick, slot_pick


def target_side(visiting, query, targets, negatives):
    part_rows = visiting.shape[0]
    model_width = visiting.shape[1]
    group_count = negatives.shape[0]
    sample_count = negatives.shape[1]
    entity_ids = jnp.arange(part_rows, dtype=jnp.int32)
    target_pick = (targets[:, None] == entity_ids[None, :]).astype(jnp.bfloat16)
    sample_pick = (negatives[:, :, None] == entity_ids[None, None, :]).astype(jnp.bfloat16)
    target_rows = jnp.dot(target_pick, visiting, preferred_element_type=jnp.float32).astype(
        jnp.bfloat16
    )
    positive = jnp.einsum("ed,ed->e", query, target_rows, preferred_element_type=jnp.float32)
    query_groups = query.reshape(group_count, -1, model_width)
    samples = jnp.einsum(
        "cnx,xd->cnd", sample_pick, visiting, preferred_element_type=jnp.float32
    ).astype(jnp.bfloat16)
    negative = jnp.einsum("cqd,cnd->cqn", query_groups, samples, preferred_element_type=jnp.float32)
    positive_weight = -jax.nn.sigmoid(-positive)
    sample_weight = (jax.nn.sigmoid(negative) * (negative_weight / sample_count)).astype(
        jnp.bfloat16
    )
    sampled_sum = jnp.einsum(
        "cqn,cnd->cqd", sample_weight, samples, preferred_element_type=jnp.float32
    )
    query_grad = positive_weight[:, None] * target_rows.astype(jnp.float32) + sampled_sum.reshape(
        -1, model_width
    )
    weight_map = jnp.einsum(
        "cnx,cqn->xcq", sample_pick, sample_weight, preferred_element_type=jnp.float32
    ).reshape(part_rows, -1)
    weight_map = weight_map + jnp.einsum(
        "ex,e->xe", target_pick.astype(jnp.float32), positive_weight
    )
    visiting_grad = split_dot("xe,ed->xd", weight_map, query)
    return query_grad, visiting_grad


def split_dot(spec, wide, narrow):
    high = wide.astype(jnp.bfloat16)
    low = (wide - high.astype(jnp.float32)).astype(jnp.bfloat16)
    return jnp.einsum(spec, high, narrow, preferred_element_type=jnp.float32) + jnp.einsum(
        spec, low, narrow, preferred_element_type=jnp.float32
    )


def swapped(value, axis, mask):
    peers = lax.axis_size(axis)
    return lax.ppermute(value, axis, [(i, i ^ mask) for i in range(peers)])


def rep_reduce(total):
    rep_count = lax.axis_size("rep")
    rep_place = lax.axis_index("rep")
    width = total.shape[1]
    kept = total
    masks = []
    while rep_count > 1 << len(masks):
        masks.insert(0, 1 << len(masks))
    for mask in masks:
        halves = kept.reshape(2, -1, width)
        upper = (rep_place // mask) % 2
        mine = lax.dynamic_index_in_dim(halves, upper, 0, keepdims=False)
        other = lax.dynamic_index_in_dim(halves, 1 - upper, 0, keepdims=False)
        kept = mine + swapped(other.astype(jnp.bfloat16), "rep", mask).astype(jnp.float32)
    return kept


def row_adagrad(rows, state, grad):
    new_state = state + jnp.mean(grad * grad, axis=-1)
    return (rows.astype(jnp.float32) - learn_rate * grad / jnp.sqrt(new_state)[:, None], new_state)


def shards(
    entities,
    entity_state,
    shared_table,
    shared_state,
    edge_src,
    edge_dst,
    edge_slot,
    neg_rows,
    list_owner,
    list_row,
):
    rep_count = lax.axis_size("rep")
    rep_place = lax.axis_index("rep")
    device_count = lax.axis_size("blk") * rep_count
    device_place = lax.axis_index("blk") * rep_count + rep_place
    part_rows = entities.shape[0]
    model_width = entities.shape[1]
    share_rows = part_rows // rep_count
    bucket_count = edge_src.shape[1]
    edge_count = edge_src.shape[2]
    owners = list_owner[0, :, 0]
    local_rows = list_row[0]
    table_ids = jnp.arange(shared_table.shape[0], dtype=jnp.int32)
    table_pick = ((owners * SH_DEV + local_rows)[:, None] == table_ids[None, :]).astype(jnp.bfloat16)
    shared_rows = jnp.dot(table_pick, shared_table, preferred_element_type=jnp.float32).astype(
        jnp.bfloat16
    )
    queries = []
    picks = []
    for bucket in range(bucket_count):
        query, source_pick, slot_pick = make_query(
            entities, edge_src[0, bucket], edge_slot[0, bucket], shared_rows
        )
        queries.append(query)
        picks.append((source_pick, slot_pick))
    arrivals = []
    for bucket in range(bucket_count):
        indices = jnp.concatenate([edge_dst[0, bucket], neg_rows[0, bucket].reshape(-1)])
        if bucket == 0:
            arrivals.append((queries[bucket], indices))
        else:
            coded = jnp.stack([indices // INDEX_SPLIT, indices % INDEX_SPLIT]).astype(jnp.bfloat16)
            parcel = jnp.concatenate([queries[bucket], coded.reshape(-1, model_width)], axis=0)
            parcel = passed_along(parcel, "blk", -bucket)
            coded = parcel[edge_count:].reshape(2, -1).astype(jnp.int32)
            arrivals.append((parcel[:edge_count], coded[0] * INDEX_SPLIT + coded[1]))
    group_shape = neg_rows.shape[2:]
    target_total = jnp.zeros((part_rows, model_width), jnp.float32)
    returned = [None] * bucket_count
    for bucket in [0] + list(range(bucket_count - 1, 0, -1)):
        query, indices = arrivals[bucket]
        targets = indices[:edge_count]
        negatives = indices[edge_count:].reshape(group_shape)
        query_grad, visiting_grad = target_side(entities, query, targets, negatives)
        target_total = target_total + visiting_grad
        if bucket == 0:
            returned[bucket] = query_grad
        else:
            returned[bucket] = passed_along(query_grad.astype(jnp.bfloat16), "blk", bucket)
    source_total = target_total
    slot_total = jnp.zeros((owners.shape[0], model_width), jnp.float32)
    for bucket in [0] + list(range(bucket_count - 1, 0, -1)):
        source_pick, slot_pick = picks[bucket]
        query_grad = returned[bucket]
        if query_grad.dtype == jnp.float32:
            source_total = source_total + split_dot("ed,ex->xd", query_grad, source_pick)
            slot_total = slot_total + split_dot("ed,el->ld", query_grad, slot_pick)
        else:
            source_total = source_total + jnp.einsum(
                "ed,ex->xd", query_grad, source_pick, preferred_element_type=jnp.float32
            )
            slot_total = slot_total + jnp.einsum(
                "ed,el->ld", query_grad, slot_pick, preferred_element_type=jnp.float32
            )
    own_grad = rep_reduce(source_total)
    own_entities = lax.dynamic_slice_in_dim(entities, rep_place * share_rows, share_rows, 0)
    new_entities, new_entity_state = row_adagrad(own_entities, entity_state, own_grad)
    slot_count = owners.shape[0]
    slot_order = jnp.arange(slot_count, dtype=jnp.int32)
    earlier_same = (owners[:, None] == owners[None, :]) & (
        slot_order[None, :] < slot_order[:, None]
    )
    slot_ranks = jnp.sum(earlier_same.astype(jnp.int32), axis=1)
    send_keys = owners * CAP + slot_ranks
    send_ids = jnp.arange(device_count * CAP, dtype=jnp.int32)
    send_pick = (send_keys[:, None] == send_ids[None, :]).astype(jnp.float32)
    outbound = jnp.einsum(
        "lk,ld->kd", send_pick, slot_total, precision=lax.Precision.HIGHEST
    ).reshape(device_count, CAP, model_width)
    labels = jnp.einsum(
        "lk,l->k", send_pick, local_rows.astype(jnp.float32), precision=lax.Precision.HIGHEST
    ).reshape(device_count, CAP)
    label_row = jnp.zeros((device_count, 1, model_width), jnp.float32)
    label_row = label_row.at[:, 0, :CAP].set(labels)
    packed = jnp.concatenate([outbound, label_row], axis=1).astype(jnp.bfloat16)
    arrived = lax.all_to_all(
        packed, ("blk", "rep"), split_axis=0, concat_axis=0, tiled=True
    ).astype(jnp.float32)
    arrived, own_grad = lax.optimization_barrier((arrived, own_grad))
    inbound = arrived[:, :CAP, :]
    inbound_labels = arrived[:, CAP, :CAP]
    table_rows = jnp.arange(SH_DEV, dtype=jnp.int32)
    selector = (
        inbound_labels.reshape(-1).astype(jnp.int32)[:, None] == table_rows[None, :]
    ).astype(jnp.float32)
    shared_grad = jnp.einsum(
        "rs,rd->sd",
        selector,
        inbound.reshape(-1, model_width),
        preferred_element_type=jnp.float32,
        precision=lax.Precision.HIGHEST,
    )
    own_shared = lax.dynamic_slice_in_dim(shared_table, device_place * SH_DEV, SH_DEV, 0)
    new_shared, new_shared_state = row_adagrad(own_shared, shared_state, shared_grad)
    return (new_entities, new_entity_state, new_shared, new_shared_state)


def solution(mesh):
    return jax.shard_map(
        shards,
        mesh=mesh,
        in_specs=(
            P("blk", None),
            P(("blk", "rep")),
            P(),
            P(("blk", "rep")),
            P("blk", None, "rep"),
            P("blk", None, "rep"),
            P("blk", None, "rep"),
            P("blk", None, "rep", None),
            P("blk", "rep", None),
            P("blk", "rep"),
        ),
        out_specs=(
            P(("blk", "rep"), None),
            P(("blk", "rep")),
            P(("blk", "rep"), None),
            P(("blk", "rep")),
        ),
        check_vma=False,
    )
```

```python
import jax
import jax.numpy as jnp
from jax import lax
from jax.sharding import PartitionSpec as P

CAP = 4
SH_DEV = 64
INDEX_SPLIT = 64


learn_rate = 0.1
negative_weight = 8.0


def passed_along(value, axis, by):
    peers = lax.axis_size(axis)
    return lax.ppermute(value, axis, [(i, (i + by) % peers) for i in range(peers)])


def make_query(resident, sources, slots, shared_rows):
    part_rows = resident.shape[0]
    entity_ids = jnp.arange(part_rows, dtype=jnp.int32)
    list_ids = jnp.arange(shared_rows.shape[0], dtype=jnp.int32)
    source_pick = (sources[:, None] == entity_ids[None, :]).astype(jnp.bfloat16)
    slot_pick = (slots[:, None] == list_ids[None, :]).astype(jnp.bfloat16)
    source_rows = jnp.dot(source_pick, resident, preferred_element_type=jnp.float32)
    shared_part = jnp.dot(slot_pick, shared_rows, preferred_element_type=jnp.float32)
    query = (source_rows + shared_part).astype(jnp.bfloat16)
    return query, source_pick, slot_pick


def target_side(visiting, query, targets, negatives):
    part_rows = visiting.shape[0]
    model_width = visiting.shape[1]
    group_count = negatives.shape[0]
    sample_count = negatives.shape[1]
    entity_ids = jnp.arange(part_rows, dtype=jnp.int32)
    target_pick = (targets[:, None] == entity_ids[None, :]).astype(jnp.bfloat16)
    sample_pick = (negatives[:, :, None] == entity_ids[None, None, :]).astype(jnp.bfloat16)
    wanted = jnp.concatenate([targets, negatives.reshape(-1)])
    wanted_pick = (wanted[:, None] == entity_ids[None, :]).astype(jnp.bfloat16)
    gathered = jnp.dot(wanted_pick, visiting, preferred_element_type=jnp.float32).astype(
        jnp.bfloat16
    )
    edge_count = targets.shape[0]
    target_rows = gathered[:edge_count]
    positive = jnp.einsum("ed,ed->e", query, target_rows, preferred_element_type=jnp.float32)
    query_groups = query.reshape(group_count, -1, model_width)
    samples = gathered[edge_count:].reshape(group_count, sample_count, model_width)
    negative = jnp.einsum("cqd,cnd->cqn", query_groups, samples, preferred_element_type=jnp.float32)
    positive_weight = -jax.nn.sigmoid(-positive)
    sample_weight = (jax.nn.sigmoid(negative) * (negative_weight / sample_count)).astype(
        jnp.bfloat16
    )
    sampled_sum = jnp.einsum(
        "cqn,cnd->cqd", sample_weight, samples, preferred_element_type=jnp.float32
    )
    query_grad = positive_weight[:, None] * target_rows.astype(jnp.float32) + sampled_sum.reshape(
        -1, model_width
    )
    weight_map = jnp.einsum(
        "cnx,cqn->xcq", sample_pick, sample_weight, preferred_element_type=jnp.float32
    ).reshape(part_rows, -1)
    weight_map = weight_map + jnp.einsum(
        "ex,e->xe", target_pick.astype(jnp.float32), positive_weight
    )
    visiting_grad = split_dot("xe,ed->xd", weight_map, query)
    return query_grad, visiting_grad


def split_dot(spec, wide, narrow):
    high = wide.astype(jnp.bfloat16)
    low = (wide - high.astype(jnp.float32)).astype(jnp.bfloat16)
    return jnp.einsum(spec, high, narrow, preferred_element_type=jnp.float32) + jnp.einsum(
        spec, low, narrow, preferred_element_type=jnp.float32
    )


def rep_reduce(total):
    rep_count = lax.axis_size("rep")
    rep_place = lax.axis_index("rep")
    pieces = total.reshape(rep_count, -1, total.shape[1])
    own = lax.dynamic_index_in_dim(pieces, rep_place, 0, keepdims=False)
    for shift in range(1, rep_count):
        outgoing = lax.dynamic_index_in_dim(
            pieces, (rep_place + shift) % rep_count, 0, keepdims=False
        ).astype(jnp.bfloat16)
        own = own + passed_along(outgoing, "rep", shift).astype(jnp.float32)
    return own


def row_adagrad(rows, state, grad):
    new_state = state + jnp.mean(grad * grad, axis=-1)
    return (rows.astype(jnp.float32) - learn_rate * grad / jnp.sqrt(new_state)[:, None], new_state)


def shards(
    entities,
    entity_state,
    shared_table,
    shared_state,
    edge_src,
    edge_dst,
    edge_slot,
    neg_rows,
    list_owner,
    list_row,
):
    rep_count = lax.axis_size("rep")
    rep_place = lax.axis_index("rep")
    device_count = lax.axis_size("blk") * rep_count
    device_place = lax.axis_index("blk") * rep_count + rep_place
    part_rows = entities.shape[0]
    model_width = entities.shape[1]
    share_rows = part_rows // rep_count
    bucket_count = edge_src.shape[1]
    edge_count = edge_src.shape[2]
    owners = list_owner[0, :, 0]
    local_rows = list_row[0]
    table_ids = jnp.arange(shared_table.shape[0], dtype=jnp.int32)
    table_pick = ((owners * SH_DEV + local_rows)[:, None] == table_ids[None, :]).astype(jnp.bfloat16)
    shared_rows = jnp.dot(table_pick, shared_table, preferred_element_type=jnp.float32).astype(
        jnp.bfloat16
    )
    queries = []
    picks = []
    for bucket in range(bucket_count):
        query, source_pick, slot_pick = make_query(
            entities, edge_src[0, bucket], edge_slot[0, bucket], shared_rows
        )
        queries.append(query)
        picks.append((source_pick, slot_pick))
    arrivals = []
    for bucket in range(bucket_count):
        indices = jnp.concatenate([edge_dst[0, bucket], neg_rows[0, bucket].reshape(-1)])
        if bucket == 0:
            arrivals.append((queries[bucket], indices))
        else:
            coded = jnp.stack([indices // INDEX_SPLIT, indices % INDEX_SPLIT]).astype(jnp.bfloat16)
            parcel = jnp.concatenate([queries[bucket], coded.reshape(-1, model_width)], axis=0)
            parcel = passed_along(parcel, "blk", -bucket)
            coded = parcel[edge_count:].reshape(2, -1).astype(jnp.int32)
            arrivals.append((parcel[:edge_count], coded[0] * INDEX_SPLIT + coded[1]))
    group_shape = neg_rows.shape[2:]
    target_total = jnp.zeros((part_rows, model_width), jnp.float32)
    returned = [None] * bucket_count
    for bucket in [0] + list(range(bucket_count - 1, 0, -1)):
        query, indices = arrivals[bucket]
        targets = indices[:edge_count]
        negatives = indices[edge_count:].reshape(group_shape)
        query_grad, visiting_grad = target_side(entities, query, targets, negatives)
        target_total = target_total + visiting_grad
        if bucket == 0:
            returned[bucket] = query_grad
        else:
            returned[bucket] = passed_along(query_grad.astype(jnp.bfloat16), "blk", bucket)
    source_total = target_total
    slot_total = jnp.zeros((owners.shape[0], model_width), jnp.float32)
    for bucket in [0] + list(range(bucket_count - 1, 0, -1)):
        source_pick, slot_pick = picks[bucket]
        query_grad = returned[bucket]
        if query_grad.dtype == jnp.float32:
            source_total = source_total + split_dot("ed,ex->xd", query_grad, source_pick)
            slot_total = slot_total + split_dot("ed,el->ld", query_grad, slot_pick)
        else:
            source_total = source_total + jnp.einsum(
                "ed,ex->xd", query_grad, source_pick, preferred_element_type=jnp.float32
            )
            slot_total = slot_total + jnp.einsum(
                "ed,el->ld", query_grad, slot_pick, preferred_element_type=jnp.float32
            )
    own_grad = rep_reduce(source_total)
    own_entities = lax.dynamic_slice_in_dim(entities, rep_place * share_rows, share_rows, 0)
    new_entities, new_entity_state = row_adagrad(own_entities, entity_state, own_grad)
    slot_count = owners.shape[0]
    slot_order = jnp.arange(slot_count, dtype=jnp.int32)
    earlier_same = (owners[:, None] == owners[None, :]) & (
        slot_order[None, :] < slot_order[:, None]
    )
    slot_ranks = jnp.sum(earlier_same.astype(jnp.int32), axis=1)
    send_keys = owners * CAP + slot_ranks
    send_ids = jnp.arange(device_count * CAP, dtype=jnp.int32)
    send_pick = (send_keys[:, None] == send_ids[None, :]).astype(jnp.float32)
    outbound = jnp.einsum(
        "lk,ld->kd", send_pick, slot_total, precision=lax.Precision.HIGHEST
    ).reshape(device_count, CAP, model_width)
    labels = jnp.einsum(
        "lk,l->k", send_pick, local_rows.astype(jnp.float32), precision=lax.Precision.HIGHEST
    ).reshape(device_count, CAP)
    label_row = jnp.zeros((device_count, 1, model_width), jnp.float32)
    label_row = label_row.at[:, 0, :CAP].set(labels)
    packed = jnp.concatenate([outbound, label_row], axis=1).astype(jnp.bfloat16)
    arrived = lax.all_to_all(
        packed, ("blk", "rep"), split_axis=0, concat_axis=0, tiled=True
    ).astype(jnp.float32)
    inbound = arrived[:, :CAP, :]
    inbound_labels = arrived[:, CAP, :CAP]
    table_rows = jnp.arange(SH_DEV, dtype=jnp.int32)
    selector = (
        inbound_labels.reshape(-1).astype(jnp.int32)[:, None] == table_rows[None, :]
    ).astype(jnp.float32)
    shared_grad = jnp.einsum(
        "rs,rd->sd",
        selector,
        inbound.reshape(-1, model_width),
        preferred_element_type=jnp.float32,
        precision=lax.Precision.HIGHEST,
    )
    own_shared = lax.dynamic_slice_in_dim(shared_table, device_place * SH_DEV, SH_DEV, 0)
    new_shared, new_shared_state = row_adagrad(own_shared, shared_state, shared_grad)
    return (new_entities, new_entity_state, new_shared, new_shared_state)


def solution(mesh):
    return jax.shard_map(
        shards,
        mesh=mesh,
        in_specs=(
            P("blk", None),
            P(("blk", "rep")),
            P(),
            P(("blk", "rep")),
            P("blk", None, "rep"),
            P("blk", None, "rep"),
            P("blk", None, "rep"),
            P("blk", None, "rep", None),
            P("blk", "rep", None),
            P("blk", "rep"),
        ),
        out_specs=(
            P(("blk", "rep"), None),
            P(("blk", "rep")),
            P(("blk", "rep"), None),
            P(("blk", "rep")),
        ),
        check_vma=False,
    )
```

```python
import jax
import jax.numpy as jnp
from jax import lax
from jax.sharding import PartitionSpec as P

CAP = 4
SH_DEV = 64
INDEX_SPLIT = 64


learn_rate = 0.1
negative_weight = 8.0


def passed_along(value, axis, by):
    peers = lax.axis_size(axis)
    return lax.ppermute(value, axis, [(i, (i + by) % peers) for i in range(peers)])


def make_query(resident, sources, slots, shared_rows):
    part_rows = resident.shape[0]
    entity_ids = jnp.arange(part_rows, dtype=jnp.int32)
    list_ids = jnp.arange(shared_rows.shape[0], dtype=jnp.int32)
    source_pick = (sources[:, None] == entity_ids[None, :]).astype(jnp.bfloat16)
    slot_pick = (slots[:, None] == list_ids[None, :]).astype(jnp.bfloat16)
    source_rows = jnp.dot(source_pick, resident, preferred_element_type=jnp.float32)
    shared_part = jnp.dot(slot_pick, shared_rows, preferred_element_type=jnp.float32)
    query = (source_rows + shared_part).astype(jnp.bfloat16)
    return query, source_pick, slot_pick


def target_side(visiting, query, targets, negatives):
    part_rows = visiting.shape[0]
    model_width = visiting.shape[1]
    group_count = negatives.shape[0]
    sample_count = negatives.shape[1]
    entity_ids = jnp.arange(part_rows, dtype=jnp.int32)
    target_pick = (targets[:, None] == entity_ids[None, :]).astype(jnp.bfloat16)
    sample_pick = (negatives[:, :, None] == entity_ids[None, None, :]).astype(jnp.bfloat16)
    target_rows = jnp.dot(target_pick, visiting, preferred_element_type=jnp.float32).astype(
        jnp.bfloat16
    )
    positive = jnp.einsum("ed,ed->e", query, target_rows, preferred_element_type=jnp.float32)
    query_groups = query.reshape(group_count, -1, model_width)
    samples = jnp.einsum(
        "cnx,xd->cnd", sample_pick, visiting, preferred_element_type=jnp.float32
    ).astype(jnp.bfloat16)
    negative = jnp.einsum("cqd,cnd->cqn", query_groups, samples, preferred_element_type=jnp.float32)
    positive_weight = -jax.nn.sigmoid(-positive)
    sample_weight = (jax.nn.sigmoid(negative) * (negative_weight / sample_count)).astype(
        jnp.bfloat16
    )
    sampled_sum = jnp.einsum(
        "cqn,cnd->cqd", sample_weight, samples, preferred_element_type=jnp.float32
    )
    query_grad = positive_weight[:, None] * target_rows.astype(jnp.float32) + sampled_sum.reshape(
        -1, model_width
    )
    weight_map = jnp.einsum(
        "cnx,cqn->xcq", sample_pick, sample_weight, preferred_element_type=jnp.float32
    ).reshape(part_rows, -1)
    weight_map = weight_map + jnp.einsum(
        "ex,e->xe", target_pick.astype(jnp.float32), positive_weight
    )
    visiting_grad = split_dot("xe,ed->xd", weight_map, query)
    return query_grad, visiting_grad


def split_dot(spec, wide, narrow):
    high = wide.astype(jnp.bfloat16)
    low = (wide - high.astype(jnp.float32)).astype(jnp.bfloat16)
    return jnp.einsum(spec, high, narrow, preferred_element_type=jnp.float32) + jnp.einsum(
        spec, low, narrow, preferred_element_type=jnp.float32
    )


def rep_reduce(total):
    rep_count = lax.axis_size("rep")
    rep_place = lax.axis_index("rep")
    pieces = total.reshape(rep_count, -1, total.shape[1])
    own = lax.dynamic_index_in_dim(pieces, rep_place, 0, keepdims=False)
    for shift in range(1, rep_count):
        outgoing = lax.dynamic_index_in_dim(
            pieces, (rep_place + shift) % rep_count, 0, keepdims=False
        ).astype(jnp.bfloat16)
        own = own + passed_along(outgoing, "rep", shift).astype(jnp.float32)
    return own


def row_adagrad(rows, state, grad):
    new_state = state + jnp.mean(grad * grad, axis=-1)
    return (rows.astype(jnp.float32) - learn_rate * grad / jnp.sqrt(new_state)[:, None], new_state)


def shards(
    entities,
    entity_state,
    shared_table,
    shared_state,
    edge_src,
    edge_dst,
    edge_slot,
    neg_rows,
    list_owner,
    list_row,
):
    rep_count = lax.axis_size("rep")
    rep_place = lax.axis_index("rep")
    device_count = lax.axis_size("blk") * rep_count
    device_place = lax.axis_index("blk") * rep_count + rep_place
    part_rows = entities.shape[0]
    model_width = entities.shape[1]
    share_rows = part_rows // rep_count
    bucket_count = edge_src.shape[1]
    edge_count = edge_src.shape[2]
    owners = list_owner[0, :, 0]
    local_rows = list_row[0]
    table_ids = jnp.arange(shared_table.shape[0], dtype=jnp.int32)
    table_pick = ((owners * SH_DEV + local_rows)[:, None] == table_ids[None, :]).astype(jnp.bfloat16)
    shared_rows = jnp.dot(table_pick, shared_table, preferred_element_type=jnp.float32).astype(
        jnp.bfloat16
    )
    queries = []
    picks = []
    for bucket in range(bucket_count):
        query, source_pick, slot_pick = make_query(
            entities, edge_src[0, bucket], edge_slot[0, bucket], shared_rows
        )
        queries.append(query)
        picks.append((source_pick, slot_pick))
    arrivals = []
    for bucket in range(bucket_count):
        indices = jnp.concatenate([edge_dst[0, bucket], neg_rows[0, bucket].reshape(-1)])
        if bucket == 0:
            arrivals.append((queries[bucket], indices))
        else:
            coded = jnp.stack([indices // INDEX_SPLIT, indices % INDEX_SPLIT]).astype(jnp.bfloat16)
            parcel = jnp.concatenate([queries[bucket], coded.reshape(-1, model_width)], axis=0)
            parcel = passed_along(parcel, "blk", -bucket)
            coded = parcel[edge_count:].reshape(2, -1).astype(jnp.int32)
            arrivals.append((parcel[:edge_count], coded[0] * INDEX_SPLIT + coded[1]))
    group_shape = neg_rows.shape[2:]
    target_total = jnp.zeros((part_rows, model_width), jnp.float32)
    returned = [None] * bucket_count

    def target_of(query, indices):
        targets = indices[:edge_count]
        negatives = indices[edge_count:].reshape(group_shape)
        return target_side(entities, query, targets, negatives)

    query_grad, target_total = target_of(*arrivals[0])
    returned[0] = query_grad

    def visit(total, parcel):
        query_grad, visiting_grad = target_of(*parcel)
        return total + visiting_grad, query_grad.astype(jnp.bfloat16)

    later = [arrivals[bucket] for bucket in range(1, bucket_count)]
    target_total, query_grads = lax.scan(
        visit,
        target_total,
        (jnp.stack([query for query, _ in later]), jnp.stack([indices for _, indices in later])),
    )
    for bucket in range(1, bucket_count):
        returned[bucket] = passed_along(query_grads[bucket - 1], "blk", bucket)
    source_total = target_total
    slot_total = jnp.zeros((owners.shape[0], model_width), jnp.float32)
    for bucket in [0] + list(range(bucket_count - 1, 0, -1)):
        source_pick, slot_pick = picks[bucket]
        query_grad = returned[bucket]
        if query_grad.dtype == jnp.float32:
            source_total = source_total + split_dot("ed,ex->xd", query_grad, source_pick)
            slot_total = slot_total + split_dot("ed,el->ld", query_grad, slot_pick)
        else:
            source_total = source_total + jnp.einsum(
                "ed,ex->xd", query_grad, source_pick, preferred_element_type=jnp.float32
            )
            slot_total = slot_total + jnp.einsum(
                "ed,el->ld", query_grad, slot_pick, preferred_element_type=jnp.float32
            )
    own_grad = rep_reduce(source_total)
    own_entities = lax.dynamic_slice_in_dim(entities, rep_place * share_rows, share_rows, 0)
    new_entities, new_entity_state = row_adagrad(own_entities, entity_state, own_grad)
    slot_count = owners.shape[0]
    slot_order = jnp.arange(slot_count, dtype=jnp.int32)
    earlier_same = (owners[:, None] == owners[None, :]) & (
        slot_order[None, :] < slot_order[:, None]
    )
    slot_ranks = jnp.sum(earlier_same.astype(jnp.int32), axis=1)
    send_keys = owners * CAP + slot_ranks
    send_ids = jnp.arange(device_count * CAP, dtype=jnp.int32)
    send_pick = (send_keys[:, None] == send_ids[None, :]).astype(jnp.float32)
    outbound = jnp.einsum(
        "lk,ld->kd", send_pick, slot_total, precision=lax.Precision.HIGHEST
    ).reshape(device_count, CAP, model_width)
    labels = jnp.einsum(
        "lk,l->k", send_pick, local_rows.astype(jnp.float32), precision=lax.Precision.HIGHEST
    ).reshape(device_count, CAP)
    label_row = jnp.zeros((device_count, 1, model_width), jnp.float32)
    label_row = label_row.at[:, 0, :CAP].set(labels)
    packed = jnp.concatenate([outbound, label_row], axis=1).astype(jnp.bfloat16)
    arrived = lax.all_to_all(
        packed, ("blk", "rep"), split_axis=0, concat_axis=0, tiled=True
    ).astype(jnp.float32)
    inbound = arrived[:, :CAP, :]
    inbound_labels = arrived[:, CAP, :CAP]
    table_rows = jnp.arange(SH_DEV, dtype=jnp.int32)
    selector = (
        inbound_labels.reshape(-1).astype(jnp.int32)[:, None] == table_rows[None, :]
    ).astype(jnp.float32)
    shared_grad = jnp.einsum(
        "rs,rd->sd",
        selector,
        inbound.reshape(-1, model_width),
        preferred_element_type=jnp.float32,
        precision=lax.Precision.HIGHEST,
    )
    own_shared = lax.dynamic_slice_in_dim(shared_table, device_place * SH_DEV, SH_DEV, 0)
    new_shared, new_shared_state = row_adagrad(own_shared, shared_state, shared_grad)
    return (new_entities, new_entity_state, new_shared, new_shared_state)


def solution(mesh):
    return jax.shard_map(
        shards,
        mesh=mesh,
        in_specs=(
            P("blk", None),
            P(("blk", "rep")),
            P(),
            P(("blk", "rep")),
            P("blk", None, "rep"),
            P("blk", None, "rep"),
            P("blk", None, "rep"),
            P("blk", None, "rep", None),
            P("blk", "rep", None),
            P("blk", "rep"),
        ),
        out_specs=(
            P(("blk", "rep"), None),
            P(("blk", "rep")),
            P(("blk", "rep"), None),
            P(("blk", "rep")),
        ),
        check_vma=False,
    )
```

```python
import jax
import jax.numpy as jnp
from jax import lax
from jax.sharding import PartitionSpec as P

CAP = 4
SH_DEV = 64
INDEX_SPLIT = 64


learn_rate = 0.1
negative_weight = 8.0


def passed_along(value, axis, by):
    peers = lax.axis_size(axis)
    return lax.ppermute(value, axis, [(i, (i + by) % peers) for i in range(peers)])


def make_query(resident, sources, slots, shared_rows):
    part_rows = resident.shape[0]
    entity_ids = jnp.arange(part_rows, dtype=jnp.int32)
    list_ids = jnp.arange(shared_rows.shape[0], dtype=jnp.int32)
    source_pick = (sources[:, None] == entity_ids[None, :]).astype(jnp.bfloat16)
    slot_pick = (slots[:, None] == list_ids[None, :]).astype(jnp.bfloat16)
    source_rows = jnp.dot(source_pick, resident, preferred_element_type=jnp.float32)
    shared_part = jnp.dot(slot_pick, shared_rows, preferred_element_type=jnp.float32)
    query = (source_rows + shared_part).astype(jnp.bfloat16)
    return query, source_pick, slot_pick


def target_side(visiting, query, targets, negatives):
    part_rows = visiting.shape[0]
    model_width = visiting.shape[1]
    group_count = negatives.shape[0]
    sample_count = negatives.shape[1]
    entity_ids = jnp.arange(part_rows, dtype=jnp.int32)
    target_pick = (targets[:, None] == entity_ids[None, :]).astype(jnp.bfloat16)
    sample_pick = (negatives[:, :, None] == entity_ids[None, None, :]).astype(jnp.bfloat16)
    target_rows = jnp.dot(target_pick, visiting, preferred_element_type=jnp.float32).astype(
        jnp.bfloat16
    )
    positive = jnp.einsum("ed,ed->e", query, target_rows, preferred_element_type=jnp.float32)
    query_groups = query.reshape(group_count, -1, model_width)
    samples = jnp.einsum(
        "cnx,xd->cnd", sample_pick, visiting, preferred_element_type=jnp.float32
    ).astype(jnp.bfloat16)
    negative = jnp.einsum("cqd,cnd->cqn", query_groups, samples, preferred_element_type=jnp.float32)
    positive_weight = -jax.nn.sigmoid(-positive)
    sample_weight = (jax.nn.sigmoid(negative) * (negative_weight / sample_count)).astype(
        jnp.bfloat16
    )
    sampled_sum = jnp.einsum(
        "cqn,cnd->cqd", sample_weight, samples, preferred_element_type=jnp.float32
    )
    query_grad = positive_weight[:, None] * target_rows.astype(jnp.float32) + sampled_sum.reshape(
        -1, model_width
    )
    weight_map = jnp.einsum(
        "cnx,cqn->xcq", sample_pick, sample_weight, preferred_element_type=jnp.float32
    ).reshape(part_rows, -1)
    weight_map = weight_map + jnp.einsum(
        "ex,e->xe", target_pick.astype(jnp.float32), positive_weight
    )
    visiting_grad = jnp.dot(
        weight_map.astype(jnp.bfloat16), query, preferred_element_type=jnp.float32
    )
    return query_grad, visiting_grad


def split_dot(spec, wide, narrow):
    high = wide.astype(jnp.bfloat16)
    low = (wide - high.astype(jnp.float32)).astype(jnp.bfloat16)
    return jnp.einsum(spec, high, narrow, preferred_element_type=jnp.float32) + jnp.einsum(
        spec, low, narrow, preferred_element_type=jnp.float32
    )


def rep_reduce(total):
    rep_count = lax.axis_size("rep")
    rep_place = lax.axis_index("rep")
    pieces = total.reshape(rep_count, -1, total.shape[1])
    own = lax.dynamic_index_in_dim(pieces, rep_place, 0, keepdims=False)
    for shift in range(1, rep_count):
        outgoing = lax.dynamic_index_in_dim(
            pieces, (rep_place + shift) % rep_count, 0, keepdims=False
        ).astype(jnp.bfloat16)
        own = own + passed_along(outgoing, "rep", shift).astype(jnp.float32)
    return own


def row_adagrad(rows, state, grad):
    new_state = state + jnp.mean(grad * grad, axis=-1)
    return (rows.astype(jnp.float32) - learn_rate * grad / jnp.sqrt(new_state)[:, None], new_state)


def shards(
    entities,
    entity_state,
    shared_table,
    shared_state,
    edge_src,
    edge_dst,
    edge_slot,
    neg_rows,
    list_owner,
    list_row,
):
    rep_count = lax.axis_size("rep")
    rep_place = lax.axis_index("rep")
    device_count = lax.axis_size("blk") * rep_count
    device_place = lax.axis_index("blk") * rep_count + rep_place
    part_rows = entities.shape[0]
    model_width = entities.shape[1]
    share_rows = part_rows // rep_count
    bucket_count = edge_src.shape[1]
    edge_count = edge_src.shape[2]
    owners = list_owner[0, :, 0]
    local_rows = list_row[0]
    table_ids = jnp.arange(shared_table.shape[0], dtype=jnp.int32)
    table_pick = ((owners * SH_DEV + local_rows)[:, None] == table_ids[None, :]).astype(jnp.bfloat16)
    shared_rows = jnp.dot(table_pick, shared_table, preferred_element_type=jnp.float32).astype(
        jnp.bfloat16
    )
    queries = []
    picks = []
    for bucket in range(bucket_count):
        query, source_pick, slot_pick = make_query(
            entities, edge_src[0, bucket], edge_slot[0, bucket], shared_rows
        )
        queries.append(query)
        picks.append((source_pick, slot_pick))
    arrivals = []
    for bucket in range(bucket_count):
        indices = jnp.concatenate([edge_dst[0, bucket], neg_rows[0, bucket].reshape(-1)])
        if bucket == 0:
            arrivals.append((queries[bucket], indices))
        else:
            coded = jnp.stack([indices // INDEX_SPLIT, indices % INDEX_SPLIT]).astype(jnp.bfloat16)
            parcel = jnp.concatenate([queries[bucket], coded.reshape(-1, model_width)], axis=0)
            parcel = passed_along(parcel, "blk", -bucket)
            coded = parcel[edge_count:].reshape(2, -1).astype(jnp.int32)
            arrivals.append((parcel[:edge_count], coded[0] * INDEX_SPLIT + coded[1]))
    group_shape = neg_rows.shape[2:]
    target_total = jnp.zeros((part_rows, model_width), jnp.float32)
    returned = [None] * bucket_count
    for bucket in [0] + list(range(bucket_count - 1, 0, -1)):
        query, indices = arrivals[bucket]
        targets = indices[:edge_count]
        negatives = indices[edge_count:].reshape(group_shape)
        query_grad, visiting_grad = target_side(entities, query, targets, negatives)
        target_total = target_total + visiting_grad
        if bucket == 0:
            returned[bucket] = query_grad
        else:
            returned[bucket] = passed_along(query_grad.astype(jnp.bfloat16), "blk", bucket)
    source_total = target_total
    slot_total = jnp.zeros((owners.shape[0], model_width), jnp.float32)
    for bucket in [0] + list(range(bucket_count - 1, 0, -1)):
        source_pick, slot_pick = picks[bucket]
        query_grad = returned[bucket]
        if query_grad.dtype == jnp.float32:
            source_total = source_total + split_dot("ed,ex->xd", query_grad, source_pick)
            slot_total = slot_total + split_dot("ed,el->ld", query_grad, slot_pick)
        else:
            source_total = source_total + jnp.einsum(
                "ed,ex->xd", query_grad, source_pick, preferred_element_type=jnp.float32
            )
            slot_total = slot_total + jnp.einsum(
                "ed,el->ld", query_grad, slot_pick, preferred_element_type=jnp.float32
            )
    own_grad = rep_reduce(source_total)
    own_entities = lax.dynamic_slice_in_dim(entities, rep_place * share_rows, share_rows, 0)
    new_entities, new_entity_state = row_adagrad(own_entities, entity_state, own_grad)
    slot_count = owners.shape[0]
    slot_order = jnp.arange(slot_count, dtype=jnp.int32)
    earlier_same = (owners[:, None] == owners[None, :]) & (
        slot_order[None, :] < slot_order[:, None]
    )
    slot_ranks = jnp.sum(earlier_same.astype(jnp.int32), axis=1)
    send_keys = owners * CAP + slot_ranks
    send_ids = jnp.arange(device_count * CAP, dtype=jnp.int32)
    send_pick = (send_keys[:, None] == send_ids[None, :]).astype(jnp.float32)
    outbound = jnp.einsum(
        "lk,ld->kd", send_pick, slot_total, precision=lax.Precision.HIGHEST
    ).reshape(device_count, CAP, model_width)
    labels = jnp.einsum(
        "lk,l->k", send_pick, local_rows.astype(jnp.float32), precision=lax.Precision.HIGHEST
    ).reshape(device_count, CAP)
    label_row = jnp.zeros((device_count, 1, model_width), jnp.float32)
    label_row = label_row.at[:, 0, :CAP].set(labels)
    packed = jnp.concatenate([outbound, label_row], axis=1).astype(jnp.bfloat16)
    arrived = lax.all_to_all(
        packed, ("blk", "rep"), split_axis=0, concat_axis=0, tiled=True
    ).astype(jnp.float32)
    inbound = arrived[:, :CAP, :]
    inbound_labels = arrived[:, CAP, :CAP]
    table_rows = jnp.arange(SH_DEV, dtype=jnp.int32)
    selector = (
        inbound_labels.reshape(-1).astype(jnp.int32)[:, None] == table_rows[None, :]
    ).astype(jnp.float32)
    shared_grad = jnp.einsum(
        "rs,rd->sd",
        selector,
        inbound.reshape(-1, model_width),
        preferred_element_type=jnp.float32,
        precision=lax.Precision.HIGHEST,
    )
    own_shared = lax.dynamic_slice_in_dim(shared_table, device_place * SH_DEV, SH_DEV, 0)
    new_shared, new_shared_state = row_adagrad(own_shared, shared_state, shared_grad)
    return (new_entities, new_entity_state, new_shared, new_shared_state)


def solution(mesh):
    return jax.shard_map(
        shards,
        mesh=mesh,
        in_specs=(
            P("blk", None),
            P(("blk", "rep")),
            P(),
            P(("blk", "rep")),
            P("blk", None, "rep"),
            P("blk", None, "rep"),
            P("blk", None, "rep"),
            P("blk", None, "rep", None),
            P("blk", "rep", None),
            P("blk", "rep"),
        ),
        out_specs=(
            P(("blk", "rep"), None),
            P(("blk", "rep")),
            P(("blk", "rep"), None),
            P(("blk", "rep")),
        ),
        check_vma=False,
    )
```

```python
import jax
import jax.numpy as jnp
from jax import lax
from jax.sharding import PartitionSpec as P

CAP = 4
SH_DEV = 64
INDEX_SPLIT = 64


learn_rate = 0.1
negative_weight = 8.0


def passed_along(value, axis, by):
    peers = lax.axis_size(axis)
    return lax.ppermute(value, axis, [(i, (i + by) % peers) for i in range(peers)])


def make_query(resident, sources, slots, shared_rows):
    part_rows = resident.shape[0]
    entity_ids = jnp.arange(part_rows, dtype=jnp.int32)
    list_ids = jnp.arange(shared_rows.shape[0], dtype=jnp.int32)
    source_pick = (sources[:, None] == entity_ids[None, :]).astype(jnp.bfloat16)
    slot_pick = (slots[:, None] == list_ids[None, :]).astype(jnp.bfloat16)
    source_rows = jnp.dot(source_pick, resident, preferred_element_type=jnp.float32)
    shared_part = jnp.dot(slot_pick, shared_rows, preferred_element_type=jnp.float32)
    query = (source_rows + shared_part).astype(jnp.bfloat16)
    return query, source_pick, slot_pick


def target_side(visiting, query, targets, negatives):
    part_rows = visiting.shape[0]
    model_width = visiting.shape[1]
    group_count = negatives.shape[0]
    sample_count = negatives.shape[1]
    entity_ids = jnp.arange(part_rows, dtype=jnp.int32)
    target_pick = (targets[:, None] == entity_ids[None, :]).astype(jnp.bfloat16)
    sample_pick = (negatives[:, :, None] == entity_ids[None, None, :]).astype(jnp.bfloat16)
    target_rows = jnp.dot(target_pick, visiting, preferred_element_type=jnp.float32).astype(
        jnp.bfloat16
    )
    positive = jnp.einsum("ed,ed->e", query, target_rows, preferred_element_type=jnp.float32)
    query_groups = query.reshape(group_count, -1, model_width)
    samples = jnp.einsum(
        "cnx,xd->cnd", sample_pick, visiting, preferred_element_type=jnp.float32
    ).astype(jnp.bfloat16)
    negative = jnp.einsum("cqd,cnd->cqn", query_groups, samples, preferred_element_type=jnp.float32)
    positive_weight = -jax.nn.sigmoid(-positive)
    sample_weight = (jax.nn.sigmoid(negative) * (negative_weight / sample_count)).astype(
        jnp.bfloat16
    )
    sampled_sum = jnp.einsum(
        "cqn,cnd->cqd", sample_weight, samples, preferred_element_type=jnp.float32
    )
    query_grad = positive_weight[:, None] * target_rows.astype(jnp.float32) + sampled_sum.reshape(
        -1, model_width
    )
    weight_map = jnp.einsum(
        "cnx,cqn->xcq", sample_pick, sample_weight, preferred_element_type=jnp.float32
    ).reshape(part_rows, -1)
    weight_map = weight_map + jnp.einsum(
        "ex,e->xe", target_pick.astype(jnp.float32), positive_weight
    )
    visiting_grad = jnp.dot(
        weight_map.astype(jnp.bfloat16), query, preferred_element_type=jnp.float32
    )
    return query_grad, visiting_grad


def rep_reduce(total):
    rep_count = lax.axis_size("rep")
    rep_place = lax.axis_index("rep")
    pieces = total.reshape(rep_count, -1, total.shape[1])
    own = lax.dynamic_index_in_dim(pieces, rep_place, 0, keepdims=False)
    for shift in range(1, rep_count):
        outgoing = lax.dynamic_index_in_dim(
            pieces, (rep_place + shift) % rep_count, 0, keepdims=False
        ).astype(jnp.bfloat16)
        own = own + passed_along(outgoing, "rep", shift).astype(jnp.float32)
    return own


def row_adagrad(rows, state, grad):
    new_state = state + jnp.mean(grad * grad, axis=-1)
    return (rows.astype(jnp.float32) - learn_rate * grad / jnp.sqrt(new_state)[:, None], new_state)


def shards(
    entities,
    entity_state,
    shared_table,
    shared_state,
    edge_src,
    edge_dst,
    edge_slot,
    neg_rows,
    list_owner,
    list_row,
):
    rep_count = lax.axis_size("rep")
    rep_place = lax.axis_index("rep")
    device_count = lax.axis_size("blk") * rep_count
    device_place = lax.axis_index("blk") * rep_count + rep_place
    part_rows = entities.shape[0]
    model_width = entities.shape[1]
    share_rows = part_rows // rep_count
    bucket_count = edge_src.shape[1]
    edge_count = edge_src.shape[2]
    owners = list_owner[0, :, 0]
    local_rows = list_row[0]
    table_ids = jnp.arange(shared_table.shape[0], dtype=jnp.int32)
    table_pick = ((owners * SH_DEV + local_rows)[:, None] == table_ids[None, :]).astype(jnp.bfloat16)
    shared_rows = jnp.dot(table_pick, shared_table, preferred_element_type=jnp.float32).astype(
        jnp.bfloat16
    )
    queries = []
    picks = []
    for bucket in range(bucket_count):
        query, source_pick, slot_pick = make_query(
            entities, edge_src[0, bucket], edge_slot[0, bucket], shared_rows
        )
        queries.append(query)
        picks.append((source_pick, slot_pick))
    arrivals = []
    for bucket in range(bucket_count):
        indices = jnp.concatenate([edge_dst[0, bucket], neg_rows[0, bucket].reshape(-1)])
        if bucket == 0:
            arrivals.append((queries[bucket], indices))
        else:
            coded = jnp.stack([indices // INDEX_SPLIT, indices % INDEX_SPLIT]).astype(jnp.bfloat16)
            parcel = jnp.concatenate([queries[bucket], coded.reshape(-1, model_width)], axis=0)
            parcel = passed_along(parcel, "blk", -bucket)
            coded = parcel[edge_count:].reshape(2, -1).astype(jnp.int32)
            arrivals.append((parcel[:edge_count], coded[0] * INDEX_SPLIT + coded[1]))
    group_shape = neg_rows.shape[2:]
    target_total = jnp.zeros((part_rows, model_width), jnp.float32)
    returned = [None] * bucket_count
    for bucket in [0] + list(range(bucket_count - 1, 0, -1)):
        query, indices = arrivals[bucket]
        targets = indices[:edge_count]
        negatives = indices[edge_count:].reshape(group_shape)
        query_grad, visiting_grad = target_side(entities, query, targets, negatives)
        target_total = target_total + visiting_grad
        if bucket == 0:
            returned[bucket] = query_grad.astype(jnp.bfloat16)
        else:
            returned[bucket] = passed_along(query_grad.astype(jnp.bfloat16), "blk", bucket)
    source_total = target_total
    slot_total = jnp.zeros((owners.shape[0], model_width), jnp.float32)
    for bucket in [0] + list(range(bucket_count - 1, 0, -1)):
        source_pick, slot_pick = picks[bucket]
        query_grad = returned[bucket]
        source_total = source_total + jnp.einsum(
            "ed,ex->xd", query_grad, source_pick, preferred_element_type=jnp.float32
        )
        slot_total = slot_total + jnp.einsum(
            "ed,el->ld", query_grad, slot_pick, preferred_element_type=jnp.float32
        )
    own_grad = rep_reduce(source_total)
    own_entities = lax.dynamic_slice_in_dim(entities, rep_place * share_rows, share_rows, 0)
    new_entities, new_entity_state = row_adagrad(own_entities, entity_state, own_grad)
    slot_count = owners.shape[0]
    slot_order = jnp.arange(slot_count, dtype=jnp.int32)
    earlier_same = (owners[:, None] == owners[None, :]) & (
        slot_order[None, :] < slot_order[:, None]
    )
    slot_ranks = jnp.sum(earlier_same.astype(jnp.int32), axis=1)
    send_keys = owners * CAP + slot_ranks
    send_ids = jnp.arange(device_count * CAP, dtype=jnp.int32)
    send_pick = (send_keys[:, None] == send_ids[None, :]).astype(jnp.float32)
    outbound = jnp.einsum(
        "lk,ld->kd", send_pick, slot_total, precision=lax.Precision.HIGHEST
    ).reshape(device_count, CAP, model_width)
    labels = jnp.einsum(
        "lk,l->k", send_pick, local_rows.astype(jnp.float32), precision=lax.Precision.HIGHEST
    ).reshape(device_count, CAP)
    label_row = jnp.zeros((device_count, 1, model_width), jnp.float32)
    label_row = label_row.at[:, 0, :CAP].set(labels)
    packed = jnp.concatenate([outbound, label_row], axis=1).astype(jnp.bfloat16)
    arrived = lax.all_to_all(
        packed, ("blk", "rep"), split_axis=0, concat_axis=0, tiled=True
    ).astype(jnp.float32)
    inbound = arrived[:, :CAP, :]
    inbound_labels = arrived[:, CAP, :CAP]
    table_rows = jnp.arange(SH_DEV, dtype=jnp.int32)
    selector = (
        inbound_labels.reshape(-1).astype(jnp.int32)[:, None] == table_rows[None, :]
    ).astype(jnp.float32)
    shared_grad = jnp.einsum(
        "rs,rd->sd",
        selector,
        inbound.reshape(-1, model_width),
        preferred_element_type=jnp.float32,
        precision=lax.Precision.HIGHEST,
    )
    own_shared = lax.dynamic_slice_in_dim(shared_table, device_place * SH_DEV, SH_DEV, 0)
    new_shared, new_shared_state = row_adagrad(own_shared, shared_state, shared_grad)
    return (new_entities, new_entity_state, new_shared, new_shared_state)


def solution(mesh):
    return jax.shard_map(
        shards,
        mesh=mesh,
        in_specs=(
            P("blk", None),
            P(("blk", "rep")),
            P(),
            P(("blk", "rep")),
            P("blk", None, "rep"),
            P("blk", None, "rep"),
            P("blk", None, "rep"),
            P("blk", None, "rep", None),
            P("blk", "rep", None),
            P("blk", "rep"),
        ),
        out_specs=(
            P(("blk", "rep"), None),
            P(("blk", "rep")),
            P(("blk", "rep"), None),
            P(("blk", "rep")),
        ),
        check_vma=False,
    )
```

```python
import jax
import jax.numpy as jnp
from jax import lax
from jax.sharding import PartitionSpec as P

CAP = 4
SH_DEV = 64
INDEX_SPLIT = 64


learn_rate = 0.1
negative_weight = 8.0


def passed_along(value, axis, by):
    peers = lax.axis_size(axis)
    return lax.ppermute(value, axis, [(i, (i + by) % peers) for i in range(peers)])


def make_query(resident, sources, slots, shared_rows):
    part_rows = resident.shape[0]
    entity_ids = jnp.arange(part_rows, dtype=jnp.int32)
    list_ids = jnp.arange(shared_rows.shape[0], dtype=jnp.int32)
    source_pick = (sources[:, None] == entity_ids[None, :]).astype(jnp.bfloat16)
    slot_pick = (slots[:, None] == list_ids[None, :]).astype(jnp.bfloat16)
    source_rows = jnp.dot(source_pick, resident, preferred_element_type=jnp.float32)
    shared_part = jnp.dot(slot_pick, shared_rows, preferred_element_type=jnp.float32)
    query = (source_rows + shared_part).astype(jnp.bfloat16)
    return query, source_pick, slot_pick


def target_side(visiting, query, targets, negatives):
    part_rows = visiting.shape[0]
    model_width = visiting.shape[1]
    group_count = negatives.shape[0]
    sample_count = negatives.shape[1]
    entity_ids = jnp.arange(part_rows, dtype=jnp.int32)
    target_pick = (targets[:, None] == entity_ids[None, :]).astype(jnp.bfloat16)
    sample_pick = (negatives[:, :, None] == entity_ids[None, None, :]).astype(jnp.bfloat16)
    target_rows = jnp.dot(target_pick, visiting, preferred_element_type=jnp.float32).astype(
        jnp.bfloat16
    )
    positive = jnp.einsum("ed,ed->e", query, target_rows, preferred_element_type=jnp.float32)
    query_groups = query.reshape(group_count, -1, model_width)
    samples = jnp.einsum(
        "cnx,xd->cnd", sample_pick, visiting, preferred_element_type=jnp.float32
    ).astype(jnp.bfloat16)
    negative = jnp.einsum("cqd,cnd->cqn", query_groups, samples, preferred_element_type=jnp.float32)
    positive_weight = -jax.nn.sigmoid(-positive)
    sample_weight = (jax.nn.sigmoid(negative) * (negative_weight / sample_count)).astype(
        jnp.bfloat16
    )
    sampled_sum = jnp.einsum(
        "cqn,cnd->cqd", sample_weight, samples, preferred_element_type=jnp.float32
    )
    query_grad = positive_weight[:, None] * target_rows.astype(jnp.float32) + sampled_sum.reshape(
        -1, model_width
    )
    weight_map = jnp.einsum(
        "cnx,cqn->xcq", sample_pick, sample_weight, preferred_element_type=jnp.float32
    ).reshape(part_rows, -1)
    weight_map = weight_map + jnp.einsum(
        "ex,e->xe", target_pick.astype(jnp.float32), positive_weight
    )
    visiting_grad = jnp.dot(
        weight_map.astype(jnp.bfloat16), query, preferred_element_type=jnp.float32
    )
    return query_grad, visiting_grad


def split_dot(spec, wide, narrow):
    high = wide.astype(jnp.bfloat16)
    low = (wide - high.astype(jnp.float32)).astype(jnp.bfloat16)
    return jnp.einsum(spec, high, narrow, preferred_element_type=jnp.float32) + jnp.einsum(
        spec, low, narrow, preferred_element_type=jnp.float32
    )


def rep_reduce(total):
    rep_count = lax.axis_size("rep")
    rep_place = lax.axis_index("rep")
    pieces = total.reshape(rep_count, -1, total.shape[1])
    own = lax.dynamic_index_in_dim(pieces, rep_place, 0, keepdims=False)
    for shift in range(1, rep_count):
        outgoing = lax.dynamic_index_in_dim(
            pieces, (rep_place + shift) % rep_count, 0, keepdims=False
        ).astype(jnp.bfloat16)
        own = own + passed_along(outgoing, "rep", shift).astype(jnp.float32)
    return own


def row_adagrad(rows, state, grad):
    new_state = state + jnp.mean(grad * grad, axis=-1)
    return (rows.astype(jnp.float32) - learn_rate * grad / jnp.sqrt(new_state)[:, None], new_state)


def shards(
    entities,
    entity_state,
    shared_table,
    shared_state,
    edge_src,
    edge_dst,
    edge_slot,
    neg_rows,
    list_owner,
    list_row,
):
    rep_count = lax.axis_size("rep")
    rep_place = lax.axis_index("rep")
    device_count = lax.axis_size("blk") * rep_count
    device_place = lax.axis_index("blk") * rep_count + rep_place
    part_rows = entities.shape[0]
    model_width = entities.shape[1]
    share_rows = part_rows // rep_count
    bucket_count = edge_src.shape[1]
    edge_count = edge_src.shape[2]
    owners = list_owner[0, :, 0]
    local_rows = list_row[0]
    table_ids = jnp.arange(shared_table.shape[0], dtype=jnp.int32)
    table_pick = ((owners * SH_DEV + local_rows)[:, None] == table_ids[None, :]).astype(jnp.bfloat16)
    shared_rows = jnp.dot(table_pick, shared_table, preferred_element_type=jnp.float32).astype(
        jnp.bfloat16
    )
    queries = []
    picks = []
    for bucket in range(bucket_count):
        query, source_pick, slot_pick = make_query(
            entities, edge_src[0, bucket], edge_slot[0, bucket], shared_rows
        )
        queries.append(query)
        picks.append((source_pick, slot_pick))
    arrivals = []
    for bucket in range(bucket_count):
        indices = jnp.concatenate([edge_dst[0, bucket], neg_rows[0, bucket].reshape(-1)])
        if bucket == 0:
            arrivals.append((queries[bucket], indices))
        else:
            coded = jnp.stack([indices // INDEX_SPLIT, indices % INDEX_SPLIT]).astype(jnp.bfloat16)
            parcel = jnp.concatenate([queries[bucket], coded.reshape(-1, model_width)], axis=0)
            parcel = passed_along(parcel, "blk", -bucket)
            coded = parcel[edge_count:].reshape(2, -1).astype(jnp.int32)
            arrivals.append((parcel[:edge_count], coded[0] * INDEX_SPLIT + coded[1]))
    group_shape = neg_rows.shape[2:]
    target_total = jnp.zeros((part_rows, model_width), jnp.float32)
    returned = [None] * bucket_count
    for bucket in [0] + list(range(bucket_count - 1, 0, -1)):
        query, indices = arrivals[bucket]
        targets = indices[:edge_count]
        negatives = indices[edge_count:].reshape(group_shape)
        query_grad, visiting_grad = target_side(entities, query, targets, negatives)
        target_total = target_total + visiting_grad
        if bucket == 0:
            returned[bucket] = query_grad
        else:
            returned[bucket] = passed_along(query_grad.astype(jnp.bfloat16), "blk", bucket)
    source_total = target_total
    slot_total = jnp.zeros((owners.shape[0], model_width), jnp.float32)
    for bucket in [0] + list(range(bucket_count - 1, 0, -1)):
        source_pick, slot_pick = picks[bucket]
        query_grad = returned[bucket]
        if query_grad.dtype == jnp.float32:
            source_total = source_total + split_dot("ed,ex->xd", query_grad, source_pick)
            slot_total = slot_total + split_dot("ed,el->ld", query_grad, slot_pick)
        else:
            source_total = source_total + jnp.einsum(
                "ed,ex->xd", query_grad, source_pick, preferred_element_type=jnp.float32
            )
            slot_total = slot_total + jnp.einsum(
                "ed,el->ld", query_grad, slot_pick, preferred_element_type=jnp.float32
            )
    own_grad = rep_reduce(source_total)
    own_entities = lax.dynamic_slice_in_dim(entities, rep_place * share_rows, share_rows, 0)
    new_entities, new_entity_state = row_adagrad(own_entities, entity_state, own_grad)
    slot_count = owners.shape[0]
    slot_order = jnp.arange(slot_count, dtype=jnp.int32)
    earlier_same = (owners[:, None] == owners[None, :]) & (
        slot_order[None, :] < slot_order[:, None]
    )
    slot_ranks = jnp.sum(earlier_same.astype(jnp.int32), axis=1)
    send_keys = owners * CAP + slot_ranks
    send_ids = jnp.arange(device_count * CAP, dtype=jnp.int32)
    send_pick = (send_keys[:, None] == send_ids[None, :]).astype(jnp.bfloat16)
    outbound = jnp.einsum(
        "lk,ld->kd", send_pick, slot_total.astype(jnp.bfloat16), preferred_element_type=jnp.float32
    ).reshape(device_count, CAP, model_width)
    labels = jnp.einsum(
        "lk,l->k", send_pick, local_rows.astype(jnp.bfloat16), preferred_element_type=jnp.float32
    ).reshape(device_count, CAP)
    label_row = jnp.zeros((device_count, 1, model_width), jnp.float32)
    label_row = label_row.at[:, 0, :CAP].set(labels)
    packed = jnp.concatenate([outbound, label_row], axis=1).astype(jnp.bfloat16)
    arrived = lax.all_to_all(
        packed, ("blk", "rep"), split_axis=0, concat_axis=0, tiled=True
    ).astype(jnp.float32)
    inbound = arrived[:, :CAP, :]
    inbound_labels = arrived[:, CAP, :CAP]
    table_rows = jnp.arange(SH_DEV, dtype=jnp.int32)
    selector = (
        inbound_labels.reshape(-1).astype(jnp.int32)[:, None] == table_rows[None, :]
    ).astype(jnp.bfloat16)
    shared_grad = jnp.einsum(
        "rs,rd->sd",
        selector,
        inbound.reshape(-1, model_width).astype(jnp.bfloat16),
        preferred_element_type=jnp.float32,
    )
    own_shared = lax.dynamic_slice_in_dim(shared_table, device_place * SH_DEV, SH_DEV, 0)
    new_shared, new_shared_state = row_adagrad(own_shared, shared_state, shared_grad)
    return (new_entities, new_entity_state, new_shared, new_shared_state)


def solution(mesh):
    return jax.shard_map(
        shards,
        mesh=mesh,
        in_specs=(
            P("blk", None),
            P(("blk", "rep")),
            P(),
            P(("blk", "rep")),
            P("blk", None, "rep"),
            P("blk", None, "rep"),
            P("blk", None, "rep"),
            P("blk", None, "rep", None),
            P("blk", "rep", None),
            P("blk", "rep"),
        ),
        out_specs=(
            P(("blk", "rep"), None),
            P(("blk", "rep")),
            P(("blk", "rep"), None),
            P(("blk", "rep")),
        ),
        check_vma=False,
    )
```

```python
import jax
import jax.numpy as jnp
from jax import lax
from jax.sharding import PartitionSpec as P

CAP = 4
SH_DEV = 64
INDEX_SPLIT = 64


learn_rate = 0.1
negative_weight = 8.0


def passed_along(value, axis, by):
    peers = lax.axis_size(axis)
    return lax.ppermute(value, axis, [(i, (i + by) % peers) for i in range(peers)])


def make_query(resident, sources, slots, shared_rows):
    part_rows = resident.shape[0]
    entity_ids = jnp.arange(part_rows, dtype=jnp.int32)
    list_ids = jnp.arange(shared_rows.shape[0], dtype=jnp.int32)
    source_pick = (sources[:, None] == entity_ids[None, :]).astype(jnp.bfloat16)
    slot_pick = (slots[:, None] == list_ids[None, :]).astype(jnp.bfloat16)
    source_rows = jnp.dot(source_pick, resident, preferred_element_type=jnp.float32)
    shared_part = jnp.dot(slot_pick, shared_rows, preferred_element_type=jnp.float32)
    query = (source_rows + shared_part).astype(jnp.bfloat16)
    return query, source_pick, slot_pick


def target_side(visiting, query, targets, negatives):
    part_rows = visiting.shape[0]
    model_width = visiting.shape[1]
    group_count = negatives.shape[0]
    sample_count = negatives.shape[1]
    entity_ids = jnp.arange(part_rows, dtype=jnp.int32)
    target_pick = (targets[:, None] == entity_ids[None, :]).astype(jnp.bfloat16)
    sample_pick = (negatives[:, :, None] == entity_ids[None, None, :]).astype(jnp.bfloat16)
    target_rows = jnp.dot(target_pick, visiting, preferred_element_type=jnp.float32).astype(
        jnp.bfloat16
    )
    positive = jnp.einsum("ed,ed->e", query, target_rows, preferred_element_type=jnp.float32)
    query_groups = query.reshape(group_count, -1, model_width)
    samples = jnp.einsum(
        "cnx,xd->cnd", sample_pick, visiting, preferred_element_type=jnp.float32
    ).astype(jnp.bfloat16)
    negative = jnp.einsum("cqd,cnd->cqn", query_groups, samples, preferred_element_type=jnp.float32)
    positive_weight = -jax.nn.sigmoid(-positive)
    sample_weight = (jax.nn.sigmoid(negative) * (negative_weight / sample_count)).astype(
        jnp.bfloat16
    )
    sampled_sum = jnp.einsum(
        "cqn,cnd->cqd", sample_weight, samples, preferred_element_type=jnp.float32
    )
    query_grad = positive_weight[:, None] * target_rows.astype(jnp.float32) + sampled_sum.reshape(
        -1, model_width
    )
    weight_map = jnp.einsum(
        "cnx,cqn->xcq", sample_pick, sample_weight, preferred_element_type=jnp.float32
    ).reshape(part_rows, -1)
    weight_map = weight_map + jnp.einsum(
        "ex,e->xe", target_pick.astype(jnp.float32), positive_weight
    )
    visiting_grad = jnp.dot(
        weight_map.astype(jnp.bfloat16), query, preferred_element_type=jnp.float32
    )
    return query_grad, visiting_grad


def split_dot(spec, wide, narrow):
    high = wide.astype(jnp.bfloat16)
    low = (wide - high.astype(jnp.float32)).astype(jnp.bfloat16)
    return jnp.einsum(spec, high, narrow, preferred_element_type=jnp.float32) + jnp.einsum(
        spec, low, narrow, preferred_element_type=jnp.float32
    )


def rep_reduce(total):
    rep_count = lax.axis_size("rep")
    rep_place = lax.axis_index("rep")
    pieces = total.reshape(rep_count, -1, total.shape[1])
    own = lax.dynamic_index_in_dim(pieces, rep_place, 0, keepdims=False)
    for shift in sorted(range(1, rep_count), key=lambda k: (k % 4 == 2, k)):
        outgoing = lax.dynamic_index_in_dim(
            pieces, (rep_place + shift) % rep_count, 0, keepdims=False
        ).astype(jnp.bfloat16)
        own = own + passed_along(outgoing, "rep", shift).astype(jnp.float32)
    return own


def row_adagrad(rows, state, grad):
    new_state = state + jnp.mean(grad * grad, axis=-1)
    return (rows.astype(jnp.float32) - learn_rate * grad / jnp.sqrt(new_state)[:, None], new_state)


def shards(
    entities,
    entity_state,
    shared_table,
    shared_state,
    edge_src,
    edge_dst,
    edge_slot,
    neg_rows,
    list_owner,
    list_row,
):
    rep_count = lax.axis_size("rep")
    rep_place = lax.axis_index("rep")
    device_count = lax.axis_size("blk") * rep_count
    device_place = lax.axis_index("blk") * rep_count + rep_place
    part_rows = entities.shape[0]
    model_width = entities.shape[1]
    share_rows = part_rows // rep_count
    bucket_count = edge_src.shape[1]
    edge_count = edge_src.shape[2]
    owners = list_owner[0, :, 0]
    local_rows = list_row[0]
    table_ids = jnp.arange(shared_table.shape[0], dtype=jnp.int32)
    table_pick = ((owners * SH_DEV + local_rows)[:, None] == table_ids[None, :]).astype(jnp.bfloat16)
    shared_rows = jnp.dot(table_pick, shared_table, preferred_element_type=jnp.float32).astype(
        jnp.bfloat16
    )
    queries = []
    picks = []
    for bucket in range(bucket_count):
        query, source_pick, slot_pick = make_query(
            entities, edge_src[0, bucket], edge_slot[0, bucket], shared_rows
        )
        queries.append(query)
        picks.append((source_pick, slot_pick))
    arrivals = []
    for bucket in range(bucket_count):
        indices = jnp.concatenate([edge_dst[0, bucket], neg_rows[0, bucket].reshape(-1)])
        if bucket == 0:
            arrivals.append((queries[bucket], indices))
        else:
            coded = jnp.stack([indices // INDEX_SPLIT, indices % INDEX_SPLIT]).astype(jnp.bfloat16)
            parcel = jnp.concatenate([queries[bucket], coded.reshape(-1, model_width)], axis=0)
            parcel = passed_along(parcel, "blk", -bucket)
            coded = parcel[edge_count:].reshape(2, -1).astype(jnp.int32)
            arrivals.append((parcel[:edge_count], coded[0] * INDEX_SPLIT + coded[1]))
    group_shape = neg_rows.shape[2:]
    target_total = jnp.zeros((part_rows, model_width), jnp.float32)
    returned = [None] * bucket_count
    for bucket in [0] + list(range(bucket_count - 1, 0, -1)):
        query, indices = arrivals[bucket]
        targets = indices[:edge_count]
        negatives = indices[edge_count:].reshape(group_shape)
        query_grad, visiting_grad = target_side(entities, query, targets, negatives)
        target_total = target_total + visiting_grad
        if bucket == 0:
            returned[bucket] = query_grad
        else:
            returned[bucket] = passed_along(query_grad.astype(jnp.bfloat16), "blk", bucket)
    source_total = target_total
    slot_total = jnp.zeros((owners.shape[0], model_width), jnp.float32)
    for bucket in [0] + list(range(bucket_count - 1, 0, -1)):
        source_pick, slot_pick = picks[bucket]
        query_grad = returned[bucket]
        if query_grad.dtype == jnp.float32:
            source_total = source_total + split_dot("ed,ex->xd", query_grad, source_pick)
            slot_total = slot_total + split_dot("ed,el->ld", query_grad, slot_pick)
        else:
            source_total = source_total + jnp.einsum(
                "ed,ex->xd", query_grad, source_pick, preferred_element_type=jnp.float32
            )
            slot_total = slot_total + jnp.einsum(
                "ed,el->ld", query_grad, slot_pick, preferred_element_type=jnp.float32
            )
    own_grad = rep_reduce(source_total)
    own_entities = lax.dynamic_slice_in_dim(entities, rep_place * share_rows, share_rows, 0)
    new_entities, new_entity_state = row_adagrad(own_entities, entity_state, own_grad)
    slot_count = owners.shape[0]
    slot_order = jnp.arange(slot_count, dtype=jnp.int32)
    earlier_same = (owners[:, None] == owners[None, :]) & (
        slot_order[None, :] < slot_order[:, None]
    )
    slot_ranks = jnp.sum(earlier_same.astype(jnp.int32), axis=1)
    send_keys = owners * CAP + slot_ranks
    send_ids = jnp.arange(device_count * CAP, dtype=jnp.int32)
    send_pick = (send_keys[:, None] == send_ids[None, :]).astype(jnp.bfloat16)
    outbound = jnp.einsum(
        "lk,ld->kd", send_pick, slot_total.astype(jnp.bfloat16), preferred_element_type=jnp.float32
    ).reshape(device_count, CAP, model_width)
    labels = jnp.einsum(
        "lk,l->k", send_pick, local_rows.astype(jnp.bfloat16), preferred_element_type=jnp.float32
    ).reshape(device_count, CAP)
    label_row = jnp.zeros((device_count, 1, model_width), jnp.float32)
    label_row = label_row.at[:, 0, :CAP].set(labels)
    packed = jnp.concatenate([outbound, label_row], axis=1).astype(jnp.bfloat16)
    arrived = lax.all_to_all(
        packed, ("blk", "rep"), split_axis=0, concat_axis=0, tiled=True
    ).astype(jnp.float32)
    inbound = arrived[:, :CAP, :]
    inbound_labels = arrived[:, CAP, :CAP]
    table_rows = jnp.arange(SH_DEV, dtype=jnp.int32)
    selector = (
        inbound_labels.reshape(-1).astype(jnp.int32)[:, None] == table_rows[None, :]
    ).astype(jnp.bfloat16)
    shared_grad = jnp.einsum(
        "rs,rd->sd",
        selector,
        inbound.reshape(-1, model_width).astype(jnp.bfloat16),
        preferred_element_type=jnp.float32,
    )
    own_shared = lax.dynamic_slice_in_dim(shared_table, device_place * SH_DEV, SH_DEV, 0)
    new_shared, new_shared_state = row_adagrad(own_shared, shared_state, shared_grad)
    return (new_entities, new_entity_state, new_shared, new_shared_state)


def solution(mesh):
    return jax.shard_map(
        shards,
        mesh=mesh,
        in_specs=(
            P("blk", None),
            P(("blk", "rep")),
            P(),
            P(("blk", "rep")),
            P("blk", None, "rep"),
            P("blk", None, "rep"),
            P("blk", None, "rep"),
            P("blk", None, "rep", None),
            P("blk", "rep", None),
            P("blk", "rep"),
        ),
        out_specs=(
            P(("blk", "rep"), None),
            P(("blk", "rep")),
            P(("blk", "rep"), None),
            P(("blk", "rep")),
        ),
        check_vma=False,
    )
```

```python
import jax
import jax.numpy as jnp
from jax import lax
from jax.sharding import PartitionSpec as P

CAP = 4
SH_DEV = 64
INDEX_SPLIT = 64


learn_rate = 0.1
negative_weight = 8.0


def passed_along(value, axis, by):
    peers = lax.axis_size(axis)
    return lax.ppermute(value, axis, [(i, (i + by) % peers) for i in range(peers)])


def make_query(resident, sources, slots, shared_rows):
    part_rows = resident.shape[0]
    entity_ids = jnp.arange(part_rows, dtype=jnp.int32)
    list_ids = jnp.arange(shared_rows.shape[0], dtype=jnp.int32)
    source_pick = (sources[:, None] == entity_ids[None, :]).astype(jnp.bfloat16)
    slot_pick = (slots[:, None] == list_ids[None, :]).astype(jnp.bfloat16)
    source_rows = jnp.dot(source_pick, resident, preferred_element_type=jnp.float32)
    shared_part = jnp.dot(slot_pick, shared_rows, preferred_element_type=jnp.float32)
    query = (source_rows + shared_part).astype(jnp.bfloat16)
    return query, source_pick, slot_pick


def target_side(visiting, query, targets, negatives):
    part_rows = visiting.shape[0]
    model_width = visiting.shape[1]
    group_count = negatives.shape[0]
    sample_count = negatives.shape[1]
    entity_ids = jnp.arange(part_rows, dtype=jnp.int32)
    target_pick = (targets[:, None] == entity_ids[None, :]).astype(jnp.bfloat16)
    sample_pick = (negatives[:, :, None] == entity_ids[None, None, :]).astype(jnp.bfloat16)
    target_rows = jnp.dot(target_pick, visiting, preferred_element_type=jnp.float32).astype(
        jnp.bfloat16
    )
    positive = jnp.einsum("ed,ed->e", query, target_rows, preferred_element_type=jnp.float32)
    query_groups = query.reshape(group_count, -1, model_width)
    samples = jnp.einsum(
        "cnx,xd->cnd", sample_pick, visiting, preferred_element_type=jnp.float32
    ).astype(jnp.bfloat16)
    negative = jnp.einsum("cqd,cnd->cqn", query_groups, samples, preferred_element_type=jnp.float32)
    positive_weight = -jax.nn.sigmoid(-positive)
    sample_weight = (jax.nn.sigmoid(negative) * (negative_weight / sample_count)).astype(
        jnp.bfloat16
    )
    sampled_sum = jnp.einsum(
        "cqn,cnd->cqd", sample_weight, samples, preferred_element_type=jnp.float32
    )
    query_grad = positive_weight[:, None] * target_rows.astype(jnp.float32) + sampled_sum.reshape(
        -1, model_width
    )
    weight_map = jnp.einsum(
        "cnx,cqn->xcq", sample_pick, sample_weight, preferred_element_type=jnp.float32
    ).reshape(part_rows, -1)
    weight_map = weight_map + jnp.einsum(
        "ex,e->xe", target_pick.astype(jnp.float32), positive_weight
    )
    visiting_grad = jnp.dot(
        weight_map.astype(jnp.bfloat16), query, preferred_element_type=jnp.float32
    )
    return query_grad, visiting_grad


def split_dot(spec, wide, narrow):
    high = wide.astype(jnp.bfloat16)
    low = (wide - high.astype(jnp.float32)).astype(jnp.bfloat16)
    return jnp.einsum(spec, high, narrow, preferred_element_type=jnp.float32) + jnp.einsum(
        spec, low, narrow, preferred_element_type=jnp.float32
    )


def rep_reduce(total):
    rep_count = lax.axis_size("rep")
    rep_place = lax.axis_index("rep")
    pieces = total.reshape(rep_count, -1, total.shape[1])
    own = lax.dynamic_index_in_dim(pieces, rep_place, 0, keepdims=False)
    for shift in sorted(range(1, rep_count), key=lambda k: (k % 4 != 2, k)):
        outgoing = lax.dynamic_index_in_dim(
            pieces, (rep_place + shift) % rep_count, 0, keepdims=False
        ).astype(jnp.bfloat16)
        own = own + passed_along(outgoing, "rep", shift).astype(jnp.float32)
    return own


def row_adagrad(rows, state, grad):
    new_state = state + jnp.mean(grad * grad, axis=-1)
    return (rows.astype(jnp.float32) - learn_rate * grad / jnp.sqrt(new_state)[:, None], new_state)


def shards(
    entities,
    entity_state,
    shared_table,
    shared_state,
    edge_src,
    edge_dst,
    edge_slot,
    neg_rows,
    list_owner,
    list_row,
):
    rep_count = lax.axis_size("rep")
    rep_place = lax.axis_index("rep")
    device_count = lax.axis_size("blk") * rep_count
    device_place = lax.axis_index("blk") * rep_count + rep_place
    part_rows = entities.shape[0]
    model_width = entities.shape[1]
    share_rows = part_rows // rep_count
    bucket_count = edge_src.shape[1]
    edge_count = edge_src.shape[2]
    owners = list_owner[0, :, 0]
    local_rows = list_row[0]
    table_ids = jnp.arange(shared_table.shape[0], dtype=jnp.int32)
    table_pick = ((owners * SH_DEV + local_rows)[:, None] == table_ids[None, :]).astype(jnp.bfloat16)
    shared_rows = jnp.dot(table_pick, shared_table, preferred_element_type=jnp.float32).astype(
        jnp.bfloat16
    )
    queries = []
    picks = []
    for bucket in range(bucket_count):
        query, source_pick, slot_pick = make_query(
            entities, edge_src[0, bucket], edge_slot[0, bucket], shared_rows
        )
        queries.append(query)
        picks.append((source_pick, slot_pick))
    arrivals = []
    for bucket in range(bucket_count):
        indices = jnp.concatenate([edge_dst[0, bucket], neg_rows[0, bucket].reshape(-1)])
        if bucket == 0:
            arrivals.append((queries[bucket], indices))
        else:
            coded = jnp.stack([indices // INDEX_SPLIT, indices % INDEX_SPLIT]).astype(jnp.bfloat16)
            parcel = jnp.concatenate([queries[bucket], coded.reshape(-1, model_width)], axis=0)
            parcel = passed_along(parcel, "blk", -bucket)
            coded = parcel[edge_count:].reshape(2, -1).astype(jnp.int32)
            arrivals.append((parcel[:edge_count], coded[0] * INDEX_SPLIT + coded[1]))
    group_shape = neg_rows.shape[2:]
    target_total = jnp.zeros((part_rows, model_width), jnp.float32)
    returned = [None] * bucket_count
    for bucket in [0] + list(range(bucket_count - 1, 0, -1)):
        query, indices = arrivals[bucket]
        targets = indices[:edge_count]
        negatives = indices[edge_count:].reshape(group_shape)
        query_grad, visiting_grad = target_side(entities, query, targets, negatives)
        target_total = target_total + visiting_grad
        if bucket == 0:
            returned[bucket] = query_grad
        else:
            returned[bucket] = passed_along(query_grad.astype(jnp.bfloat16), "blk", bucket)
    source_total = target_total
    slot_total = jnp.zeros((owners.shape[0], model_width), jnp.float32)
    for bucket in [0] + list(range(bucket_count - 1, 0, -1)):
        source_pick, slot_pick = picks[bucket]
        query_grad = returned[bucket]
        if query_grad.dtype == jnp.float32:
            source_total = source_total + split_dot("ed,ex->xd", query_grad, source_pick)
            slot_total = slot_total + split_dot("ed,el->ld", query_grad, slot_pick)
        else:
            source_total = source_total + jnp.einsum(
                "ed,ex->xd", query_grad, source_pick, preferred_element_type=jnp.float32
            )
            slot_total = slot_total + jnp.einsum(
                "ed,el->ld", query_grad, slot_pick, preferred_element_type=jnp.float32
            )
    own_grad = rep_reduce(source_total)
    own_entities = lax.dynamic_slice_in_dim(entities, rep_place * share_rows, share_rows, 0)
    new_entities, new_entity_state = row_adagrad(own_entities, entity_state, own_grad)
    slot_count = owners.shape[0]
    slot_order = jnp.arange(slot_count, dtype=jnp.int32)
    earlier_same = (owners[:, None] == owners[None, :]) & (
        slot_order[None, :] < slot_order[:, None]
    )
    slot_ranks = jnp.sum(earlier_same.astype(jnp.int32), axis=1)
    send_keys = owners * CAP + slot_ranks
    send_ids = jnp.arange(device_count * CAP, dtype=jnp.int32)
    send_pick = (send_keys[:, None] == send_ids[None, :]).astype(jnp.bfloat16)
    outbound = jnp.einsum(
        "lk,ld->kd", send_pick, slot_total.astype(jnp.bfloat16), preferred_element_type=jnp.float32
    ).reshape(device_count, CAP, model_width)
    labels = jnp.einsum(
        "lk,l->k", send_pick, local_rows.astype(jnp.bfloat16), preferred_element_type=jnp.float32
    ).reshape(device_count, CAP)
    label_row = jnp.zeros((device_count, 1, model_width), jnp.float32)
    label_row = label_row.at[:, 0, :CAP].set(labels)
    packed = jnp.concatenate([outbound, label_row], axis=1).astype(jnp.bfloat16)
    arrived = lax.all_to_all(
        packed, ("blk", "rep"), split_axis=0, concat_axis=0, tiled=True
    ).astype(jnp.float32)
    inbound = arrived[:, :CAP, :]
    inbound_labels = arrived[:, CAP, :CAP]
    table_rows = jnp.arange(SH_DEV, dtype=jnp.int32)
    selector = (
        inbound_labels.reshape(-1).astype(jnp.int32)[:, None] == table_rows[None, :]
    ).astype(jnp.bfloat16)
    shared_grad = jnp.einsum(
        "rs,rd->sd",
        selector,
        inbound.reshape(-1, model_width).astype(jnp.bfloat16),
        preferred_element_type=jnp.float32,
    )
    own_shared = lax.dynamic_slice_in_dim(shared_table, device_place * SH_DEV, SH_DEV, 0)
    new_shared, new_shared_state = row_adagrad(own_shared, shared_state, shared_grad)
    return (new_entities, new_entity_state, new_shared, new_shared_state)


def solution(mesh):
    return jax.shard_map(
        shards,
        mesh=mesh,
        in_specs=(
            P("blk", None),
            P(("blk", "rep")),
            P(),
            P(("blk", "rep")),
            P("blk", None, "rep"),
            P("blk", None, "rep"),
            P("blk", None, "rep"),
            P("blk", None, "rep", None),
            P("blk", "rep", None),
            P("blk", "rep"),
        ),
        out_specs=(
            P(("blk", "rep"), None),
            P(("blk", "rep")),
            P(("blk", "rep"), None),
            P(("blk", "rep")),
        ),
        check_vma=False,
    )
```

```python
import jax
import jax.numpy as jnp
from jax import lax
from jax.sharding import PartitionSpec as P

CAP = 4
SH_DEV = 64
INDEX_SPLIT = 64


learn_rate = 0.1
negative_weight = 8.0


def passed_along(value, axis, by):
    peers = lax.axis_size(axis)
    return lax.ppermute(value, axis, [(i, (i + by) % peers) for i in range(peers)])


def make_query(resident, sources, slots, shared_rows):
    part_rows = resident.shape[0]
    entity_ids = jnp.arange(part_rows, dtype=jnp.int32)
    list_ids = jnp.arange(shared_rows.shape[0], dtype=jnp.int32)
    source_pick = (sources[:, None] == entity_ids[None, :]).astype(jnp.bfloat16)
    slot_pick = (slots[:, None] == list_ids[None, :]).astype(jnp.bfloat16)
    source_rows = jnp.dot(source_pick, resident, preferred_element_type=jnp.float32)
    shared_part = jnp.dot(slot_pick, shared_rows, preferred_element_type=jnp.float32)
    query = (source_rows + shared_part).astype(jnp.bfloat16)
    return query, source_pick, slot_pick


def target_side(visiting, query, targets, negatives):
    part_rows = visiting.shape[0]
    model_width = visiting.shape[1]
    group_count = negatives.shape[0]
    sample_count = negatives.shape[1]
    entity_ids = jnp.arange(part_rows, dtype=jnp.int32)
    target_pick = (targets[:, None] == entity_ids[None, :]).astype(jnp.bfloat16)
    sample_pick = (negatives[:, :, None] == entity_ids[None, None, :]).astype(jnp.bfloat16)
    target_rows = jnp.dot(target_pick, visiting, preferred_element_type=jnp.float32).astype(
        jnp.bfloat16
    )
    positive = jnp.einsum("ed,ed->e", query, target_rows, preferred_element_type=jnp.float32)
    query_groups = query.reshape(group_count, -1, model_width)
    samples = jnp.einsum(
        "cnx,xd->cnd", sample_pick, visiting, preferred_element_type=jnp.float32
    ).astype(jnp.bfloat16)
    negative = jnp.einsum("cqd,cnd->cqn", query_groups, samples, preferred_element_type=jnp.float32)
    positive_weight = -jax.nn.sigmoid(-positive)
    sample_weight = (jax.nn.sigmoid(negative) * (negative_weight / sample_count)).astype(
        jnp.bfloat16
    )
    sampled_sum = jnp.einsum(
        "cqn,cnd->cqd", sample_weight, samples, preferred_element_type=jnp.float32
    )
    query_grad = positive_weight[:, None] * target_rows.astype(jnp.float32) + sampled_sum.reshape(
        -1, model_width
    )
    weight_map = jnp.einsum(
        "cnx,cqn->xcq", sample_pick, sample_weight, preferred_element_type=jnp.float32
    ).reshape(part_rows, -1)
    weight_map = weight_map + jnp.einsum(
        "ex,e->xe", target_pick.astype(jnp.float32), positive_weight
    )
    visiting_grad = jnp.dot(
        weight_map.astype(jnp.bfloat16), query, preferred_element_type=jnp.float32
    )
    return query_grad, visiting_grad


def rep_reduce(total):
    rep_count = lax.axis_size("rep")
    rep_place = lax.axis_index("rep")
    pieces = total.reshape(rep_count, -1, total.shape[1])
    own = lax.dynamic_index_in_dim(pieces, rep_place, 0, keepdims=False)
    for shift in range(1, rep_count):
        outgoing = lax.dynamic_index_in_dim(
            pieces, (rep_place + shift) % rep_count, 0, keepdims=False
        ).astype(jnp.bfloat16)
        own = own + passed_along(outgoing, "rep", shift).astype(jnp.float32)
    return own


def row_adagrad(rows, state, grad):
    new_state = state + jnp.mean(grad * grad, axis=-1)
    return (rows.astype(jnp.float32) - learn_rate * grad / jnp.sqrt(new_state)[:, None], new_state)


def shards(
    entities,
    entity_state,
    shared_table,
    shared_state,
    edge_src,
    edge_dst,
    edge_slot,
    neg_rows,
    list_owner,
    list_row,
):
    rep_count = lax.axis_size("rep")
    rep_place = lax.axis_index("rep")
    device_count = lax.axis_size("blk") * rep_count
    device_place = lax.axis_index("blk") * rep_count + rep_place
    part_rows = entities.shape[0]
    model_width = entities.shape[1]
    share_rows = part_rows // rep_count
    bucket_count = edge_src.shape[1]
    edge_count = edge_src.shape[2]
    owners = list_owner[0, :, 0]
    local_rows = list_row[0]
    table_ids = jnp.arange(shared_table.shape[0], dtype=jnp.int32)
    table_pick = ((owners * SH_DEV + local_rows)[:, None] == table_ids[None, :]).astype(jnp.bfloat16)
    shared_rows = jnp.dot(table_pick, shared_table, preferred_element_type=jnp.float32).astype(
        jnp.bfloat16
    )
    queries = []
    picks = []
    for bucket in range(bucket_count):
        query, source_pick, slot_pick = make_query(
            entities, edge_src[0, bucket], edge_slot[0, bucket], shared_rows
        )
        queries.append(query)
        picks.append((source_pick, slot_pick))
    arrivals = []
    for bucket in range(bucket_count):
        indices = jnp.concatenate([edge_dst[0, bucket], neg_rows[0, bucket].reshape(-1)])
        if bucket == 0:
            arrivals.append((queries[bucket], indices))
        else:
            coded = jnp.stack([indices // INDEX_SPLIT, indices % INDEX_SPLIT]).astype(jnp.bfloat16)
            parcel = jnp.concatenate([queries[bucket], coded.reshape(-1, model_width)], axis=0)
            parcel = passed_along(parcel, "blk", -bucket)
            coded = parcel[edge_count:].reshape(2, -1).astype(jnp.int32)
            arrivals.append((parcel[:edge_count], coded[0] * INDEX_SPLIT + coded[1]))
    group_shape = neg_rows.shape[2:]
    target_total = jnp.zeros((part_rows, model_width), jnp.float32)
    returned = [None] * bucket_count
    for bucket in [0] + list(range(bucket_count - 1, 0, -1)):
        query, indices = arrivals[bucket]
        targets = indices[:edge_count]
        negatives = indices[edge_count:].reshape(group_shape)
        query_grad, visiting_grad = target_side(entities, query, targets, negatives)
        target_total = target_total + visiting_grad
        if bucket == 0:
            returned[bucket] = query_grad.astype(jnp.bfloat16)
        else:
            returned[bucket] = passed_along(query_grad.astype(jnp.bfloat16), "blk", bucket)
    source_total = target_total
    slot_total = jnp.zeros((owners.shape[0], model_width), jnp.float32)
    for bucket in [0] + list(range(bucket_count - 1, 0, -1)):
        source_pick, slot_pick = picks[bucket]
        query_grad = returned[bucket]
        source_total = source_total + jnp.einsum(
            "ed,ex->xd", query_grad, source_pick, preferred_element_type=jnp.float32
        )
        slot_total = slot_total + jnp.einsum(
            "ed,el->ld", query_grad, slot_pick, preferred_element_type=jnp.float32
        )
    own_grad = rep_reduce(source_total)
    own_entities = lax.dynamic_slice_in_dim(entities, rep_place * share_rows, share_rows, 0)
    new_entities, new_entity_state = row_adagrad(own_entities, entity_state, own_grad)
    slot_count = owners.shape[0]
    slot_order = jnp.arange(slot_count, dtype=jnp.int32)
    earlier_same = (owners[:, None] == owners[None, :]) & (
        slot_order[None, :] < slot_order[:, None]
    )
    slot_ranks = jnp.sum(earlier_same.astype(jnp.int32), axis=1)
    send_keys = owners * CAP + slot_ranks
    send_ids = jnp.arange(device_count * CAP, dtype=jnp.int32)
    send_pick = (send_keys[:, None] == send_ids[None, :]).astype(jnp.bfloat16)
    outbound = jnp.einsum(
        "lk,ld->kd", send_pick, slot_total.astype(jnp.bfloat16), preferred_element_type=jnp.float32
    ).reshape(device_count, CAP, model_width)
    labels = jnp.einsum(
        "lk,l->k", send_pick, local_rows.astype(jnp.bfloat16), preferred_element_type=jnp.float32
    ).reshape(device_count, CAP)
    label_row = jnp.zeros((device_count, 1, model_width), jnp.float32)
    label_row = label_row.at[:, 0, :CAP].set(labels)
    packed = jnp.concatenate([outbound, label_row], axis=1).astype(jnp.bfloat16)
    arrived = lax.all_to_all(
        packed, ("blk", "rep"), split_axis=0, concat_axis=0, tiled=True
    ).astype(jnp.float32)
    inbound = arrived[:, :CAP, :]
    inbound_labels = arrived[:, CAP, :CAP]
    table_rows = jnp.arange(SH_DEV, dtype=jnp.int32)
    selector = (
        inbound_labels.reshape(-1).astype(jnp.int32)[:, None] == table_rows[None, :]
    ).astype(jnp.bfloat16)
    shared_grad = jnp.einsum(
        "rs,rd->sd",
        selector,
        inbound.reshape(-1, model_width).astype(jnp.bfloat16),
        preferred_element_type=jnp.float32,
    )
    own_shared = lax.dynamic_slice_in_dim(shared_table, device_place * SH_DEV, SH_DEV, 0)
    new_shared, new_shared_state = row_adagrad(own_shared, shared_state, shared_grad)
    return (new_entities, new_entity_state, new_shared, new_shared_state)


def solution(mesh):
    return jax.shard_map(
        shards,
        mesh=mesh,
        in_specs=(
            P("blk", None),
            P(("blk", "rep")),
            P(),
            P(("blk", "rep")),
            P("blk", None, "rep"),
            P("blk", None, "rep"),
            P("blk", None, "rep"),
            P("blk", None, "rep", None),
            P("blk", "rep", None),
            P("blk", "rep"),
        ),
        out_specs=(
            P(("blk", "rep"), None),
            P(("blk", "rep")),
            P(("blk", "rep"), None),
            P(("blk", "rep")),
        ),
        check_vma=False,
    )
```
